32 devices in a mesh: swath: 2 (over y), sub: 4 (over z), beam: 2 (over x), half: 2 (over core).
Axes of the slice: x: 2, y: 2, z: 4, core: 2. Of those that a mesh axis runs over, the one named last changes fastest.
Arguments:
- images: bfloat16 [4, 2, 2048, 1024], P('sub', None, ('swath', 'half'), 'beam'), parts along dimension 2, may hold values from -6 to 6
- offsets: float32 [4], replicated, may hold values from 3840 to 4505
- owners: int32 [2, 4], replicated, may hold values from 0 to 3, each once within a row
Outputs:
- sectors: bfloat16 [8, 1, 2, 512, 2048], P(('sub', 'beam'), None, None, None, ('swath', 'half')), parts along dimension 4
The draws below stay inside these ranges and needn't reach their ends.
There are 2 independent parts, one for each index of `swath`. The reference program is written for one: setup_inputs(seed, part) draws one part's arguments, and reference() takes and returns one part's arrays. A program takes and returns all parts, laid end to end along the dimension named above; an argument that names none is the same for every part. Nothing has to cross between parts.
Inputs may be any that keep to these rules, and one draw needn't show every extreme that they name: Each row of owners names every one of the 4 sectors of its beam shard exactly once.
All inputs are finite; a program needn't handle non-finite values.
Results may differ from the reference program's by a relative error of at most 0.0052.
Values may be sent and summed in bfloat16 or wider, within the bound.
No kernel may reach another device: no remote copies, remote signals or barrier semaphores. Data moves between devices by JAX's collectives and lax.ppermute only.
A program may use at most 64 MiB of HBM per device.

```python
import math
import jax
import jax.numpy as jnp
from jax import lax

B = 1024
NR = 1024
SUB_DEV = 1
NSUB = 4
GROUPS = 1
BEAM_SHARDS = 2
SUB_SHARDS = 4
SECTORS = 8
SECTOR_W = 512
N_SUB = 4
N_BEAM = 2


def steps_of(key, dims, shards, low, high):
    def one(axis_at, parts):
        draws = jax.random.uniform(jax.random.fold_in(jax.random.fold_in(key, 6), axis_at), (parts,), jnp.float32, low / len(shards), high / len(shards))
        return jnp.repeat(jnp.exp(draws), dims[axis_at] // parts).reshape((-1,) + (1,) * (len(dims) - axis_at - 1))

    loudness = one(*shards[0])
    for cut in shards[1:]:
        loudness = loudness * one(*cut)
    return loudness


def gaussian(rng, dims, deviation, bound, cuts=(), kind=jnp.bfloat16):
    result = jax.random.normal(rng, dims, jnp.float32) * deviation
    if len(cuts) > 0:
        result = steps_of(rng, dims, cuts, -0.22, 0.18) * result
    return jnp.clip(result, min=-bound, max=bound).astype(kind)


def setup_inputs(seed: int = 0, part: int = 0) -> dict:
    keys = jax.random.split(jax.random.key(seed), 4)
    own_keys = jax.random.split(jax.random.fold_in(keys[3], part), 4)
    images = gaussian(own_keys[0], (NSUB, 2, NR, B), 1.0, 6.0, ((0, 4), (2, 2), (3, 2)))
    offsets = jnp.clip(jax.random.uniform(keys[1], (NSUB,), jnp.float32, 3840.0, 4505.0), 3840.0, 4505.0)
    owners = jax.vmap(lambda own: jax.random.permutation(own, SUB_SHARDS))(jax.random.split(keys[2], BEAM_SHARDS)).reshape((BEAM_SHARDS, SUB_SHARDS)).astype(jnp.int32)
    return {"images": images, "offsets": offsets, "owners": owners}


def odd_kernel(beam_total, first_at, columns):
    source_ix = lax.broadcasted_iota(jnp.int32, (beam_total, columns), 0)
    target_ix = lax.broadcasted_iota(jnp.int32, (beam_total, columns), 1) + first_at
    spacing = target_ix - source_ix
    parity = jnp.where(spacing % 2 == 0, 1.0, -1.0).astype(jnp.float32)
    angles = (2.0 * spacing.astype(jnp.float32) + 1.0) * (math.pi / (2.0 * beam_total))
    return (parity * jnp.cos(angles) / (beam_total * jnp.sin(angles))).astype(jnp.bfloat16)


def upsample(children, kernel):
    beam_total = children.shape[-1]
    odd_beams = jnp.dot(children.reshape(-1, beam_total), kernel, preferred_element_type=jnp.float32)
    odd_beams = odd_beams.reshape(children.shape[:-1] + (kernel.shape[1],))
    joined = jnp.stack([children.astype(jnp.float32), odd_beams], -1)
    return joined.reshape(children.shape[:-1] + (2 * kernel.shape[1],))


def steer_phase(upsampled, shifts, rows_at, beams_at, beams_out):
    ratios = NR / (NR + rows_at.astype(jnp.float32))
    tilts = (2.0 * beams_at.astype(jnp.float32) + 1.0) / beams_out - 1.0
    phases = (ratios[:, None] * tilts[None, :]) * shifts[..., None, None]
    cosine = jnp.cos(phases)
    sines = jnp.sin(phases)
    real_part = upsampled[..., 0, :, :]
    imag_part = upsampled[..., 1, :, :]
    return jnp.stack([real_part * cosine - imag_part * sines, real_part * sines + imag_part * cosine], -3)


def merge_pair(children, shifts, kernel):
    upsampled = upsample(children, kernel)
    rows_at = jnp.arange(NR, dtype=jnp.int32)
    beams_at = jnp.arange(upsampled.shape[-1], dtype=jnp.int32)
    return jnp.sum(steer_phase(upsampled, shifts, rows_at, beams_at, upsampled.shape[-1]), axis=0)


def reference(images, offsets, owners):
    kernel_one = odd_kernel(B, 0, B)
    kernel_two = odd_kernel(2 * B, 0, 2 * B)
    grouped = images.reshape(N_SUB // 4, 4, SUB_DEV, 2, NR, B)
    shifted = offsets.reshape(N_SUB // 4, 4, SUB_DEV)

    def merge_group(blocks):
        members, shifts = blocks
        first = jnp.stack([merge_pair(members[2 * member:2 * member + 2], shifts[2 * member:2 * member + 2], kernel_one).astype(jnp.bfloat16) for member in range(2)])
        centers = (shifts[0::2] + shifts[1::2]) * 0.5
        return merge_pair(first, centers, kernel_two).astype(jnp.bfloat16)

    merged = lax.map(merge_group, (grouped, shifted))
    merged = merged.reshape(GROUPS, 2, NR, 4 * B)
    sector_tiles = merged.reshape(GROUPS, 2, NR, N_BEAM, N_SUB, SECTOR_W)
    beam_ids = jnp.arange(N_BEAM, dtype=jnp.int32)[:, None]
    picked = sector_tiles[:, :, :, beam_ids, owners, :]
    ordered = picked.transpose(4, 3, 0, 1, 5, 2)
    return ordered.reshape(SECTORS, GROUPS, 2, SECTOR_W, NR)
```

```python
import math

import jax
import numpy as np
import jax.numpy as jnp
from jax import lax
from jax.sharding import PartitionSpec as P

B = 1024
NR = 1024


def swapped(value, axis, distance):
    return lax.ppermute(value, axis, [(i, i ^ 1 << distance) for i in range(lax.axis_size(axis))])


def odd_kernel(beam_total, columns):
    spacing = np.arange(columns, dtype=np.int64)[None, :] - np.arange(beam_total, dtype=np.int64)[:, None]
    parity = np.where(spacing % 2 == 0, 1.0, -1.0).astype(np.float32)
    angles = (2.0 * spacing.astype(np.float32) + np.float32(1.0)) * np.float32(math.pi / (2.0 * beam_total))
    values = parity * np.cos(angles) / (np.float32(beam_total) * np.sin(angles))
    return jnp.asarray(values.astype(np.float32).astype(jnp.bfloat16))


def steer_phase(upsampled, shifts, rows_at, beams_at, beams_out):
    ratios = NR / (NR + rows_at.astype(jnp.float32))
    tilts = (2.0 * beams_at.astype(jnp.float32) + 1.0) / beams_out - 1.0
    phases = ratios[:, None] * tilts[None, :] * shifts[..., None, None]
    cosine = jnp.cos(phases)
    sines = jnp.sin(phases)
    real_part = upsampled[..., 0, :, :]
    imag_part = upsampled[..., 1, :, :]
    return jnp.stack(
        [real_part * cosine - imag_part * sines, real_part * sines + imag_part * cosine], -3
    )


def rotate_sum(children, odd_beams, shifts, rows_at, beams_out):
    count = children.shape[-1]
    even_at = 2 * jnp.arange(count, dtype=jnp.int32)
    even_sum = jnp.sum(
        steer_phase(children.astype(jnp.float32), shifts, rows_at, even_at, beams_out), axis=0
    )
    odd_sum = jnp.sum(steer_phase(odd_beams, shifts, rows_at, even_at + 1, beams_out), axis=0)
    joined = jnp.stack([even_sum, odd_sum], -1)
    return joined.reshape(even_sum.shape[:-1] + (2 * count,)).astype(jnp.bfloat16)


def odd_local(children, kernel):
    product = jnp.dot(
        children.reshape(-1, children.shape[-1]), kernel, preferred_element_type=jnp.float32
    )
    return product.reshape(children.shape[:-1] + (kernel.shape[1],))


def swap_first(pieces):
    return swapped(pieces, "sub", 0)


def swap_second(pieces):
    return swapped(pieces, "sub", 1)


def keep_and_trade(field, which_bit, swapper):
    length = field.shape[2] // 2
    kept = lax.dynamic_slice_in_dim(field, which_bit * length, length, 2)
    given = lax.dynamic_slice_in_dim(field, (1 - which_bit) * length, length, 2)
    return (jnp.stack([kept, swapper(given)]), length)


def shift_block(offsets, index, per_device):
    return lax.dynamic_slice_in_dim(offsets, index * per_device, per_device, 0)


def body(images, offsets, owners):
    sub_count = lax.axis_size("sub")
    beam_count = lax.axis_size("beam")
    sub_place = lax.axis_index("sub")
    beam_lane = lax.axis_index("beam")
    half_side = lax.axis_index("half")
    low_bit = sub_place % 2
    high_bit = sub_place // 2 % 2
    per_device = images.shape[0]
    half_rows = images.shape[2]
    own_shift = shift_block(offsets, sub_place, per_device)
    mate_shift = shift_block(offsets, jnp.bitwise_xor(sub_place, 1), per_device)
    shifts_one = jnp.stack([own_shift, mate_shift])
    pair_base = sub_place - low_bit
    mate_base = jnp.bitwise_xor(sub_place, 2) - low_bit
    center_own = (
        shift_block(offsets, pair_base, per_device)
        + shift_block(offsets, pair_base + 1, per_device)
    ) * 0.5
    center_mate = (
        shift_block(offsets, mate_base, per_device)
        + shift_block(offsets, mate_base + 1, per_device)
    ) * 0.5
    shifts_two = jnp.stack([center_own, center_mate])
    all_beams = lax.all_to_all(images, "beam", split_axis=2, concat_axis=3, tiled=True)
    block_rows = all_beams.shape[2]
    start_row = half_side * half_rows + beam_lane * block_rows
    children, length = keep_and_trade(all_beams, low_bit, swap_first)
    rows_at = start_row + low_bit * length + jnp.arange(length, dtype=jnp.int32)
    odd_beams = odd_local(children, odd_kernel(B, B))
    first_merge = rotate_sum(children, odd_beams, shifts_one, rows_at, 2 * B)
    children, quarter = keep_and_trade(first_merge, high_bit, swap_second)
    rows_at = (
        start_row + low_bit * length + high_bit * quarter + jnp.arange(quarter, dtype=jnp.int32)
    )
    odd_beams = odd_local(children, odd_kernel(2 * B, 2 * B))
    merged = rotate_sum(children, odd_beams, shifts_two, rows_at, 4 * B)
    sector_tiles = merged.reshape(per_device, 2, quarter, beam_count, sub_count, -1)
    beam_ids = jnp.arange(beam_count, dtype=jnp.int32)[:, None]
    picked = sector_tiles[:, :, :, beam_ids, owners, :]
    outgoing = picked.transpose(4, 3, 0, 1, 5, 2)
    received = lax.all_to_all(
        lax.all_to_all(outgoing, "sub", split_axis=0, concat_axis=0, tiled=True),
        "beam",
        split_axis=1,
        concat_axis=1,
        tiled=True,
    )
    sector_width = received.shape[4]
    received = received.reshape(
        sub_count // 4, 2, 2, beam_count, per_device, 2, sector_width, quarter
    )
    received = received.transpose(0, 4, 5, 6, 3, 2, 1, 7)
    return received.reshape(1, sub_count // 4 * per_device, 2, sector_width, half_rows)


def solution(mesh):
    placed = (P("sub", None, ("swath", "half"), "beam"), P(), P())
    return jax.shard_map(
        body,
        mesh=mesh,
        in_specs=placed,
        out_specs=P(("sub", "beam"), None, None, None, ("swath", "half")),
        check_vma=False,
    )
```

```python
import math

import jax
import numpy as np
import jax.numpy as jnp
from jax import lax
from jax.sharding import Mesh
from jax.sharding import PartitionSpec as P

B = 1024
NR = 1024
GROUP_SUBS = 4


def odd_kernel(beam_total, columns):
    spacing = np.arange(columns, dtype=np.int64)[None, :] - np.arange(beam_total, dtype=np.int64)[:, None]
    parity = np.where(spacing % 2 == 0, 1.0, -1.0).astype(np.float32)
    angles = (2.0 * spacing.astype(np.float32) + np.float32(1.0)) * np.float32(math.pi / (2.0 * beam_total))
    values = parity * np.cos(angles) / (np.float32(beam_total) * np.sin(angles))
    return jnp.asarray(values.astype(np.float32).astype(jnp.bfloat16))


def steer_phase(upsampled, shifts, rows_at, beams_at, beams_out):
    ratios = NR / (NR + rows_at.astype(jnp.float32))
    tilts = (2.0 * beams_at.astype(jnp.float32) + 1.0) / beams_out - 1.0
    phases = ratios[:, None] * tilts[None, :] * shifts[..., None, None]
    cosine = jnp.cos(phases)
    sines = jnp.sin(phases)
    real_part = upsampled[..., 0, :, :]
    imag_part = upsampled[..., 1, :, :]
    return jnp.stack(
        [real_part * cosine - imag_part * sines, real_part * sines + imag_part * cosine], -3
    )


def odd_local(children, kernel):
    product = jnp.dot(
        children.reshape(-1, children.shape[-1]), kernel, preferred_element_type=jnp.float32
    )
    return product.reshape(children.shape[:-1] + (kernel.shape[1],))


def merge_pairs(children, shifts, rows_at, kernel):
    count = children.shape[-1]
    beams_out = 2 * count
    even_at = 2 * jnp.arange(count, dtype=jnp.int32)
    odd_beams = odd_local(children, kernel)
    even_sum = jnp.sum(
        steer_phase(children.astype(jnp.float32), shifts, rows_at, even_at, beams_out), axis=1
    )
    odd_sum = jnp.sum(steer_phase(odd_beams, shifts, rows_at, even_at + 1, beams_out), axis=1)
    joined = jnp.stack([even_sum, odd_sum], -1)
    return joined.reshape(even_sum.shape[:-1] + (beams_out,)).astype(jnp.bfloat16)


def body(images, offsets, owners):
    group_count = lax.axis_size("grp")
    sub_count = group_count * GROUP_SUBS
    beam_count = lax.axis_size("beam")
    group_at = lax.axis_index("grp")
    member_at = lax.axis_index("sub4") * beam_count + lax.axis_index("beam")
    half_side = lax.axis_index("half")
    members = GROUP_SUBS * beam_count
    half_rows = images.shape[2]
    own_rows = half_rows // members
    local_beams = images.shape[3]

    pieces = images[0].reshape(2, members, own_rows, local_beams).transpose(1, 0, 2, 3)
    gathered = lax.all_to_all(pieces, ("sub4", "beam"), 0, 0, tiled=True)
    gathered = gathered.reshape(GROUP_SUBS, beam_count, 2, own_rows, local_beams)
    children = gathered.transpose(0, 2, 3, 1, 4).reshape(
        GROUP_SUBS // 2, 2, 2, own_rows, beam_count * local_beams
    )
    rows_at = half_side * half_rows + member_at * own_rows + jnp.arange(own_rows, dtype=jnp.int32)
    shifts = lax.dynamic_slice_in_dim(offsets, group_at * GROUP_SUBS, GROUP_SUBS, 0)
    shifts_one = shifts.reshape(GROUP_SUBS // 2, 2)
    first = merge_pairs(children, shifts_one, rows_at, odd_kernel(B, B))
    centers = (shifts_one[:, 0] + shifts_one[:, 1]) * 0.5
    merged = merge_pairs(first[None], centers[None], rows_at, odd_kernel(2 * B, 2 * B))[0]

    sector_width = merged.shape[-1] // (beam_count * sub_count)
    tiles = merged.reshape(2, own_rows, beam_count, sub_count, sector_width)
    beam_ids = jnp.arange(beam_count, dtype=jnp.int32)[:, None]
    picked = tiles[:, :, beam_ids, owners, :]
    outgoing = picked.transpose(3, 2, 0, 1, 4).reshape(sub_count * beam_count, 2, own_rows, sector_width)
    received = lax.all_to_all(outgoing, ("grp", "sub4", "beam"), 0, 0, tiled=True)
    received = received.reshape(group_count, members, 2, own_rows, sector_width)
    received = received.transpose(0, 2, 4, 1, 3)
    return received.reshape(1, group_count, 2, sector_width, members * own_rows)


def solution(mesh):
    shape = dict(mesh.shape)
    devices = mesh.devices.reshape(
        shape["swath"], shape["sub"] // GROUP_SUBS, GROUP_SUBS, shape["beam"], shape["half"]
    )
    split = Mesh(devices, ("swath", "grp", "sub4", "beam", "half"))
    placed = (P(("grp", "sub4"), None, ("swath", "half"), "beam"), P(), P())
    return jax.shard_map(
        body,
        mesh=split,
        in_specs=placed,
        out_specs=P(("grp", "sub4", "beam"), None, None, None, ("swath", "half")),
        check_vma=False,
    )
```

```python
import math

import jax
import numpy as np
import jax.numpy as jnp
from jax import lax
from jax.sharding import Mesh
from jax.sharding import PartitionSpec as P

B = 1024
NR = 1024
GROUP_SUBS = 4


def odd_values(beam_total):
    spacing = np.arange(beam_total, dtype=np.int64)[None, :] - np.arange(beam_total, dtype=np.int64)[:, None]
    parity = np.where(spacing % 2 == 0, 1.0, -1.0).astype(np.float32)
    angles = (2.0 * spacing.astype(np.float32) + np.float32(1.0)) * np.float32(math.pi / (2.0 * beam_total))
    values = parity * np.cos(angles) / (np.float32(beam_total) * np.sin(angles))
    return values.astype(np.float32).astype(jnp.bfloat16)


def split_order(beam_total):
    return np.concatenate([np.arange(0, beam_total, 2), np.arange(1, beam_total, 2)])


def spin(parts, scale, lead, first_at, beams_out):
    count = parts.shape[-1]
    lanes = 128
    coarse = jnp.asarray(
        (2.0 * lead * lanes / beams_out) * np.arange(count // lanes) + ((2 * first_at + 1) / beams_out - 1.0),
        jnp.float32,
    )
    fine = jnp.asarray((2.0 * lead / beams_out) * np.arange(lanes), jnp.float32)
    rough = scale[..., None] * coarse
    small = scale[..., None] * fine
    c1 = jnp.cos(rough)[..., None]
    s1 = jnp.sin(rough)[..., None]
    c2 = jnp.cos(small)[..., None, :]
    s2 = jnp.sin(small)[..., None, :]
    cosine = c1 * c2 - s1 * s2
    sines = s1 * c2 + c1 * s2
    grid = parts.shape[:-3] + (parts.shape[-2], count // lanes, lanes)
    real_part = parts[..., 0, :, :].reshape(grid)
    imag_part = parts[..., 1, :, :].reshape(grid)
    turned = jnp.stack(
        [real_part * cosine - imag_part * sines, real_part * sines + imag_part * cosine], -4
    )
    return turned.reshape(parts.shape)


def odd_local(children, kernel):
    product = jnp.dot(
        children.reshape(-1, children.shape[-1]), kernel, preferred_element_type=jnp.float32
    )
    return product.reshape(children.shape[:-1] + (kernel.shape[1],))


def body(images, offsets, owners):
    group_count = lax.axis_size("grp")
    sub_count = group_count * GROUP_SUBS
    beam_count = lax.axis_size("beam")
    group_at = lax.axis_index("grp")
    member_at = lax.axis_index("sub4") * beam_count + lax.axis_index("beam")
    half_side = lax.axis_index("half")
    members = GROUP_SUBS * beam_count
    half_rows = images.shape[2]
    own_rows = half_rows // members
    local_beams = images.shape[3]

    pieces = images[0].reshape(2, members, own_rows, local_beams).transpose(1, 0, 2, 3)
    gathered = lax.all_to_all(pieces, ("sub4", "beam"), 0, 0, tiled=True)
    gathered = gathered.reshape(GROUP_SUBS, beam_count, 2, own_rows, local_beams)
    children = gathered.transpose(0, 2, 3, 1, 4)
    rows_at = half_side * half_rows + member_at * own_rows + jnp.arange(own_rows, dtype=jnp.int32)
    ratios = NR / (NR + rows_at.astype(jnp.float32))
    shifts = lax.dynamic_slice_in_dim(offsets, group_at * GROUP_SUBS, GROUP_SUBS, 0)
    children = children.reshape(GROUP_SUBS, 2, own_rows, B)
    scale_one = shifts[:, None] * ratios[None, :]
    odd_one = odd_local(children, jnp.asarray(odd_values(B)))
    even_one = spin(children.astype(jnp.float32), scale_one, 2, 0, 2 * B)
    odd_one = spin(odd_one, scale_one, 2, 1, 2 * B)
    pairs = (GROUP_SUBS // 2, 2, 2, own_rows, B)
    first = jnp.concatenate(
        [even_one.reshape(pairs).sum(1), odd_one.reshape(pairs).sum(1)], -1
    ).astype(jnp.bfloat16)
    order = split_order(2 * B)
    kernel_two = jnp.asarray(odd_values(2 * B)[order][:, order])
    centers = (shifts[0::2] + shifts[1::2]) * 0.5
    scale_two = centers[:, None] * ratios[None, :]
    odd_two = odd_local(first, kernel_two)
    first_f = first.astype(jnp.float32)
    merged = jnp.stack(
        [
            spin(first_f[..., :B], scale_two, 4, 0, 4 * B).sum(0),
            spin(odd_two[..., :B], scale_two, 4, 1, 4 * B).sum(0),
            spin(first_f[..., B:], scale_two, 4, 2, 4 * B).sum(0),
            spin(odd_two[..., B:], scale_two, 4, 3, 4 * B).sum(0),
        ]
    ).astype(jnp.bfloat16)

    sector_width = 4 * B // (beam_count * sub_count)
    tiles = merged.reshape(4, 2, own_rows, beam_count, sub_count, sector_width // 4)
    beam_ids = jnp.arange(beam_count, dtype=jnp.int32)[:, None]
    picked = tiles[:, :, :, beam_ids, owners, :]
    outgoing = picked.transpose(4, 3, 1, 5, 0, 2).reshape(
        sub_count * beam_count, 2, sector_width, own_rows
    )
    received = lax.all_to_all(outgoing, ("grp", "sub4", "beam"), 0, 0, tiled=True)
    received = received.reshape(group_count, members, 2, sector_width, own_rows)
    received = received.transpose(0, 2, 3, 1, 4)
    return received.reshape(1, group_count, 2, sector_width, members * own_rows)


def solution(mesh):
    shape = dict(mesh.shape)
    devices = mesh.devices.reshape(
        shape["swath"], shape["sub"] // GROUP_SUBS, GROUP_SUBS, shape["beam"], shape["half"]
    )
    split = Mesh(devices, ("swath", "grp", "sub4", "beam", "half"))
    placed = (P(("grp", "sub4"), None, ("swath", "half"), "beam"), P(), P())
    return jax.shard_map(
        body,
        mesh=split,
        in_specs=placed,
        out_specs=P(("grp", "sub4", "beam"), None, None, None, ("swath", "half")),
        check_vma=False,
    )
```

```python
import math

import jax
import numpy as np
import jax.numpy as jnp
from jax import lax
from jax.sharding import Mesh
from jax.sharding import PartitionSpec as P

B = 1024
NR = 1024
GROUP_SUBS = 4
CHUNKS = 2


def odd_values(beam_total):
    spacing = np.arange(beam_total, dtype=np.int64)[None, :] - np.arange(beam_total, dtype=np.int64)[:, None]
    parity = np.where(spacing % 2 == 0, 1.0, -1.0).astype(np.float32)
    angles = (2.0 * spacing.astype(np.float32) + np.float32(1.0)) * np.float32(math.pi / (2.0 * beam_total))
    values = parity * np.cos(angles) / (np.float32(beam_total) * np.sin(angles))
    return values.astype(np.float32).astype(jnp.bfloat16)


def split_order(beam_total):
    return np.concatenate([np.arange(0, beam_total, 2), np.arange(1, beam_total, 2)])


def spin(parts, scale, lead, first_at, beams_out):
    count = parts.shape[-1]
    lanes = 128
    coarse = jnp.asarray(
        (2.0 * lead * lanes / beams_out) * np.arange(count // lanes) + ((2 * first_at + 1) / beams_out - 1.0),
        jnp.float32,
    )
    fine = jnp.asarray((2.0 * lead / beams_out) * np.arange(lanes), jnp.float32)
    rough = scale[..., None] * coarse
    small = scale[..., None] * fine
    c1 = jnp.cos(rough)[..., None]
    s1 = jnp.sin(rough)[..., None]
    c2 = jnp.cos(small)[..., None, :]
    s2 = jnp.sin(small)[..., None, :]
    cosine = c1 * c2 - s1 * s2
    sines = s1 * c2 + c1 * s2
    grid = parts.shape[:-3] + (parts.shape[-2], count // lanes, lanes)
    real_part = parts[..., 0, :, :].reshape(grid)
    imag_part = parts[..., 1, :, :].reshape(grid)
    turned = jnp.stack(
        [real_part * cosine - imag_part * sines, real_part * sines + imag_part * cosine], -4
    )
    return turned.reshape(parts.shape)


def odd_local(children, kernel):
    product = jnp.dot(
        children.reshape(-1, children.shape[-1]), kernel, preferred_element_type=jnp.float32
    )
    return product.reshape(children.shape[:-1] + (kernel.shape[1],))


def merge_rows(children, offsets, rows_at, group_at):
    ratios = NR / (NR + rows_at.astype(jnp.float32))
    shifts = lax.dynamic_slice_in_dim(offsets, group_at * GROUP_SUBS, GROUP_SUBS, 0)
    rows = children.shape[2]
    scale_one = shifts[:, None] * ratios[None, :]
    odd_one = odd_local(children, jnp.asarray(odd_values(B)))
    even_one = spin(children.astype(jnp.float32), scale_one, 2, 0, 2 * B)
    odd_one = spin(odd_one, scale_one, 2, 1, 2 * B)
    pairs = (GROUP_SUBS // 2, 2, 2, rows, B)
    first = jnp.concatenate(
        [even_one.reshape(pairs).sum(1), odd_one.reshape(pairs).sum(1)], -1
    ).astype(jnp.bfloat16)
    order = split_order(2 * B)
    kernel_two = jnp.asarray(odd_values(2 * B)[order][:, order])
    centers = (shifts[0::2] + shifts[1::2]) * 0.5
    scale_two = centers[:, None] * ratios[None, :]
    odd_two = odd_local(first, kernel_two)
    first_f = first.astype(jnp.float32)
    return jnp.stack(
        [
            spin(first_f[..., :B], scale_two, 4, 0, 4 * B).sum(0),
            spin(odd_two[..., :B], scale_two, 4, 1, 4 * B).sum(0),
            spin(first_f[..., B:], scale_two, 4, 2, 4 * B).sum(0),
            spin(odd_two[..., B:], scale_two, 4, 3, 4 * B).sum(0),
        ]
    ).astype(jnp.bfloat16)


def body(images, offsets, owners):
    group_count = lax.axis_size("grp")
    sub_count = group_count * GROUP_SUBS
    beam_count = lax.axis_size("beam")
    group_at = lax.axis_index("grp")
    member_at = lax.axis_index("sub4") * beam_count + lax.axis_index("beam")
    half_side = lax.axis_index("half")
    members = GROUP_SUBS * beam_count
    half_rows = images.shape[2]
    own_rows = half_rows // members
    chunks = CHUNKS if own_rows % (8 * CHUNKS) == 0 else 1
    chunk_rows = own_rows // chunks
    local_beams = images.shape[3]
    sector_width = 4 * B // (beam_count * sub_count)
    beam_ids = jnp.arange(beam_count, dtype=jnp.int32)[:, None]
    split_rows = images[0].reshape(2, members, chunks, chunk_rows, local_beams)
    results = []
    for chunk in range(chunks):
        pieces = split_rows[:, :, chunk].transpose(1, 0, 2, 3)
        gathered = lax.all_to_all(pieces, ("sub4", "beam"), 0, 0, tiled=True)
        gathered = gathered.reshape(GROUP_SUBS, beam_count, 2, chunk_rows, local_beams)
        children = gathered.transpose(0, 2, 3, 1, 4).reshape(GROUP_SUBS, 2, chunk_rows, B)
        rows_at = (
            half_side * half_rows
            + member_at * own_rows
            + chunk * chunk_rows
            + jnp.arange(chunk_rows, dtype=jnp.int32)
        )
        merged = merge_rows(children, offsets, rows_at, group_at)
        tiles = merged.reshape(4, 2, chunk_rows, beam_count, sub_count, sector_width // 4)
        picked = tiles[:, :, :, beam_ids, owners, :]
        outgoing = picked.transpose(4, 3, 1, 5, 0, 2).reshape(
            sub_count * beam_count, 2, sector_width, chunk_rows
        )
        results.append(lax.all_to_all(outgoing, ("grp", "sub4", "beam"), 0, 0, tiled=True))
    received = jnp.stack(results, -2)
    received = received.reshape(group_count, members, 2, sector_width, own_rows)
    received = received.transpose(0, 2, 3, 1, 4)
    return received.reshape(1, group_count, 2, sector_width, members * own_rows)


def solution(mesh):
    shape = dict(mesh.shape)
    devices = mesh.devices.reshape(
        shape["swath"], shape["sub"] // GROUP_SUBS, GROUP_SUBS, shape["beam"], shape["half"]
    )
    split = Mesh(devices, ("swath", "grp", "sub4", "beam", "half"))
    placed = (P(("grp", "sub4"), None, ("swath", "half"), "beam"), P(), P())
    return jax.shard_map(
        body,
        mesh=split,
        in_specs=placed,
        out_specs=P(("grp", "sub4", "beam"), None, None, None, ("swath", "half")),
        check_vma=False,
    )
```

```python
import math

import jax
import numpy as np
import jax.numpy as jnp
from jax import lax
from jax.sharding import Mesh
from jax.sharding import PartitionSpec as P

B = 1024
NR = 1024
GROUP_SUBS = 4


def odd_values(beam_total):
    spacing = np.arange(beam_total, dtype=np.int64)[None, :] - np.arange(beam_total, dtype=np.int64)[:, None]
    parity = np.where(spacing % 2 == 0, 1.0, -1.0).astype(np.float32)
    angles = (2.0 * spacing.astype(np.float32) + np.float32(1.0)) * np.float32(math.pi / (2.0 * beam_total))
    values = parity * np.cos(angles) / (np.float32(beam_total) * np.sin(angles))
    return values.astype(np.float32).astype(jnp.bfloat16)


def split_order(beam_total):
    return np.concatenate([np.arange(0, beam_total, 2), np.arange(1, beam_total, 2)])


def spin(parts, scale, lead, first_at, beams_out):
    count = parts.shape[-1]
    lanes = 128
    coarse = jnp.asarray(
        (2.0 * lead * lanes / beams_out) * np.arange(count // lanes) + ((2 * first_at + 1) / beams_out - 1.0),
        jnp.float32,
    )
    fine = jnp.asarray((2.0 * lead / beams_out) * np.arange(lanes), jnp.float32)
    rough = scale[..., None] * coarse
    small = scale[..., None] * fine
    c1 = jnp.cos(rough)[..., None]
    s1 = jnp.sin(rough)[..., None]
    c2 = jnp.cos(small)[..., None, :]
    s2 = jnp.sin(small)[..., None, :]
    cosine = c1 * c2 - s1 * s2
    sines = s1 * c2 + c1 * s2
    grid = parts.shape[:-3] + (parts.shape[-2], count // lanes, lanes)
    real_part = parts[..., 0, :, :].reshape(grid)
    imag_part = parts[..., 1, :, :].reshape(grid)
    turned = jnp.stack(
        [real_part * cosine - imag_part * sines, real_part * sines + imag_part * cosine], -4
    )
    return turned.reshape(parts.shape)


def odd_local(children, kernel):
    product = jnp.dot(
        children.reshape(-1, children.shape[-1]), kernel, preferred_element_type=jnp.float32
    )
    return product.reshape(children.shape[:-1] + (kernel.shape[1],))


def swap_pieces(pieces, place, axes):
    count = pieces.shape[0]
    flips = jnp.bitwise_xor(place, jnp.arange(count, dtype=jnp.int32))
    ordered = jnp.take(pieces, flips, axis=0)
    moved = [ordered[0]]
    for flip in range(1, count):
        pairs = [(i, i ^ flip) for i in range(count)]
        moved.append(lax.ppermute(ordered[flip], axes, pairs))
    return jnp.take(jnp.stack(moved), flips, axis=0)


def body(images, offsets, owners):
    group_count = lax.axis_size("grp")
    sub_count = group_count * GROUP_SUBS
    beam_count = lax.axis_size("beam")
    group_at = lax.axis_index("grp")
    member_at = lax.axis_index("sub4") * beam_count + lax.axis_index("beam")
    half_side = lax.axis_index("half")
    members = GROUP_SUBS * beam_count
    half_rows = images.shape[2]
    own_rows = half_rows // members
    local_beams = images.shape[3]

    pieces = images[0].reshape(2, members, own_rows, local_beams).transpose(1, 0, 2, 3)
    gathered = lax.all_to_all(pieces, ("sub4", "beam"), 0, 0, tiled=True)
    gathered = gathered.reshape(GROUP_SUBS, beam_count, 2, own_rows, local_beams)
    children = gathered.transpose(0, 2, 3, 1, 4)
    rows_at = half_side * half_rows + member_at * own_rows + jnp.arange(own_rows, dtype=jnp.int32)
    ratios = NR / (NR + rows_at.astype(jnp.float32))
    shifts = lax.dynamic_slice_in_dim(offsets, group_at * GROUP_SUBS, GROUP_SUBS, 0)
    children = children.reshape(GROUP_SUBS, 2, own_rows, B)
    scale_one = shifts[:, None] * ratios[None, :]
    odd_one = odd_local(children, jnp.asarray(odd_values(B)))
    even_one = spin(children.astype(jnp.float32), scale_one, 2, 0, 2 * B)
    odd_one = spin(odd_one, scale_one, 2, 1, 2 * B)
    pairs = (GROUP_SUBS // 2, 2, 2, own_rows, B)
    first = jnp.concatenate(
        [even_one.reshape(pairs).sum(1), odd_one.reshape(pairs).sum(1)], -1
    ).astype(jnp.bfloat16)
    order = split_order(2 * B)
    kernel_two = jnp.asarray(odd_values(2 * B)[order][:, order])
    centers = (shifts[0::2] + shifts[1::2]) * 0.5
    scale_two = centers[:, None] * ratios[None, :]
    odd_two = odd_local(first, kernel_two)
    first_f = first.astype(jnp.float32)
    merged = jnp.stack(
        [
            spin(first_f[..., :B], scale_two, 4, 0, 4 * B).sum(0),
            spin(odd_two[..., :B], scale_two, 4, 1, 4 * B).sum(0),
            spin(first_f[..., B:], scale_two, 4, 2, 4 * B).sum(0),
            spin(odd_two[..., B:], scale_two, 4, 3, 4 * B).sum(0),
        ]
    ).astype(jnp.bfloat16)

    sector_width = 4 * B // (beam_count * sub_count)
    tiles = merged.reshape(4, 2, own_rows, beam_count, sub_count, sector_width // 4)
    beam_ids = jnp.arange(beam_count, dtype=jnp.int32)[:, None]
    picked = tiles[:, :, :, beam_ids, owners, :]
    outgoing = picked.transpose(4, 3, 1, 5, 0, 2).reshape(
        sub_count * beam_count, 2, sector_width, own_rows
    )
    if group_count == 1:
        received = swap_pieces(outgoing, member_at, ("sub4", "beam"))
    else:
        received = lax.all_to_all(outgoing, ("grp", "sub4", "beam"), 0, 0, tiled=True)
    received = received.reshape(group_count, members, 2, sector_width, own_rows)
    received = received.transpose(0, 2, 3, 1, 4)
    return received.reshape(1, group_count, 2, sector_width, members * own_rows)


def solution(mesh):
    shape = dict(mesh.shape)
    devices = mesh.devices.reshape(
        shape["swath"], shape["sub"] // GROUP_SUBS, GROUP_SUBS, shape["beam"], shape["half"]
    )
    split = Mesh(devices, ("swath", "grp", "sub4", "beam", "half"))
    placed = (P(("grp", "sub4"), None, ("swath", "half"), "beam"), P(), P())
    return jax.shard_map(
        body,
        mesh=split,
        in_specs=placed,
        out_specs=P(("grp", "sub4", "beam"), None, None, None, ("swath", "half")),
        check_vma=False,
    )
```

```python
import math

import jax
import numpy as np
import jax.numpy as jnp
from jax import lax
from jax.sharding import Mesh
from jax.sharding import PartitionSpec as P

B = 1024
NR = 1024
GROUP_SUBS = 4


def odd_values(beam_total):
    spacing = np.arange(beam_total, dtype=np.int64)[None, :] - np.arange(beam_total, dtype=np.int64)[:, None]
    parity = np.where(spacing % 2 == 0, 1.0, -1.0).astype(np.float32)
    angles = (2.0 * spacing.astype(np.float32) + np.float32(1.0)) * np.float32(math.pi / (2.0 * beam_total))
    values = parity * np.cos(angles) / (np.float32(beam_total) * np.sin(angles))
    return values.astype(np.float32).astype(jnp.bfloat16)


def split_order(beam_total):
    return np.concatenate([np.arange(0, beam_total, 2), np.arange(1, beam_total, 2)])


def spin(parts, scale, lead, first_at, beams_out):
    count = parts.shape[-1]
    lanes = 128
    coarse = jnp.asarray(
        (2.0 * lead * lanes / beams_out) * np.arange(count // lanes) + ((2 * first_at + 1) / beams_out - 1.0),
        jnp.float32,
    )
    fine = jnp.asarray((2.0 * lead / beams_out) * np.arange(lanes), jnp.float32)
    rough = scale[..., None] * coarse
    small = scale[..., None] * fine
    c1 = jnp.cos(rough)[..., None]
    s1 = jnp.sin(rough)[..., None]
    c2 = jnp.cos(small)[..., None, :]
    s2 = jnp.sin(small)[..., None, :]
    grid = parts.shape[:-3] + (parts.shape[-2], count // lanes, lanes)
    real_part = parts[..., 0, :, :].reshape(grid)
    imag_part = parts[..., 1, :, :].reshape(grid)
    real_fine = real_part * c2 - imag_part * s2
    imag_fine = real_part * s2 + imag_part * c2
    turned = jnp.stack(
        [real_fine * c1 - imag_fine * s1, real_fine * s1 + imag_fine * c1], -4
    )
    return turned.reshape(parts.shape)


def odd_local(children, kernel):
    product = jnp.dot(
        children.reshape(-1, children.shape[-1]), kernel, preferred_element_type=jnp.float32
    )
    return product.reshape(children.shape[:-1] + (kernel.shape[1],))


def swap_sectors(tiles, owners, place, beam_count):
    count = tiles.shape[3] * tiles.shape[4]
    flips = jnp.bitwise_xor(place, jnp.arange(count, dtype=jnp.int32))
    shard_ids = flips % beam_count
    sector_ids = owners[shard_ids, flips // beam_count]
    ordered = tiles[:, :, :, shard_ids, sector_ids, :].transpose(3, 0, 1, 2, 4)
    moved = [ordered[0]]
    for flip in range(1, count):
        pairs = [(i, i ^ flip) for i in range(count)]
        moved.append(lax.ppermute(ordered[flip], ("sub4", "beam"), pairs))
    senders = jnp.take(jnp.stack(moved), flips, axis=0)
    return senders.transpose(2, 4, 1, 0, 3)


def body(images, offsets, owners):
    group_count = lax.axis_size("grp")
    sub_count = group_count * GROUP_SUBS
    beam_count = lax.axis_size("beam")
    group_at = lax.axis_index("grp")
    member_at = lax.axis_index("sub4") * beam_count + lax.axis_index("beam")
    half_side = lax.axis_index("half")
    members = GROUP_SUBS * beam_count
    half_rows = images.shape[2]
    own_rows = half_rows // members
    local_beams = images.shape[3]

    pieces = images[0].reshape(2, members, own_rows, local_beams).transpose(1, 0, 2, 3)
    gathered = lax.all_to_all(pieces, ("sub4", "beam"), 0, 0, tiled=True)
    gathered = gathered.reshape(GROUP_SUBS, beam_count, 2, own_rows, local_beams)
    children = gathered.transpose(0, 2, 3, 1, 4)
    rows_at = half_side * half_rows + member_at * own_rows + jnp.arange(own_rows, dtype=jnp.int32)
    ratios = NR / (NR + rows_at.astype(jnp.float32))
    shifts = lax.dynamic_slice_in_dim(offsets, group_at * GROUP_SUBS, GROUP_SUBS, 0)
    children = children.reshape(GROUP_SUBS, 2, own_rows, B)
    scale_one = shifts[:, None] * ratios[None, :]
    odd_one = odd_local(children, jnp.asarray(odd_values(B)))
    even_one = spin(children.astype(jnp.float32), scale_one, 2, 0, 2 * B)
    odd_one = spin(odd_one, scale_one, 2, 1, 2 * B)
    pairs = (GROUP_SUBS // 2, 2, 2, own_rows, B)
    first = jnp.concatenate(
        [even_one.reshape(pairs).sum(1), odd_one.reshape(pairs).sum(1)], -1
    ).astype(jnp.bfloat16)
    order = split_order(2 * B)
    kernel_two = jnp.asarray(odd_values(2 * B)[order][:, order])
    centers = (shifts[0::2] + shifts[1::2]) * 0.5
    scale_two = centers[:, None] * ratios[None, :]
    odd_two = odd_local(first, kernel_two)
    first_f = first.astype(jnp.float32)
    merged = jnp.stack(
        [
            spin(first_f[..., :B], scale_two, 4, 0, 4 * B).sum(0),
            spin(odd_two[..., :B], scale_two, 4, 1, 4 * B).sum(0),
            spin(first_f[..., B:], scale_two, 4, 2, 4 * B).sum(0),
            spin(odd_two[..., B:], scale_two, 4, 3, 4 * B).sum(0),
        ]
    ).astype(jnp.bfloat16)

    sector_width = 4 * B // (beam_count * sub_count)
    tiles = merged.reshape(4, 2, own_rows, beam_count, sub_count, sector_width // 4)
    if group_count == 1:
        received = swap_sectors(tiles, owners, member_at, beam_count)
        return received.reshape(1, 1, 2, sector_width, members * own_rows)
    beam_ids = jnp.arange(beam_count, dtype=jnp.int32)[:, None]
    picked = tiles[:, :, :, beam_ids, owners, :]
    outgoing = picked.transpose(4, 3, 1, 5, 0, 2).reshape(
        sub_count * beam_count, 2, sector_width, own_rows
    )
    received = lax.all_to_all(outgoing, ("grp", "sub4", "beam"), 0, 0, tiled=True)
    received = received.reshape(group_count, members, 2, sector_width, own_rows)
    received = received.transpose(0, 2, 3, 1, 4)
    return received.reshape(1, group_count, 2, sector_width, members * own_rows)


def solution(mesh):
    shape = dict(mesh.shape)
    devices = mesh.devices.reshape(
        shape["swath"], shape["sub"] // GROUP_SUBS, GROUP_SUBS, shape["beam"], shape["half"]
    )
    split = Mesh(devices, ("swath", "grp", "sub4", "beam", "half"))
    placed = (P(("grp", "sub4"), None, ("swath", "half"), "beam"), P(), P())
    return jax.shard_map(
        body,
        mesh=split,
        in_specs=placed,
        out_specs=P(("grp", "sub4", "beam"), None, None, None, ("swath", "half")),
        check_vma=False,
    )
```

```python
import math

import jax
import numpy as np
import jax.numpy as jnp
from jax import lax
from jax.experimental import pallas as pl
from jax.experimental.pallas import tpu as pltpu
from jax.sharding import Mesh
from jax.sharding import PartitionSpec as P

B = 1024
NR = 1024
GROUP_SUBS = 4


def odd_values(beam_total):
    spacing = np.arange(beam_total, dtype=np.int64)[None, :] - np.arange(beam_total, dtype=np.int64)[:, None]
    parity = np.where(spacing % 2 == 0, 1.0, -1.0).astype(np.float32)
    angles = (2.0 * spacing.astype(np.float32) + np.float32(1.0)) * np.float32(math.pi / (2.0 * beam_total))
    values = parity * np.cos(angles) / (np.float32(beam_total) * np.sin(angles))
    return values.astype(np.float32).astype(jnp.bfloat16)


def split_order(beam_total):
    return np.concatenate([np.arange(0, beam_total, 2), np.arange(1, beam_total, 2)])


def spin(parts, scale, lead, first_at, beams_out):
    count = parts.shape[-1]
    lanes = 128
    coarse = jnp.asarray(
        (2.0 * lead * lanes / beams_out) * np.arange(count // lanes) + ((2 * first_at + 1) / beams_out - 1.0),
        jnp.float32,
    )
    fine = jnp.asarray((2.0 * lead / beams_out) * np.arange(lanes), jnp.float32)
    rough = scale[..., None] * coarse
    small = scale[..., None] * fine
    c1 = jnp.cos(rough)[..., None]
    s1 = jnp.sin(rough)[..., None]
    c2 = jnp.cos(small)[..., None, :]
    s2 = jnp.sin(small)[..., None, :]
    cosine = c1 * c2 - s1 * s2
    sines = s1 * c2 + c1 * s2
    grid = parts.shape[:-3] + (parts.shape[-2], count // lanes, lanes)
    real_part = parts[..., 0, :, :].reshape(grid)
    imag_part = parts[..., 1, :, :].reshape(grid)
    turned = jnp.stack(
        [real_part * cosine - imag_part * sines, real_part * sines + imag_part * cosine], -4
    )
    return turned.reshape(parts.shape)


def odd_local(children, kernel):
    product = jnp.dot(
        children.reshape(-1, children.shape[-1]), kernel, preferred_element_type=jnp.float32
    )
    return product.reshape(children.shape[:-1] + (kernel.shape[1],))


LANES = 128


def merge_kernel(x_ref, t1c, t1s, f1c, f1s, t2c, t2s, f2c, f2s, k1_hbm, k2_hbm, o_ref,
                 k1_v, k2_v, first_v, odd1_v, odd2_v, sems):
    members, _, rows, local = x_ref.shape
    beam_count = members // 4
    blocks = local // LANES
    wide = beam_count * blocks
    half = wide * LANES
    load_one = pltpu.make_async_copy(k1_hbm, k1_v, sems.at[0])
    load_two = pltpu.make_async_copy(k2_hbm, k2_v, sems.at[1])
    load_one.start()
    load_two.start()

    def turn(xr, xi, c1, s1, c2, s2):
        cosine = c1 * c2 - s1 * s2
        sines = s1 * c2 + c1 * s2
        return xr * cosine - xi * sines, xr * sines + xi * cosine

    for pair in range(2):
        for u in range(wide):
            b, k = divmod(u, blocks)
            cols = pl.ds(k * LANES, LANES)
            re_sum = None
            for m in range(2):
                s = 2 * pair + m
                xr = x_ref[s * beam_count + b, 0, :, cols].astype(jnp.float32)
                xi = x_ref[s * beam_count + b, 1, :, cols].astype(jnp.float32)
                re, im = turn(xr, xi, t1c[s, 0, u], t1s[s, 0, u], f1c[s], f1s[s])
                re_sum = re if re_sum is None else re_sum + re
                im_sum = im if m == 0 else im_sum + im
            out_cols = pl.ds(u * LANES, LANES)
            first_v[pair, pl.ds(0, rows), out_cols] = re_sum.astype(first_v.dtype)
            first_v[pair, pl.ds(rows, rows), out_cols] = im_sum.astype(first_v.dtype)

    load_one.wait()
    for s in range(4):
        total = None
        for b in range(beam_count):
            part = x_ref[s * beam_count + b].reshape(2 * rows, local)
            term = jnp.dot(part, k1_v[pl.ds(b * local, local), :], preferred_element_type=jnp.float32)
            total = term if total is None else total + term
        odd1_v[s] = total

    for pair in range(2):
        for u in range(wide):
            cols = pl.ds(u * LANES, LANES)
            for m in range(2):
                s = 2 * pair + m
                xr = odd1_v[s, pl.ds(0, rows), cols]
                xi = odd1_v[s, pl.ds(rows, rows), cols]
                re, im = turn(xr, xi, t1c[s, 1, u], t1s[s, 1, u], f1c[s], f1s[s])
                re_sum = re if m == 0 else re_sum + re
                im_sum = im if m == 0 else im_sum + im
            out_cols = pl.ds(half + u * LANES, LANES)
            first_v[pair, pl.ds(0, rows), out_cols] = re_sum.astype(first_v.dtype)
            first_v[pair, pl.ds(rows, rows), out_cols] = im_sum.astype(first_v.dtype)

    load_two.wait()
    for pair in range(2):
        odd2_v[pair] = jnp.dot(first_v[pair], k2_v[...], preferred_element_type=jnp.float32)

    for t in range(4):
        for u in range(wide):
            at = (t // 2) * half + u * LANES if t % 2 == 0 else (t // 2) * half + u * LANES
            cols = pl.ds(at, LANES)
            for pair in range(2):
                if t % 2 == 0:
                    xr = first_v[pair, pl.ds(0, rows), cols].astype(jnp.float32)
                    xi = first_v[pair, pl.ds(rows, rows), cols].astype(jnp.float32)
                else:
                    xr = odd2_v[pair, pl.ds(0, rows), cols]
                    xi = odd2_v[pair, pl.ds(rows, rows), cols]
                re, im = turn(xr, xi, t2c[pair, t, u], t2s[pair, t, u], f2c[pair], f2s[pair])
                re_sum = re if pair == 0 else re_sum + re
                im_sum = im if pair == 0 else im_sum + im
            o_ref[t, 0, :, pl.ds(u * LANES, LANES)] = re_sum.astype(o_ref.dtype)
            o_ref[t, 1, :, pl.ds(u * LANES, LANES)] = im_sum.astype(o_ref.dtype)


def merge_call(x, tables, k1, k2, interpret=False):
    members, _, rows, local = x.shape
    width = k1.shape[0]
    vmem = pl.BlockSpec(memory_space=pltpu.VMEM)
    hbm = pl.BlockSpec(memory_space=pl.ANY)
    return pl.pallas_call(
        merge_kernel,
        out_shape=jax.ShapeDtypeStruct((4, 2, rows, width), jnp.bfloat16),
        in_specs=[vmem] * 9 + [hbm, hbm],
        out_specs=vmem,
        scratch_shapes=[
            pltpu.VMEM((width, width), jnp.bfloat16),
            pltpu.VMEM((2 * width, 2 * width), jnp.bfloat16),
            pltpu.VMEM((2, 2 * rows, 2 * width), jnp.bfloat16),
            pltpu.VMEM((4, 2 * rows, width), jnp.float32),
            pltpu.VMEM((2, 2 * rows, 2 * width), jnp.float32),
            pltpu.SemaphoreType.DMA((2,)),
        ],
        compiler_params=pltpu.CompilerParams(vmem_limit_bytes=48 * 1024 * 1024),
        interpret=interpret,
    )(x, *tables, k1, k2)


def merge_tables(shifts, ratios, width):
    units = np.arange(width // LANES)
    fine = jnp.asarray(np.arange(LANES) / 512.0, jnp.float32)
    scale_one = shifts[:, None] * ratios[None, :]
    coarse_one = jnp.asarray(
        [0.25 * units + ((2 * t + 1) / (2 * width) - 1.0) for t in range(2)], jnp.float32
    )
    rough_one = (scale_one[:, None, None, :] * coarse_one[None, :, :, None])[..., None]
    small_one = scale_one[:, :, None] * fine
    centers = (shifts[0::2] + shifts[1::2]) * 0.5
    scale_two = centers[:, None] * ratios[None, :]
    coarse_two = jnp.asarray(
        [0.25 * units + ((2 * t + 1) / (4 * width) - 1.0) for t in range(4)], jnp.float32
    )
    rough_two = (scale_two[:, None, None, :] * coarse_two[None, :, :, None])[..., None]
    small_two = scale_two[:, :, None] * fine
    return (jnp.cos(rough_one), jnp.sin(rough_one), jnp.cos(small_one), jnp.sin(small_one),
            jnp.cos(rough_two), jnp.sin(rough_two), jnp.cos(small_two), jnp.sin(small_two))


def swap_pieces(pieces, place, axes):
    count = pieces.shape[0]
    flips = jnp.bitwise_xor(place, jnp.arange(count, dtype=jnp.int32))
    ordered = jnp.take(pieces, flips, axis=0)
    moved = [ordered[0]]
    for flip in range(1, count):
        pairs = [(i, i ^ flip) for i in range(count)]
        moved.append(lax.ppermute(ordered[flip], axes, pairs))
    return jnp.take(jnp.stack(moved), flips, axis=0)


def body(images, offsets, owners):
    group_count = lax.axis_size("grp")
    sub_count = group_count * GROUP_SUBS
    beam_count = lax.axis_size("beam")
    group_at = lax.axis_index("grp")
    member_at = lax.axis_index("sub4") * beam_count + lax.axis_index("beam")
    half_side = lax.axis_index("half")
    members = GROUP_SUBS * beam_count
    half_rows = images.shape[2]
    own_rows = half_rows // members
    local_beams = images.shape[3]

    pieces = images[0].reshape(2, members, own_rows, local_beams).transpose(1, 0, 2, 3)
    gathered = lax.all_to_all(pieces, ("sub4", "beam"), 0, 0, tiled=True)
    rows_at = half_side * half_rows + member_at * own_rows + jnp.arange(own_rows, dtype=jnp.int32)
    ratios = NR / (NR + rows_at.astype(jnp.float32))
    shifts = lax.dynamic_slice_in_dim(offsets, group_at * GROUP_SUBS, GROUP_SUBS, 0)
    order = split_order(2 * B)
    merged = merge_call(
        gathered,
        merge_tables(shifts, ratios, B),
        jnp.asarray(odd_values(B)),
        jnp.asarray(odd_values(2 * B)[order][:, order]),
    )

    sector_width = 4 * B // (beam_count * sub_count)
    tiles = merged.reshape(4, 2, own_rows, beam_count, sub_count, sector_width // 4)
    beam_ids = jnp.arange(beam_count, dtype=jnp.int32)[:, None]
    picked = tiles[:, :, :, beam_ids, owners, :]
    outgoing = picked.transpose(4, 3, 1, 5, 0, 2).reshape(
        sub_count * beam_count, 2, sector_width, own_rows
    )
    if group_count == 1:
        received = swap_pieces(outgoing, member_at, ("sub4", "beam"))
    else:
        received = lax.all_to_all(outgoing, ("grp", "sub4", "beam"), 0, 0, tiled=True)
    received = received.reshape(group_count, members, 2, sector_width, own_rows)
    received = received.transpose(0, 2, 3, 1, 4)
    return received.reshape(1, group_count, 2, sector_width, members * own_rows)


def solution(mesh):
    shape = dict(mesh.shape)
    devices = mesh.devices.reshape(
        shape["swath"], shape["sub"] // GROUP_SUBS, GROUP_SUBS, shape["beam"], shape["half"]
    )
    split = Mesh(devices, ("swath", "grp", "sub4", "beam", "half"))
    placed = (P(("grp", "sub4"), None, ("swath", "half"), "beam"), P(), P())
    return jax.shard_map(
        body,
        mesh=split,
        in_specs=placed,
        out_specs=P(("grp", "sub4", "beam"), None, None, None, ("swath", "half")),
        check_vma=False,
    )
```

```python
import math

import jax
import numpy as np
import jax.numpy as jnp
from jax import lax
from jax.experimental import pallas as pl
from jax.experimental.pallas import tpu as pltpu
from jax.sharding import Mesh
from jax.sharding import PartitionSpec as P

B = 1024
NR = 1024
GROUP_SUBS = 4


def odd_values(beam_total):
    spacing = np.arange(beam_total, dtype=np.int64)[None, :] - np.arange(beam_total, dtype=np.int64)[:, None]
    parity = np.where(spacing % 2 == 0, 1.0, -1.0).astype(np.float32)
    angles = (2.0 * spacing.astype(np.float32) + np.float32(1.0)) * np.float32(math.pi / (2.0 * beam_total))
    values = parity * np.cos(angles) / (np.float32(beam_total) * np.sin(angles))
    return values.astype(np.float32).astype(jnp.bfloat16)


def split_order(beam_total):
    return np.concatenate([np.arange(0, beam_total, 2), np.arange(1, beam_total, 2)])


def spin(parts, scale, lead, first_at, beams_out):
    count = parts.shape[-1]
    lanes = 128
    coarse = jnp.asarray(
        (2.0 * lead * lanes / beams_out) * np.arange(count // lanes) + ((2 * first_at + 1) / beams_out - 1.0),
        jnp.float32,
    )
    fine = jnp.asarray((2.0 * lead / beams_out) * np.arange(lanes), jnp.float32)
    rough = scale[..., None] * coarse
    small = scale[..., None] * fine
    c1 = jnp.cos(rough)[..., None]
    s1 = jnp.sin(rough)[..., None]
    c2 = jnp.cos(small)[..., None, :]
    s2 = jnp.sin(small)[..., None, :]
    cosine = c1 * c2 - s1 * s2
    sines = s1 * c2 + c1 * s2
    grid = parts.shape[:-3] + (parts.shape[-2], count // lanes, lanes)
    real_part = parts[..., 0, :, :].reshape(grid)
    imag_part = parts[..., 1, :, :].reshape(grid)
    turned = jnp.stack(
        [real_part * cosine - imag_part * sines, real_part * sines + imag_part * cosine], -4
    )
    return turned.reshape(parts.shape)


def odd_local(children, kernel):
    product = jnp.dot(
        children.reshape(-1, children.shape[-1]), kernel, preferred_element_type=jnp.float32
    )
    return product.reshape(children.shape[:-1] + (kernel.shape[1],))


LANES = 128


def merge_kernel(slot_ref, x_ref, t1c, t1s, f1c, f1s, t2c, t2s, f2c, f2s, k1_hbm, k2_hbm, o_ref,
                 k1_v, k2_v, first_v, odd1_v, odd2_v, sems):
    members, _, rows, local = x_ref.shape
    beam_count = members // 4
    blocks = local // LANES
    wide = beam_count * blocks
    half = wide * LANES
    load_one = pltpu.make_async_copy(k1_hbm, k1_v, sems.at[0])
    load_two = pltpu.make_async_copy(k2_hbm, k2_v, sems.at[1])
    load_one.start()
    load_two.start()

    def turn(xr, xi, c1, s1, c2, s2):
        cosine = c1 * c2 - s1 * s2
        sines = s1 * c2 + c1 * s2
        return xr * cosine - xi * sines, xr * sines + xi * cosine

    for pair in range(2):
        for u in range(wide):
            b, k = divmod(u, blocks)
            cols = pl.ds(k * LANES, LANES)
            re_sum = None
            for m in range(2):
                s = 2 * pair + m
                xr = x_ref[s * beam_count + b, 0, :, cols].astype(jnp.float32)
                xi = x_ref[s * beam_count + b, 1, :, cols].astype(jnp.float32)
                re, im = turn(xr, xi, t1c[s, 0, u], t1s[s, 0, u], f1c[s], f1s[s])
                re_sum = re if re_sum is None else re_sum + re
                im_sum = im if m == 0 else im_sum + im
            out_cols = pl.ds(u * LANES, LANES)
            first_v[pair, pl.ds(0, rows), out_cols] = re_sum.astype(first_v.dtype)
            first_v[pair, pl.ds(rows, rows), out_cols] = im_sum.astype(first_v.dtype)

    load_one.wait()
    for s in range(4):
        total = None
        for b in range(beam_count):
            part = x_ref[s * beam_count + b].reshape(2 * rows, local)
            term = jnp.dot(part, k1_v[pl.ds(b * local, local), :], preferred_element_type=jnp.float32)
            total = term if total is None else total + term
        odd1_v[s] = total

    for pair in range(2):
        for u in range(wide):
            cols = pl.ds(u * LANES, LANES)
            for m in range(2):
                s = 2 * pair + m
                xr = odd1_v[s, pl.ds(0, rows), cols]
                xi = odd1_v[s, pl.ds(rows, rows), cols]
                re, im = turn(xr, xi, t1c[s, 1, u], t1s[s, 1, u], f1c[s], f1s[s])
                re_sum = re if m == 0 else re_sum + re
                im_sum = im if m == 0 else im_sum + im
            out_cols = pl.ds(half + u * LANES, LANES)
            first_v[pair, pl.ds(0, rows), out_cols] = re_sum.astype(first_v.dtype)
            first_v[pair, pl.ds(rows, rows), out_cols] = im_sum.astype(first_v.dtype)

    load_two.wait()
    for pair in range(2):
        odd2_v[pair] = jnp.dot(first_v[pair], k2_v[...], preferred_element_type=jnp.float32)

    for t in range(4):
        for u in range(wide):
            at = (t // 2) * half + u * LANES if t % 2 == 0 else (t // 2) * half + u * LANES
            cols = pl.ds(at, LANES)
            for pair in range(2):
                if t % 2 == 0:
                    xr = first_v[pair, pl.ds(0, rows), cols].astype(jnp.float32)
                    xi = first_v[pair, pl.ds(rows, rows), cols].astype(jnp.float32)
                else:
                    xr = odd2_v[pair, pl.ds(0, rows), cols]
                    xi = odd2_v[pair, pl.ds(rows, rows), cols]
                re, im = turn(xr, xi, t2c[pair, t, u], t2s[pair, t, u], f2c[pair], f2s[pair])
                re_sum = re if pair == 0 else re_sum + re
                im_sum = im if pair == 0 else im_sum + im
            slot = slot_ref[u]
            o_ref[slot, t, 0] = re_sum.astype(o_ref.dtype)
            o_ref[slot, t, 1] = im_sum.astype(o_ref.dtype)


def merge_call(slots, x, tables, k1, k2, interpret=False):
    members, _, rows, local = x.shape
    width = k1.shape[0]
    vmem = pl.BlockSpec(memory_space=pltpu.VMEM)
    hbm = pl.BlockSpec(memory_space=pl.ANY)
    smem = pl.BlockSpec(memory_space=pltpu.SMEM)
    return pl.pallas_call(
        merge_kernel,
        out_shape=jax.ShapeDtypeStruct((width // LANES, 4, 2, rows, LANES), jnp.bfloat16),
        in_specs=[smem] + [vmem] * 9 + [hbm, hbm],
        out_specs=vmem,
        scratch_shapes=[
            pltpu.VMEM((width, width), jnp.bfloat16),
            pltpu.VMEM((2 * width, 2 * width), jnp.bfloat16),
            pltpu.VMEM((2, 2 * rows, 2 * width), jnp.bfloat16),
            pltpu.VMEM((4, 2 * rows, width), jnp.float32),
            pltpu.VMEM((2, 2 * rows, 2 * width), jnp.float32),
            pltpu.SemaphoreType.DMA((2,)),
        ],
        compiler_params=pltpu.CompilerParams(vmem_limit_bytes=48 * 1024 * 1024),
        interpret=interpret,
    )(slots, x, *tables, k1, k2)


def merge_tables(shifts, ratios, width):
    units = np.arange(width // LANES)
    fine = jnp.asarray(np.arange(LANES) / 512.0, jnp.float32)
    scale_one = shifts[:, None] * ratios[None, :]
    coarse_one = jnp.asarray(
        [0.25 * units + ((2 * t + 1) / (2 * width) - 1.0) for t in range(2)], jnp.float32
    )
    rough_one = (scale_one[:, None, None, :] * coarse_one[None, :, :, None])[..., None]
    small_one = scale_one[:, :, None] * fine
    centers = (shifts[0::2] + shifts[1::2]) * 0.5
    scale_two = centers[:, None] * ratios[None, :]
    coarse_two = jnp.asarray(
        [0.25 * units + ((2 * t + 1) / (4 * width) - 1.0) for t in range(4)], jnp.float32
    )
    rough_two = (scale_two[:, None, None, :] * coarse_two[None, :, :, None])[..., None]
    small_two = scale_two[:, :, None] * fine
    return (jnp.cos(rough_one), jnp.sin(rough_one), jnp.cos(small_one), jnp.sin(small_one),
            jnp.cos(rough_two), jnp.sin(rough_two), jnp.cos(small_two), jnp.sin(small_two))


def swap_ordered(ordered, place, axes):
    count = ordered.shape[0]
    moved = [ordered[0]]
    for flip in range(1, count):
        pairs = [(i, i ^ flip) for i in range(count)]
        moved.append(lax.ppermute(ordered[flip], axes, pairs))
    flips = jnp.bitwise_xor(place, jnp.arange(count, dtype=jnp.int32))
    return jnp.take(jnp.stack(moved), flips, axis=0)


def body(images, offsets, owners):
    group_count = lax.axis_size("grp")
    sub_count = group_count * GROUP_SUBS
    beam_count = lax.axis_size("beam")
    group_at = lax.axis_index("grp")
    member_at = lax.axis_index("sub4") * beam_count + lax.axis_index("beam")
    half_side = lax.axis_index("half")
    members = GROUP_SUBS * beam_count
    half_rows = images.shape[2]
    own_rows = half_rows // members
    local_beams = images.shape[3]

    pieces = images[0].reshape(2, members, own_rows, local_beams).transpose(1, 0, 2, 3)
    gathered = lax.all_to_all(pieces, ("sub4", "beam"), 0, 0, tiled=True)
    rows_at = half_side * half_rows + member_at * own_rows + jnp.arange(own_rows, dtype=jnp.int32)
    ratios = NR / (NR + rows_at.astype(jnp.float32))
    shifts = lax.dynamic_slice_in_dim(offsets, group_at * GROUP_SUBS, GROUP_SUBS, 0)
    order = split_order(2 * B)
    blocks = B // LANES
    sector_width = 4 * B // (beam_count * sub_count)
    direct = group_count == 1 and sector_width == 4 * LANES
    if direct:
        shard_of = jnp.arange(blocks, dtype=jnp.int32) // sub_count
        sector_of = jnp.arange(blocks, dtype=jnp.int32) % sub_count
        holder = jnp.argmax(owners[shard_of] == sector_of[:, None], axis=1).astype(jnp.int32)
        slots = jnp.bitwise_xor(member_at, holder * beam_count + shard_of)
    else:
        slots = jnp.arange(blocks, dtype=jnp.int32)
    merged = merge_call(
        slots,
        gathered,
        merge_tables(shifts, ratios, B),
        jnp.asarray(odd_values(B)),
        jnp.asarray(odd_values(2 * B)[order][:, order]),
    )
    if direct:
        ordered = merged.transpose(0, 2, 4, 1, 3).reshape(blocks, 2, sector_width, own_rows)
        received = swap_ordered(ordered, member_at, ("sub4", "beam"))
        received = received.transpose(1, 2, 0, 3)
        return received.reshape(1, 1, 2, sector_width, members * own_rows)
    merged = merged.transpose(1, 2, 3, 0, 4).reshape(4, 2, own_rows, B)

    tiles = merged.reshape(4, 2, own_rows, beam_count, sub_count, sector_width // 4)
    beam_ids = jnp.arange(beam_count, dtype=jnp.int32)[:, None]
    picked = tiles[:, :, :, beam_ids, owners, :]
    outgoing = picked.transpose(4, 3, 1, 5, 0, 2).reshape(
        sub_count * beam_count, 2, sector_width, own_rows
    )
    received = lax.all_to_all(outgoing, ("grp", "sub4", "beam"), 0, 0, tiled=True)
    received = received.reshape(group_count, members, 2, sector_width, own_rows)
    received = received.transpose(0, 2, 3, 1, 4)
    return received.reshape(1, group_count, 2, sector_width, members * own_rows)


def solution(mesh):
    shape = dict(mesh.shape)
    devices = mesh.devices.reshape(
        shape["swath"], shape["sub"] // GROUP_SUBS, GROUP_SUBS, shape["beam"], shape["half"]
    )
    split = Mesh(devices, ("swath", "grp", "sub4", "beam", "half"))
    placed = (P(("grp", "sub4"), None, ("swath", "half"), "beam"), P(), P())
    return jax.shard_map(
        body,
        mesh=split,
        in_specs=placed,
        out_specs=P(("grp", "sub4", "beam"), None, None, None, ("swath", "half")),
        check_vma=False,
    )
```

```python
import math

import jax
import numpy as np
import jax.numpy as jnp
from jax import lax
from jax.experimental import pallas as pl
from jax.experimental.pallas import tpu as pltpu
from jax.sharding import Mesh
from jax.sharding import PartitionSpec as P

B = 1024
NR = 1024
GROUP_SUBS = 4


def odd_values(beam_total):
    spacing = np.arange(beam_total, dtype=np.int64)[None, :] - np.arange(beam_total, dtype=np.int64)[:, None]
    parity = np.where(spacing % 2 == 0, 1.0, -1.0).astype(np.float32)
    angles = (2.0 * spacing.astype(np.float32) + np.float32(1.0)) * np.float32(math.pi / (2.0 * beam_total))
    values = parity * np.cos(angles) / (np.float32(beam_total) * np.sin(angles))
    return values.astype(np.float32).astype(jnp.bfloat16)


def split_order(beam_total):
    return np.concatenate([np.arange(0, beam_total, 2), np.arange(1, beam_total, 2)])


def spin(parts, scale, lead, first_at, beams_out):
    count = parts.shape[-1]
    lanes = 128
    coarse = jnp.asarray(
        (2.0 * lead * lanes / beams_out) * np.arange(count // lanes) + ((2 * first_at + 1) / beams_out - 1.0),
        jnp.float32,
    )
    fine = jnp.asarray((2.0 * lead / beams_out) * np.arange(lanes), jnp.float32)
    rough = scale[..., None] * coarse
    small = scale[..., None] * fine
    c1 = jnp.cos(rough)[..., None]
    s1 = jnp.sin(rough)[..., None]
    c2 = jnp.cos(small)[..., None, :]
    s2 = jnp.sin(small)[..., None, :]
    cosine = c1 * c2 - s1 * s2
    sines = s1 * c2 + c1 * s2
    grid = parts.shape[:-3] + (parts.shape[-2], count // lanes, lanes)
    real_part = parts[..., 0, :, :].reshape(grid)
    imag_part = parts[..., 1, :, :].reshape(grid)
    turned = jnp.stack(
        [real_part * cosine - imag_part * sines, real_part * sines + imag_part * cosine], -4
    )
    return turned.reshape(parts.shape)


def odd_local(children, kernel):
    product = jnp.dot(
        children.reshape(-1, children.shape[-1]), kernel, preferred_element_type=jnp.float32
    )
    return product.reshape(children.shape[:-1] + (kernel.shape[1],))


LANES = 128


def merge_kernel(slot_ref, sender_ref, x_ref, t1c, t1s, f1c, f1s, t2c, t2s, f2c, f2s, k1_hbm, k2_hbm, o_ref,
                 k1_v, k2_v, first_v, odd1_v, odd2_v, sems):
    members, _, rows, local = x_ref.shape
    beam_count = members // 4
    blocks = local // LANES
    wide = beam_count * blocks
    half = wide * LANES
    load_one = pltpu.make_async_copy(k1_hbm, k1_v, sems.at[0])
    load_two = pltpu.make_async_copy(k2_hbm, k2_v, sems.at[1])
    load_one.start()
    load_two.start()

    def turn(xr, xi, c1, s1, c2, s2):
        cosine = c1 * c2 - s1 * s2
        sines = s1 * c2 + c1 * s2
        return xr * cosine - xi * sines, xr * sines + xi * cosine

    for pair in range(2):
        for u in range(wide):
            b, k = divmod(u, blocks)
            cols = pl.ds(k * LANES, LANES)
            re_sum = None
            for m in range(2):
                s = 2 * pair + m
                xr = x_ref[sender_ref[s * beam_count + b], 0, :, cols].astype(jnp.float32)
                xi = x_ref[sender_ref[s * beam_count + b], 1, :, cols].astype(jnp.float32)
                re, im = turn(xr, xi, t1c[s, 0, u], t1s[s, 0, u], f1c[s], f1s[s])
                re_sum = re if re_sum is None else re_sum + re
                im_sum = im if m == 0 else im_sum + im
            out_cols = pl.ds(u * LANES, LANES)
            first_v[pair, pl.ds(0, rows), out_cols] = re_sum.astype(first_v.dtype)
            first_v[pair, pl.ds(rows, rows), out_cols] = im_sum.astype(first_v.dtype)

    load_one.wait()
    for s in range(4):
        total = None
        for b in range(beam_count):
            part = x_ref[sender_ref[s * beam_count + b]].reshape(2 * rows, local)
            term = jnp.dot(part, k1_v[pl.ds(b * local, local), :], preferred_element_type=jnp.float32)
            total = term if total is None else total + term
        odd1_v[s] = total

    for pair in range(2):
        for u in range(wide):
            cols = pl.ds(u * LANES, LANES)
            for m in range(2):
                s = 2 * pair + m
                xr = odd1_v[s, pl.ds(0, rows), cols]
                xi = odd1_v[s, pl.ds(rows, rows), cols]
                re, im = turn(xr, xi, t1c[s, 1, u], t1s[s, 1, u], f1c[s], f1s[s])
                re_sum = re if m == 0 else re_sum + re
                im_sum = im if m == 0 else im_sum + im
            out_cols = pl.ds(half + u * LANES, LANES)
            first_v[pair, pl.ds(0, rows), out_cols] = re_sum.astype(first_v.dtype)
            first_v[pair, pl.ds(rows, rows), out_cols] = im_sum.astype(first_v.dtype)

    load_two.wait()
    for pair in range(2):
        odd2_v[pair] = jnp.dot(first_v[pair], k2_v[...], preferred_element_type=jnp.float32)

    for t in range(4):
        for u in range(wide):
            at = (t // 2) * half + u * LANES if t % 2 == 0 else (t // 2) * half + u * LANES
            cols = pl.ds(at, LANES)
            for pair in range(2):
                if t % 2 == 0:
                    xr = first_v[pair, pl.ds(0, rows), cols].astype(jnp.float32)
                    xi = first_v[pair, pl.ds(rows, rows), cols].astype(jnp.float32)
                else:
                    xr = odd2_v[pair, pl.ds(0, rows), cols]
                    xi = odd2_v[pair, pl.ds(rows, rows), cols]
                re, im = turn(xr, xi, t2c[pair, t, u], t2s[pair, t, u], f2c[pair], f2s[pair])
                re_sum = re if pair == 0 else re_sum + re
                im_sum = im if pair == 0 else im_sum + im
            slot = slot_ref[u]
            o_ref[slot, t, 0] = re_sum.astype(o_ref.dtype)
            o_ref[slot, t, 1] = im_sum.astype(o_ref.dtype)


def merge_call(slots, senders, x, tables, k1, k2, interpret=False):
    members, _, rows, local = x.shape
    width = k1.shape[0]
    vmem = pl.BlockSpec(memory_space=pltpu.VMEM)
    hbm = pl.BlockSpec(memory_space=pl.ANY)
    smem = pl.BlockSpec(memory_space=pltpu.SMEM)
    return pl.pallas_call(
        merge_kernel,
        out_shape=jax.ShapeDtypeStruct((width // LANES, 4, 2, rows, LANES), jnp.bfloat16),
        in_specs=[smem, smem] + [vmem] * 9 + [hbm, hbm],
        out_specs=vmem,
        scratch_shapes=[
            pltpu.VMEM((width, width), jnp.bfloat16),
            pltpu.VMEM((2 * width, 2 * width), jnp.bfloat16),
            pltpu.VMEM((2, 2 * rows, 2 * width), jnp.bfloat16),
            pltpu.VMEM((4, 2 * rows, width), jnp.float32),
            pltpu.VMEM((2, 2 * rows, 2 * width), jnp.float32),
            pltpu.SemaphoreType.DMA((2,)),
        ],
        compiler_params=pltpu.CompilerParams(vmem_limit_bytes=48 * 1024 * 1024),
        interpret=interpret,
    )(slots, senders, x, *tables, k1, k2)


def merge_tables(shifts, ratios, width):
    units = np.arange(width // LANES)
    fine = jnp.asarray(np.arange(LANES) / 512.0, jnp.float32)
    scale_one = shifts[:, None] * ratios[None, :]
    coarse_one = jnp.asarray(
        [0.25 * units + ((2 * t + 1) / (2 * width) - 1.0) for t in range(2)], jnp.float32
    )
    rough_one = scale_one[:, None, None, :] * coarse_one[None, :, :, None]
    small_one = scale_one[:, :, None] * fine
    centers = (shifts[0::2] + shifts[1::2]) * 0.5
    scale_two = centers[:, None] * ratios[None, :]
    coarse_two = jnp.asarray(
        [0.25 * units + ((2 * t + 1) / (4 * width) - 1.0) for t in range(4)], jnp.float32
    )
    rough_two = scale_two[:, None, None, :] * coarse_two[None, :, :, None]
    small_two = scale_two[:, :, None] * fine
    compact = lax.optimization_barrier(
        (jnp.cos(rough_one), jnp.sin(rough_one), jnp.cos(rough_two), jnp.sin(rough_two))
    )
    c1, s1, c2, s2 = (part[..., None] for part in compact)
    return (c1, s1, jnp.cos(small_one), jnp.sin(small_one),
            c2, s2, jnp.cos(small_two), jnp.sin(small_two))


def swap_ordered(ordered, place, axes):
    count = ordered.shape[0]
    moved = [ordered[0]]
    for flip in range(1, count):
        pairs = [(i, i ^ flip) for i in range(count)]
        moved.append(lax.ppermute(ordered[flip], axes, pairs))
    flips = jnp.bitwise_xor(place, jnp.arange(count, dtype=jnp.int32))
    return jnp.take(jnp.stack(moved), flips, axis=0)


def body(images, offsets, owners):
    group_count = lax.axis_size("grp")
    sub_count = group_count * GROUP_SUBS
    beam_count = lax.axis_size("beam")
    group_at = lax.axis_index("grp")
    member_at = lax.axis_index("sub4") * beam_count + lax.axis_index("beam")
    half_side = lax.axis_index("half")
    members = GROUP_SUBS * beam_count
    half_rows = images.shape[2]
    own_rows = half_rows // members
    local_beams = images.shape[3]

    flips = jnp.bitwise_xor(member_at, jnp.arange(members, dtype=jnp.int32))
    image = images[0]
    moved = [lax.dynamic_slice_in_dim(image, member_at * own_rows, own_rows, 1)]
    for flip in range(1, members):
        piece = lax.dynamic_slice_in_dim(image, flips[flip] * own_rows, own_rows, 1)
        pairs = [(i, i ^ flip) for i in range(members)]
        moved.append(lax.ppermute(piece, ("sub4", "beam"), pairs))
    gathered = jnp.stack(moved)
    rows_at = half_side * half_rows + member_at * own_rows + jnp.arange(own_rows, dtype=jnp.int32)
    ratios = NR / (NR + rows_at.astype(jnp.float32))
    shifts = lax.dynamic_slice_in_dim(offsets, group_at * GROUP_SUBS, GROUP_SUBS, 0)
    order = split_order(2 * B)
    blocks = B // LANES
    sector_width = 4 * B // (beam_count * sub_count)
    direct = group_count == 1 and sector_width == 4 * LANES
    if direct:
        shard_of = jnp.arange(blocks, dtype=jnp.int32) // sub_count
        sector_of = jnp.arange(blocks, dtype=jnp.int32) % sub_count
        holder = jnp.argmax(owners[shard_of] == sector_of[:, None], axis=1).astype(jnp.int32)
        slots = jnp.bitwise_xor(member_at, holder * beam_count + shard_of)
    else:
        slots = jnp.arange(blocks, dtype=jnp.int32)
    merged = merge_call(
        slots,
        flips,
        gathered,
        merge_tables(shifts, ratios, B),
        jnp.asarray(odd_values(B)),
        jnp.asarray(odd_values(2 * B)[order][:, order]),
    )
    if direct:
        ordered = merged.transpose(0, 2, 4, 1, 3).reshape(blocks, 2, sector_width, own_rows)
        received = swap_ordered(ordered, member_at, ("sub4", "beam"))
        received = received.transpose(1, 2, 0, 3)
        return received.reshape(1, 1, 2, sector_width, members * own_rows)
    merged = merged.transpose(1, 2, 3, 0, 4).reshape(4, 2, own_rows, B)

    tiles = merged.reshape(4, 2, own_rows, beam_count, sub_count, sector_width // 4)
    beam_ids = jnp.arange(beam_count, dtype=jnp.int32)[:, None]
    picked = tiles[:, :, :, beam_ids, owners, :]
    outgoing = picked.transpose(4, 3, 1, 5, 0, 2).reshape(
        sub_count * beam_count, 2, sector_width, own_rows
    )
    received = lax.all_to_all(outgoing, ("grp", "sub4", "beam"), 0, 0, tiled=True)
    received = received.reshape(group_count, members, 2, sector_width, own_rows)
    received = received.transpose(0, 2, 3, 1, 4)
    return received.reshape(1, group_count, 2, sector_width, members * own_rows)


def solution(mesh):
    shape = dict(mesh.shape)
    devices = mesh.devices.reshape(
        shape["swath"], shape["sub"] // GROUP_SUBS, GROUP_SUBS, shape["beam"], shape["half"]
    )
    split = Mesh(devices, ("swath", "grp", "sub4", "beam", "half"))
    placed = (P(("grp", "sub4"), None, ("swath", "half"), "beam"), P(), P())
    return jax.shard_map(
        body,
        mesh=split,
        in_specs=placed,
        out_specs=P(("grp", "sub4", "beam"), None, None, None, ("swath", "half")),
        check_vma=False,
    )
```

```python
import math

import jax
import numpy as np
import jax.numpy as jnp
from jax import lax
from jax.experimental import pallas as pl
from jax.experimental.pallas import tpu as pltpu
from jax.sharding import Mesh
from jax.sharding import PartitionSpec as P

B = 1024
NR = 1024
GROUP_SUBS = 4


def odd_values(beam_total):
    spacing = np.arange(beam_total, dtype=np.int64)[None, :] - np.arange(beam_total, dtype=np.int64)[:, None]
    parity = np.where(spacing % 2 == 0, 1.0, -1.0).astype(np.float32)
    angles = (2.0 * spacing.astype(np.float32) + np.float32(1.0)) * np.float32(math.pi / (2.0 * beam_total))
    values = parity * np.cos(angles) / (np.float32(beam_total) * np.sin(angles))
    return values.astype(np.float32).astype(jnp.bfloat16)


def split_order(beam_total):
    return np.concatenate([np.arange(0, beam_total, 2), np.arange(1, beam_total, 2)])


def spin(parts, scale, lead, first_at, beams_out):
    count = parts.shape[-1]
    lanes = 128
    coarse = jnp.asarray(
        (2.0 * lead * lanes / beams_out) * np.arange(count // lanes) + ((2 * first_at + 1) / beams_out - 1.0),
        jnp.float32,
    )
    fine = jnp.asarray((2.0 * lead / beams_out) * np.arange(lanes), jnp.float32)
    rough = scale[..., None] * coarse
    small = scale[..., None] * fine
    c1 = jnp.cos(rough)[..., None]
    s1 = jnp.sin(rough)[..., None]
    c2 = jnp.cos(small)[..., None, :]
    s2 = jnp.sin(small)[..., None, :]
    cosine = c1 * c2 - s1 * s2
    sines = s1 * c2 + c1 * s2
    grid = parts.shape[:-3] + (parts.shape[-2], count // lanes, lanes)
    real_part = parts[..., 0, :, :].reshape(grid)
    imag_part = parts[..., 1, :, :].reshape(grid)
    turned = jnp.stack(
        [real_part * cosine - imag_part * sines, real_part * sines + imag_part * cosine], -4
    )
    return turned.reshape(parts.shape)


def odd_local(children, kernel):
    product = jnp.dot(
        children.reshape(-1, children.shape[-1]), kernel, preferred_element_type=jnp.float32
    )
    return product.reshape(children.shape[:-1] + (kernel.shape[1],))


LANES = 128


def merge_kernel(slot_ref, x_ref, t1c, t1s, f1c, f1s, t2c, t2s, f2c, f2s, k1_hbm, k2_hbm, o_ref,
                 k1_v, k2_v, first_v, odd1_v, odd2_v, sems):
    members, _, rows, local = x_ref.shape
    beam_count = members // 4
    blocks = local // LANES
    wide = beam_count * blocks
    half = wide * LANES
    load_one = pltpu.make_async_copy(k1_hbm, k1_v, sems.at[0])
    load_two = pltpu.make_async_copy(k2_hbm, k2_v, sems.at[1])
    load_one.start()
    load_two.start()

    def turn(xr, xi, c1, s1, c2, s2):
        cosine = c1 * c2 - s1 * s2
        sines = s1 * c2 + c1 * s2
        return xr * cosine - xi * sines, xr * sines + xi * cosine

    for pair in range(2):
        for u in range(wide):
            b, k = divmod(u, blocks)
            cols = pl.ds(k * LANES, LANES)
            re_sum = None
            for m in range(2):
                s = 2 * pair + m
                xr = x_ref[s * beam_count + b, 0, :, cols].astype(jnp.float32)
                xi = x_ref[s * beam_count + b, 1, :, cols].astype(jnp.float32)
                re, im = turn(xr, xi, t1c[s, 0, u], t1s[s, 0, u], f1c[s], f1s[s])
                re_sum = re if re_sum is None else re_sum + re
                im_sum = im if m == 0 else im_sum + im
            out_cols = pl.ds(u * LANES, LANES)
            first_v[pair, pl.ds(0, rows), out_cols] = re_sum.astype(first_v.dtype)
            first_v[pair, pl.ds(rows, rows), out_cols] = im_sum.astype(first_v.dtype)

    load_one.wait()
    for s in range(4):
        total = None
        for b in range(beam_count):
            part = x_ref[s * beam_count + b].reshape(2 * rows, local)
            term = jnp.dot(part, k1_v[pl.ds(b * local, local), :], preferred_element_type=jnp.float32)
            total = term if total is None else total + term
        odd1_v[s] = total

    for pair in range(2):
        for u in range(wide):
            cols = pl.ds(u * LANES, LANES)
            for m in range(2):
                s = 2 * pair + m
                xr = odd1_v[s, pl.ds(0, rows), cols]
                xi = odd1_v[s, pl.ds(rows, rows), cols]
                re, im = turn(xr, xi, t1c[s, 1, u], t1s[s, 1, u], f1c[s], f1s[s])
                re_sum = re if m == 0 else re_sum + re
                im_sum = im if m == 0 else im_sum + im
            out_cols = pl.ds(half + u * LANES, LANES)
            first_v[pair, pl.ds(0, rows), out_cols] = re_sum.astype(first_v.dtype)
            first_v[pair, pl.ds(rows, rows), out_cols] = im_sum.astype(first_v.dtype)

    load_two.wait()
    for pair in range(2):
        odd2_v[pair] = jnp.dot(first_v[pair], k2_v[...], preferred_element_type=jnp.float32)

    for t in range(4):
        for u in range(wide):
            at = (t // 2) * half + u * LANES if t % 2 == 0 else (t // 2) * half + u * LANES
            cols = pl.ds(at, LANES)
            for pair in range(2):
                if t % 2 == 0:
                    xr = first_v[pair, pl.ds(0, rows), cols].astype(jnp.float32)
                    xi = first_v[pair, pl.ds(rows, rows), cols].astype(jnp.float32)
                else:
                    xr = odd2_v[pair, pl.ds(0, rows), cols]
                    xi = odd2_v[pair, pl.ds(rows, rows), cols]
                re, im = turn(xr, xi, t2c[pair, t, u], t2s[pair, t, u], f2c[pair], f2s[pair])
                re_sum = re if pair == 0 else re_sum + re
                im_sum = im if pair == 0 else im_sum + im
            slot = slot_ref[u]
            o_ref[slot, t, 0] = re_sum.astype(o_ref.dtype)
            o_ref[slot, t, 1] = im_sum.astype(o_ref.dtype)


def merge_call(slots, x, tables, k1, k2, interpret=False):
    members, _, rows, local = x.shape
    width = k1.shape[0]
    vmem = pl.BlockSpec(memory_space=pltpu.VMEM)
    hbm = pl.BlockSpec(memory_space=pl.ANY)
    smem = pl.BlockSpec(memory_space=pltpu.SMEM)
    return pl.pallas_call(
        merge_kernel,
        out_shape=jax.ShapeDtypeStruct((width // LANES, 4, 2, rows, LANES), jnp.bfloat16),
        in_specs=[smem] + [vmem] * 9 + [hbm, hbm],
        out_specs=vmem,
        scratch_shapes=[
            pltpu.VMEM((width, width), jnp.bfloat16),
            pltpu.VMEM((2 * width, 2 * width), jnp.bfloat16),
            pltpu.VMEM((2, 2 * rows, 2 * width), jnp.bfloat16),
            pltpu.VMEM((4, 2 * rows, width), jnp.float32),
            pltpu.VMEM((2, 2 * rows, 2 * width), jnp.float32),
            pltpu.SemaphoreType.DMA((2,)),
        ],
        compiler_params=pltpu.CompilerParams(vmem_limit_bytes=48 * 1024 * 1024),
        interpret=interpret,
    )(slots, x, *tables, k1, k2)


def merge_tables(shifts, ratios, width):
    units = np.arange(width // LANES)
    fine = jnp.asarray(np.arange(LANES) / 512.0, jnp.float32)
    scale_one = shifts[:, None] * ratios[None, :]
    coarse_one = jnp.asarray(
        [0.25 * units + ((2 * t + 1) / (2 * width) - 1.0) for t in range(2)], jnp.float32
    )
    rough_one = (scale_one[:, None, None, :] * coarse_one[None, :, :, None])[..., None]
    small_one = scale_one[:, :, None] * fine
    centers = (shifts[0::2] + shifts[1::2]) * 0.5
    scale_two = centers[:, None] * ratios[None, :]
    coarse_two = jnp.asarray(
        [0.25 * units + ((2 * t + 1) / (4 * width) - 1.0) for t in range(4)], jnp.float32
    )
    rough_two = (scale_two[:, None, None, :] * coarse_two[None, :, :, None])[..., None]
    small_two = scale_two[:, :, None] * fine
    return (jnp.cos(rough_one), jnp.sin(rough_one), jnp.cos(small_one), jnp.sin(small_one),
            jnp.cos(rough_two), jnp.sin(rough_two), jnp.cos(small_two), jnp.sin(small_two))


def flip_order(count, beam_count):
    rest = sorted(range(1, count), key=lambda f: (-(f // beam_count), f))
    return np.array([0] + rest, dtype=np.int32)


def swap_ordered(ordered, place, axes, order):
    count = ordered.shape[0]
    moved = [ordered[0]]
    for at in range(1, count):
        flip = int(order[at])
        pairs = [(i, i ^ flip) for i in range(count)]
        moved.append(lax.ppermute(ordered[at], axes, pairs))
    position = jnp.asarray(np.argsort(order).astype(np.int32))
    senders = position[jnp.bitwise_xor(place, jnp.arange(count, dtype=jnp.int32))]
    return jnp.take(jnp.stack(moved), senders, axis=0)


def body(images, offsets, owners):
    group_count = lax.axis_size("grp")
    sub_count = group_count * GROUP_SUBS
    beam_count = lax.axis_size("beam")
    group_at = lax.axis_index("grp")
    member_at = lax.axis_index("sub4") * beam_count + lax.axis_index("beam")
    half_side = lax.axis_index("half")
    members = GROUP_SUBS * beam_count
    half_rows = images.shape[2]
    own_rows = half_rows // members
    local_beams = images.shape[3]

    pieces = images[0].reshape(2, members, own_rows, local_beams).transpose(1, 0, 2, 3)
    gathered = lax.all_to_all(pieces, ("sub4", "beam"), 0, 0, tiled=True)
    rows_at = half_side * half_rows + member_at * own_rows + jnp.arange(own_rows, dtype=jnp.int32)
    ratios = NR / (NR + rows_at.astype(jnp.float32))
    shifts = lax.dynamic_slice_in_dim(offsets, group_at * GROUP_SUBS, GROUP_SUBS, 0)
    order = split_order(2 * B)
    blocks = B // LANES
    sector_width = 4 * B // (beam_count * sub_count)
    direct = group_count == 1 and sector_width == 4 * LANES
    if direct:
        shard_of = jnp.arange(blocks, dtype=jnp.int32) // sub_count
        sector_of = jnp.arange(blocks, dtype=jnp.int32) % sub_count
        holder = jnp.argmax(owners[shard_of] == sector_of[:, None], axis=1).astype(jnp.int32)
        sequence = flip_order(members, beam_count)
        position = jnp.asarray(np.argsort(sequence).astype(np.int32))
        slots = position[jnp.bitwise_xor(member_at, holder * beam_count + shard_of)]
    else:
        slots = jnp.arange(blocks, dtype=jnp.int32)
    merged = merge_call(
        slots,
        gathered,
        merge_tables(shifts, ratios, B),
        jnp.asarray(odd_values(B)),
        jnp.asarray(odd_values(2 * B)[order][:, order]),
    )
    if direct:
        ordered = merged.transpose(0, 2, 4, 1, 3).reshape(blocks, 2, sector_width, own_rows)
        received = swap_ordered(ordered, member_at, ("sub4", "beam"), sequence)
        received = received.transpose(1, 2, 0, 3)
        return received.reshape(1, 1, 2, sector_width, members * own_rows)
    merged = merged.transpose(1, 2, 3, 0, 4).reshape(4, 2, own_rows, B)

    tiles = merged.reshape(4, 2, own_rows, beam_count, sub_count, sector_width // 4)
    beam_ids = jnp.arange(beam_count, dtype=jnp.int32)[:, None]
    picked = tiles[:, :, :, beam_ids, owners, :]
    outgoing = picked.transpose(4, 3, 1, 5, 0, 2).reshape(
        sub_count * beam_count, 2, sector_width, own_rows
    )
    received = lax.all_to_all(outgoing, ("grp", "sub4", "beam"), 0, 0, tiled=True)
    received = received.reshape(group_count, members, 2, sector_width, own_rows)
    received = received.transpose(0, 2, 3, 1, 4)
    return received.reshape(1, group_count, 2, sector_width, members * own_rows)


def solution(mesh):
    shape = dict(mesh.shape)
    devices = mesh.devices.reshape(
        shape["swath"], shape["sub"] // GROUP_SUBS, GROUP_SUBS, shape["beam"], shape["half"]
    )
    split = Mesh(devices, ("swath", "grp", "sub4", "beam", "half"))
    placed = (P(("grp", "sub4"), None, ("swath", "half"), "beam"), P(), P())
    return jax.shard_map(
        body,
        mesh=split,
        in_specs=placed,
        out_specs=P(("grp", "sub4", "beam"), None, None, None, ("swath", "half")),
        check_vma=False,
    )
```

```python
import math

import jax
import numpy as np
import jax.numpy as jnp
from jax import lax
from jax.experimental import pallas as pl
from jax.experimental.pallas import tpu as pltpu
from jax.sharding import Mesh
from jax.sharding import PartitionSpec as P

B = 1024
NR = 1024
GROUP_SUBS = 4


def odd_values(beam_total):
    spacing = np.arange(beam_total, dtype=np.int64)[None, :] - np.arange(beam_total, dtype=np.int64)[:, None]
    parity = np.where(spacing % 2 == 0, 1.0, -1.0).astype(np.float32)
    angles = (2.0 * spacing.astype(np.float32) + np.float32(1.0)) * np.float32(math.pi / (2.0 * beam_total))
    values = parity * np.cos(angles) / (np.float32(beam_total) * np.sin(angles))
    return values.astype(np.float32).astype(jnp.bfloat16)


def split_order(beam_total):
    return np.concatenate([np.arange(0, beam_total, 2), np.arange(1, beam_total, 2)])


def spin(parts, scale, lead, first_at, beams_out):
    count = parts.shape[-1]
    lanes = 128
    coarse = jnp.asarray(
        (2.0 * lead * lanes / beams_out) * np.arange(count // lanes) + ((2 * first_at + 1) / beams_out - 1.0),
        jnp.float32,
    )
    fine = jnp.asarray((2.0 * lead / beams_out) * np.arange(lanes), jnp.float32)
    rough = scale[..., None] * coarse
    small = scale[..., None] * fine
    c1 = jnp.cos(rough)[..., None]
    s1 = jnp.sin(rough)[..., None]
    c2 = jnp.cos(small)[..., None, :]
    s2 = jnp.sin(small)[..., None, :]
    cosine = c1 * c2 - s1 * s2
    sines = s1 * c2 + c1 * s2
    grid = parts.shape[:-3] + (parts.shape[-2], count // lanes, lanes)
    real_part = parts[..., 0, :, :].reshape(grid)
    imag_part = parts[..., 1, :, :].reshape(grid)
    turned = jnp.stack(
        [real_part * cosine - imag_part * sines, real_part * sines + imag_part * cosine], -4
    )
    return turned.reshape(parts.shape)


def odd_local(children, kernel):
    product = jnp.dot(
        children.reshape(-1, children.shape[-1]), kernel, preferred_element_type=jnp.float32
    )
    return product.reshape(children.shape[:-1] + (kernel.shape[1],))


LANES = 128


TILE = 256


def toeplitz_tiles(matrix):
    count = matrix.shape[0] // TILE
    tiles = []
    for gap in range(-(count - 1), count):
        i = max(0, -gap)
        j = i + gap
        tiles.append(matrix[i * TILE:(i + 1) * TILE, j * TILE:(j + 1) * TILE])
    tiles = np.stack(tiles)
    for i in range(count):
        for j in range(count):
            assert np.array_equal(matrix[i * TILE:(i + 1) * TILE, j * TILE:(j + 1) * TILE], tiles[j - i + count - 1])
    return tiles


def kernel_tables(width):
    one = toeplitz_tiles(odd_values(width))
    order = split_order(2 * width)
    two = odd_values(2 * width)[order][:, order]
    assert np.array_equal(two[:width, :width], two[width:, width:])
    quads = np.stack([toeplitz_tiles(two[:width, :width]), toeplitz_tiles(two[:width, width:]),
                      toeplitz_tiles(two[width:, :width])])
    return jnp.asarray(one), jnp.asarray(quads)


def merge_kernel(slot_ref, x_ref, t1c, t1s, f1c, f1s, t2c, t2s, f2c, f2s, k1_hbm, k2_hbm, o_ref,
                 k1_v, k2_v, first_v, odd1_v, odd2_v, sems):
    members, _, rows, local = x_ref.shape
    beam_count = members // 4
    blocks = local // LANES
    wide = beam_count * blocks
    half = wide * LANES
    load_one = pltpu.make_async_copy(k1_hbm, k1_v, sems.at[0])
    load_two = pltpu.make_async_copy(k2_hbm, k2_v, sems.at[1])
    load_one.start()
    load_two.start()

    def turn(xr, xi, c1, s1, c2, s2):
        cosine = c1 * c2 - s1 * s2
        sines = s1 * c2 + c1 * s2
        return xr * cosine - xi * sines, xr * sines + xi * cosine

    for pair in range(2):
        for u in range(wide):
            b, k = divmod(u, blocks)
            cols = pl.ds(k * LANES, LANES)
            re_sum = None
            for m in range(2):
                s = 2 * pair + m
                xr = x_ref[s * beam_count + b, 0, :, cols].astype(jnp.float32)
                xi = x_ref[s * beam_count + b, 1, :, cols].astype(jnp.float32)
                re, im = turn(xr, xi, t1c[s, 0, u], t1s[s, 0, u], f1c[s], f1s[s])
                re_sum = re if re_sum is None else re_sum + re
                im_sum = im if m == 0 else im_sum + im
            out_cols = pl.ds(u * LANES, LANES)
            first_v[pair, pl.ds(0, rows), out_cols] = re_sum.astype(first_v.dtype)
            first_v[pair, pl.ds(rows, rows), out_cols] = im_sum.astype(first_v.dtype)

    load_one.wait()
    count = half // TILE
    per_piece = local // TILE
    for s in range(4):
        parts = []
        for i in range(count):
            b, k = divmod(i, per_piece)
            piece = x_ref[s * beam_count + b, :, :, pl.ds(k * TILE, TILE)]
            parts.append(piece.reshape(2 * rows, TILE))
        for j in range(count):
            total = None
            for i in range(count):
                term = jnp.dot(parts[i], k1_v[j - i + count - 1], preferred_element_type=jnp.float32)
                total = term if total is None else total + term
            odd1_v[s, :, pl.ds(j * TILE, TILE)] = total

    for pair in range(2):
        for u in range(wide):
            cols = pl.ds(u * LANES, LANES)
            for m in range(2):
                s = 2 * pair + m
                xr = odd1_v[s, pl.ds(0, rows), cols]
                xi = odd1_v[s, pl.ds(rows, rows), cols]
                re, im = turn(xr, xi, t1c[s, 1, u], t1s[s, 1, u], f1c[s], f1s[s])
                re_sum = re if m == 0 else re_sum + re
                im_sum = im if m == 0 else im_sum + im
            out_cols = pl.ds(half + u * LANES, LANES)
            first_v[pair, pl.ds(0, rows), out_cols] = re_sum.astype(first_v.dtype)
            first_v[pair, pl.ds(rows, rows), out_cols] = im_sum.astype(first_v.dtype)

    load_two.wait()
    for pair in range(2):
        evens = [first_v[pair, :, pl.ds(i * TILE, TILE)] for i in range(count)]
        odds = [first_v[pair, :, pl.ds(half + i * TILE, TILE)] for i in range(count)]
        for j in range(count):
            even_out = None
            odd_out = None
            for i in range(count):
                gap = j - i + count - 1
                term_e = jnp.dot(evens[i], k2_v[0, gap], preferred_element_type=jnp.float32)
                term_e += jnp.dot(odds[i], k2_v[2, gap], preferred_element_type=jnp.float32)
                term_o = jnp.dot(evens[i], k2_v[1, gap], preferred_element_type=jnp.float32)
                term_o += jnp.dot(odds[i], k2_v[0, gap], preferred_element_type=jnp.float32)
                even_out = term_e if even_out is None else even_out + term_e
                odd_out = term_o if odd_out is None else odd_out + term_o
            odd2_v[pair, :, pl.ds(j * TILE, TILE)] = even_out
            odd2_v[pair, :, pl.ds(half + j * TILE, TILE)] = odd_out

    for t in range(4):
        for u in range(wide):
            at = (t // 2) * half + u * LANES if t % 2 == 0 else (t // 2) * half + u * LANES
            cols = pl.ds(at, LANES)
            for pair in range(2):
                if t % 2 == 0:
                    xr = first_v[pair, pl.ds(0, rows), cols].astype(jnp.float32)
                    xi = first_v[pair, pl.ds(rows, rows), cols].astype(jnp.float32)
                else:
                    xr = odd2_v[pair, pl.ds(0, rows), cols]
                    xi = odd2_v[pair, pl.ds(rows, rows), cols]
                re, im = turn(xr, xi, t2c[pair, t, u], t2s[pair, t, u], f2c[pair], f2s[pair])
                re_sum = re if pair == 0 else re_sum + re
                im_sum = im if pair == 0 else im_sum + im
            slot = slot_ref[u]
            o_ref[slot, t, 0] = re_sum.astype(o_ref.dtype)
            o_ref[slot, t, 1] = im_sum.astype(o_ref.dtype)


def merge_call(slots, x, tables, k1, k2, interpret=False):
    members, _, rows, local = x.shape
    width = local * members // 4
    vmem = pl.BlockSpec(memory_space=pltpu.VMEM)
    hbm = pl.BlockSpec(memory_space=pl.ANY)
    smem = pl.BlockSpec(memory_space=pltpu.SMEM)
    return pl.pallas_call(
        merge_kernel,
        out_shape=jax.ShapeDtypeStruct((width // LANES, 4, 2, rows, LANES), jnp.bfloat16),
        in_specs=[smem] + [vmem] * 9 + [hbm, hbm],
        out_specs=vmem,
        scratch_shapes=[
            pltpu.VMEM(k1.shape, jnp.bfloat16),
            pltpu.VMEM(k2.shape, jnp.bfloat16),
            pltpu.VMEM((2, 2 * rows, 2 * width), jnp.bfloat16),
            pltpu.VMEM((4, 2 * rows, width), jnp.float32),
            pltpu.VMEM((2, 2 * rows, 2 * width), jnp.float32),
            pltpu.SemaphoreType.DMA((2,)),
        ],
        compiler_params=pltpu.CompilerParams(vmem_limit_bytes=48 * 1024 * 1024),
        interpret=interpret,
    )(slots, x, *tables, k1, k2)


def merge_tables(shifts, ratios, width):
    units = np.arange(width // LANES)
    fine = jnp.asarray(np.arange(LANES) / 512.0, jnp.float32)
    scale_one = shifts[:, None] * ratios[None, :]
    coarse_one = jnp.asarray(
        [0.25 * units + ((2 * t + 1) / (2 * width) - 1.0) for t in range(2)], jnp.float32
    )
    rough_one = (scale_one[:, None, None, :] * coarse_one[None, :, :, None])[..., None]
    small_one = scale_one[:, :, None] * fine
    centers = (shifts[0::2] + shifts[1::2]) * 0.5
    scale_two = centers[:, None] * ratios[None, :]
    coarse_two = jnp.asarray(
        [0.25 * units + ((2 * t + 1) / (4 * width) - 1.0) for t in range(4)], jnp.float32
    )
    rough_two = (scale_two[:, None, None, :] * coarse_two[None, :, :, None])[..., None]
    small_two = scale_two[:, :, None] * fine
    return (jnp.cos(rough_one), jnp.sin(rough_one), jnp.cos(small_one), jnp.sin(small_one),
            jnp.cos(rough_two), jnp.sin(rough_two), jnp.cos(small_two), jnp.sin(small_two))


def flip_order(count, beam_count):
    rest = sorted(range(1, count), key=lambda f: (-(f // beam_count), f))
    return np.array([0] + rest, dtype=np.int32)


def swap_ordered(ordered, place, axes, order):
    count = ordered.shape[0]
    moved = [ordered[0]]
    for at in range(1, count):
        flip = int(order[at])
        pairs = [(i, i ^ flip) for i in range(count)]
        moved.append(lax.ppermute(ordered[at], axes, pairs))
    position = jnp.asarray(np.argsort(order).astype(np.int32))
    senders = position[jnp.bitwise_xor(place, jnp.arange(count, dtype=jnp.int32))]
    return jnp.take(jnp.stack(moved), senders, axis=0)


def body(images, offsets, owners):
    group_count = lax.axis_size("grp")
    sub_count = group_count * GROUP_SUBS
    beam_count = lax.axis_size("beam")
    group_at = lax.axis_index("grp")
    member_at = lax.axis_index("sub4") * beam_count + lax.axis_index("beam")
    half_side = lax.axis_index("half")
    members = GROUP_SUBS * beam_count
    half_rows = images.shape[2]
    own_rows = half_rows // members
    local_beams = images.shape[3]

    pieces = images[0].reshape(2, members, own_rows, local_beams).transpose(1, 0, 2, 3)
    gathered = lax.all_to_all(pieces, ("sub4", "beam"), 0, 0, tiled=True)
    rows_at = half_side * half_rows + member_at * own_rows + jnp.arange(own_rows, dtype=jnp.int32)
    ratios = NR / (NR + rows_at.astype(jnp.float32))
    shifts = lax.dynamic_slice_in_dim(offsets, group_at * GROUP_SUBS, GROUP_SUBS, 0)
    order = split_order(2 * B)
    blocks = B // LANES
    sector_width = 4 * B // (beam_count * sub_count)
    direct = group_count == 1 and sector_width == 4 * LANES
    if direct:
        shard_of = jnp.arange(blocks, dtype=jnp.int32) // sub_count
        sector_of = jnp.arange(blocks, dtype=jnp.int32) % sub_count
        holder = jnp.argmax(owners[shard_of] == sector_of[:, None], axis=1).astype(jnp.int32)
        sequence = flip_order(members, beam_count)
        position = jnp.asarray(np.argsort(sequence).astype(np.int32))
        slots = position[jnp.bitwise_xor(member_at, holder * beam_count + shard_of)]
    else:
        slots = jnp.arange(blocks, dtype=jnp.int32)
    merged = merge_call(
        slots,
        gathered,
        merge_tables(shifts, ratios, B),
        *kernel_tables(B),
    )
    if direct:
        ordered = merged.transpose(0, 2, 4, 1, 3).reshape(blocks, 2, sector_width, own_rows)
        received = swap_ordered(ordered, member_at, ("sub4", "beam"), sequence)
        received = received.transpose(1, 2, 0, 3)
        return received.reshape(1, 1, 2, sector_width, members * own_rows)
    merged = merged.transpose(1, 2, 3, 0, 4).reshape(4, 2, own_rows, B)

    tiles = merged.reshape(4, 2, own_rows, beam_count, sub_count, sector_width // 4)
    beam_ids = jnp.arange(beam_count, dtype=jnp.int32)[:, None]
    picked = tiles[:, :, :, beam_ids, owners, :]
    outgoing = picked.transpose(4, 3, 1, 5, 0, 2).reshape(
        sub_count * beam_count, 2, sector_width, own_rows
    )
    received = lax.all_to_all(outgoing, ("grp", "sub4", "beam"), 0, 0, tiled=True)
    received = received.reshape(group_count, members, 2, sector_width, own_rows)
    received = received.transpose(0, 2, 3, 1, 4)
    return received.reshape(1, group_count, 2, sector_width, members * own_rows)


def solution(mesh):
    shape = dict(mesh.shape)
    devices = mesh.devices.reshape(
        shape["swath"], shape["sub"] // GROUP_SUBS, GROUP_SUBS, shape["beam"], shape["half"]
    )
    split = Mesh(devices, ("swath", "grp", "sub4", "beam", "half"))
    placed = (P(("grp", "sub4"), None, ("swath", "half"), "beam"), P(), P())
    return jax.shard_map(
        body,
        mesh=split,
        in_specs=placed,
        out_specs=P(("grp", "sub4", "beam"), None, None, None, ("swath", "half")),
        check_vma=False,
    )
```

```python
import math

import jax
import numpy as np
import jax.numpy as jnp
from jax import lax
from jax.experimental import pallas as pl
from jax.experimental.pallas import tpu as pltpu
from jax.sharding import Mesh
from jax.sharding import PartitionSpec as P

B = 1024
NR = 1024
GROUP_SUBS = 4


def odd_values(beam_total):
    spacing = np.arange(beam_total, dtype=np.int64)[None, :] - np.arange(beam_total, dtype=np.int64)[:, None]
    parity = np.where(spacing % 2 == 0, 1.0, -1.0).astype(np.float32)
    angles = (2.0 * spacing.astype(np.float32) + np.float32(1.0)) * np.float32(math.pi / (2.0 * beam_total))
    values = parity * np.cos(angles) / (np.float32(beam_total) * np.sin(angles))
    return values.astype(np.float32).astype(jnp.bfloat16)


def split_order(beam_total):
    return np.concatenate([np.arange(0, beam_total, 2), np.arange(1, beam_total, 2)])


def spin(parts, scale, lead, first_at, beams_out):
    count = parts.shape[-1]
    lanes = 128
    coarse = jnp.asarray(
        (2.0 * lead * lanes / beams_out) * np.arange(count // lanes) + ((2 * first_at + 1) / beams_out - 1.0),
        jnp.float32,
    )
    fine = jnp.asarray((2.0 * lead / beams_out) * np.arange(lanes), jnp.float32)
    rough = scale[..., None] * coarse
    small = scale[..., None] * fine
    c1 = jnp.cos(rough)[..., None]
    s1 = jnp.sin(rough)[..., None]
    c2 = jnp.cos(small)[..., None, :]
    s2 = jnp.sin(small)[..., None, :]
    cosine = c1 * c2 - s1 * s2
    sines = s1 * c2 + c1 * s2
    grid = parts.shape[:-3] + (parts.shape[-2], count // lanes, lanes)
    real_part = parts[..., 0, :, :].reshape(grid)
    imag_part = parts[..., 1, :, :].reshape(grid)
    turned = jnp.stack(
        [real_part * cosine - imag_part * sines, real_part * sines + imag_part * cosine], -4
    )
    return turned.reshape(parts.shape)


def odd_local(children, kernel):
    product = jnp.dot(
        children.reshape(-1, children.shape[-1]), kernel, preferred_element_type=jnp.float32
    )
    return product.reshape(children.shape[:-1] + (kernel.shape[1],))


LANES = 128


TILE = 256


def toeplitz_tiles(matrix):
    count = matrix.shape[0] // TILE
    tiles = []
    for gap in range(-(count - 1), count):
        i = max(0, -gap)
        j = i + gap
        tiles.append(matrix[i * TILE:(i + 1) * TILE, j * TILE:(j + 1) * TILE])
    tiles = np.stack(tiles)
    for i in range(count):
        for j in range(count):
            assert np.array_equal(matrix[i * TILE:(i + 1) * TILE, j * TILE:(j + 1) * TILE], tiles[j - i + count - 1])
    return tiles


def kernel_tables(width):
    one = toeplitz_tiles(odd_values(width))
    order = split_order(2 * width)
    two = odd_values(2 * width)[order][:, order]
    assert np.array_equal(two[:width, :width], two[width:, width:])
    quads = np.stack([toeplitz_tiles(two[:width, :width]), toeplitz_tiles(two[:width, width:]),
                      toeplitz_tiles(two[width:, :width])])
    return jnp.asarray(one), jnp.asarray(quads)


def merge_kernel(slot_ref, x_ref, t1c, t1s, f1c, f1s, t2c, t2s, f2c, f2s, k1_hbm, k2_hbm, o_ref,
                 k1_v, k2_v, first_v, odd1_v, odd2_v, sems):
    members, _, rows, local = x_ref.shape
    beam_count = members // 4
    blocks = local // LANES
    wide = beam_count * blocks
    half = wide * LANES
    load_one = pltpu.make_async_copy(k1_hbm, k1_v, sems.at[0])
    load_two = pltpu.make_async_copy(k2_hbm, k2_v, sems.at[1])
    load_one.start()
    load_two.start()

    def turn(xr, xi, c1, s1, c2, s2):
        cosine = c1 * c2 - s1 * s2
        sines = s1 * c2 + c1 * s2
        return xr * cosine - xi * sines, xr * sines + xi * cosine

    for pair in range(2):
        for u in range(wide):
            b, k = divmod(u, blocks)
            cols = pl.ds(k * LANES, LANES)
            re_sum = None
            for m in range(2):
                s = 2 * pair + m
                xr = x_ref[s * beam_count + b, 0, :, cols].astype(jnp.float32)
                xi = x_ref[s * beam_count + b, 1, :, cols].astype(jnp.float32)
                re, im = turn(xr, xi, t1c[s, 0, u], t1s[s, 0, u], f1c[s], f1s[s])
                re_sum = re if re_sum is None else re_sum + re
                im_sum = im if m == 0 else im_sum + im
            out_cols = pl.ds(u * LANES, LANES)
            first_v[pair, pl.ds(0, rows), out_cols] = re_sum.astype(first_v.dtype)
            first_v[pair, pl.ds(rows, rows), out_cols] = im_sum.astype(first_v.dtype)

    load_one.wait()
    count = half // TILE
    per_piece = local // TILE
    parts = []
    for i in range(count):
        b, k = divmod(i, per_piece)
        stacked = [x_ref[s * beam_count + b, :, :, pl.ds(k * TILE, TILE)] for s in range(4)]
        parts.append(jnp.concatenate(stacked, axis=0).reshape(8 * rows, TILE))
    for j in range(count):
        total = None
        for i in range(count):
            term = jnp.dot(parts[i], k1_v[j - i + count - 1], preferred_element_type=jnp.float32)
            total = term if total is None else total + term
        odd1_v[:, :, pl.ds(j * TILE, TILE)] = total.reshape(4, 2 * rows, TILE)

    for pair in range(2):
        for u in range(wide):
            cols = pl.ds(u * LANES, LANES)
            for m in range(2):
                s = 2 * pair + m
                xr = odd1_v[s, pl.ds(0, rows), cols]
                xi = odd1_v[s, pl.ds(rows, rows), cols]
                re, im = turn(xr, xi, t1c[s, 1, u], t1s[s, 1, u], f1c[s], f1s[s])
                re_sum = re if m == 0 else re_sum + re
                im_sum = im if m == 0 else im_sum + im
            out_cols = pl.ds(half + u * LANES, LANES)
            first_v[pair, pl.ds(0, rows), out_cols] = re_sum.astype(first_v.dtype)
            first_v[pair, pl.ds(rows, rows), out_cols] = im_sum.astype(first_v.dtype)

    load_two.wait()
    evens = [first_v[:, :, pl.ds(i * TILE, TILE)].reshape(4 * rows, TILE) for i in range(count)]
    odds = [first_v[:, :, pl.ds(half + i * TILE, TILE)].reshape(4 * rows, TILE) for i in range(count)]
    for j in range(count):
        even_out = None
        odd_out = None
        for i in range(count):
            gap = j - i + count - 1
            term_e = jnp.dot(evens[i], k2_v[0, gap], preferred_element_type=jnp.float32)
            term_e += jnp.dot(odds[i], k2_v[2, gap], preferred_element_type=jnp.float32)
            term_o = jnp.dot(evens[i], k2_v[1, gap], preferred_element_type=jnp.float32)
            term_o += jnp.dot(odds[i], k2_v[0, gap], preferred_element_type=jnp.float32)
            even_out = term_e if even_out is None else even_out + term_e
            odd_out = term_o if odd_out is None else odd_out + term_o
        odd2_v[:, :, pl.ds(j * TILE, TILE)] = even_out.reshape(2, 2 * rows, TILE)
        odd2_v[:, :, pl.ds(half + j * TILE, TILE)] = odd_out.reshape(2, 2 * rows, TILE)

    for t in range(4):
        for u in range(wide):
            at = (t // 2) * half + u * LANES if t % 2 == 0 else (t // 2) * half + u * LANES
            cols = pl.ds(at, LANES)
            for pair in range(2):
                if t % 2 == 0:
                    xr = first_v[pair, pl.ds(0, rows), cols].astype(jnp.float32)
                    xi = first_v[pair, pl.ds(rows, rows), cols].astype(jnp.float32)
                else:
                    xr = odd2_v[pair, pl.ds(0, rows), cols]
                    xi = odd2_v[pair, pl.ds(rows, rows), cols]
                re, im = turn(xr, xi, t2c[pair, t, u], t2s[pair, t, u], f2c[pair], f2s[pair])
                re_sum = re if pair == 0 else re_sum + re
                im_sum = im if pair == 0 else im_sum + im
            slot = slot_ref[u]
            o_ref[slot, t, 0] = re_sum.astype(o_ref.dtype)
            o_ref[slot, t, 1] = im_sum.astype(o_ref.dtype)


def merge_call(slots, x, tables, k1, k2, interpret=False):
    members, _, rows, local = x.shape
    width = local * members // 4
    vmem = pl.BlockSpec(memory_space=pltpu.VMEM)
    hbm = pl.BlockSpec(memory_space=pl.ANY)
    smem = pl.BlockSpec(memory_space=pltpu.SMEM)
    return pl.pallas_call(
        merge_kernel,
        out_shape=jax.ShapeDtypeStruct((width // LANES, 4, 2, rows, LANES), jnp.bfloat16),
        in_specs=[smem] + [vmem] * 9 + [hbm, hbm],
        out_specs=vmem,
        scratch_shapes=[
            pltpu.VMEM(k1.shape, jnp.bfloat16),
            pltpu.VMEM(k2.shape, jnp.bfloat16),
            pltpu.VMEM((2, 2 * rows, 2 * width), jnp.bfloat16),
            pltpu.VMEM((4, 2 * rows, width), jnp.float32),
            pltpu.VMEM((2, 2 * rows, 2 * width), jnp.float32),
            pltpu.SemaphoreType.DMA((2,)),
        ],
        compiler_params=pltpu.CompilerParams(vmem_limit_bytes=48 * 1024 * 1024),
        interpret=interpret,
    )(slots, x, *tables, k1, k2)


def merge_tables(shifts, ratios, width):
    units = np.arange(width // LANES)
    fine = jnp.asarray(np.arange(LANES) / 512.0, jnp.float32)
    scale_one = shifts[:, None] * ratios[None, :]
    coarse_one = jnp.asarray(
        [0.25 * units + ((2 * t + 1) / (2 * width) - 1.0) for t in range(2)], jnp.float32
    )
    rough_one = (scale_one[:, None, None, :] * coarse_one[None, :, :, None])[..., None]
    small_one = scale_one[:, :, None] * fine
    centers = (shifts[0::2] + shifts[1::2]) * 0.5
    scale_two = centers[:, None] * ratios[None, :]
    coarse_two = jnp.asarray(
        [0.25 * units + ((2 * t + 1) / (4 * width) - 1.0) for t in range(4)], jnp.float32
    )
    rough_two = (scale_two[:, None, None, :] * coarse_two[None, :, :, None])[..., None]
    small_two = scale_two[:, :, None] * fine
    return (jnp.cos(rough_one), jnp.sin(rough_one), jnp.cos(small_one), jnp.sin(small_one),
            jnp.cos(rough_two), jnp.sin(rough_two), jnp.cos(small_two), jnp.sin(small_two))


def flip_order(count, beam_count):
    rest = sorted(range(1, count), key=lambda f: (-(f // beam_count), f))
    return np.array([0] + rest, dtype=np.int32)


def swap_ordered(ordered, place, axes, order):
    count = ordered.shape[0]
    moved = [ordered[0]]
    for at in range(1, count):
        flip = int(order[at])
        pairs = [(i, i ^ flip) for i in range(count)]
        moved.append(lax.ppermute(ordered[at], axes, pairs))
    position = jnp.asarray(np.argsort(order).astype(np.int32))
    senders = position[jnp.bitwise_xor(place, jnp.arange(count, dtype=jnp.int32))]
    return jnp.take(jnp.stack(moved), senders, axis=0)


def body(images, offsets, owners):
    group_count = lax.axis_size("grp")
    sub_count = group_count * GROUP_SUBS
    beam_count = lax.axis_size("beam")
    group_at = lax.axis_index("grp")
    member_at = lax.axis_index("sub4") * beam_count + lax.axis_index("beam")
    half_side = lax.axis_index("half")
    members = GROUP_SUBS * beam_count
    half_rows = images.shape[2]
    own_rows = half_rows // members
    local_beams = images.shape[3]

    pieces = images[0].reshape(2, members, own_rows, local_beams).transpose(1, 0, 2, 3)
    gathered = lax.all_to_all(pieces, ("sub4", "beam"), 0, 0, tiled=True)
    rows_at = half_side * half_rows + member_at * own_rows + jnp.arange(own_rows, dtype=jnp.int32)
    ratios = NR / (NR + rows_at.astype(jnp.float32))
    shifts = lax.dynamic_slice_in_dim(offsets, group_at * GROUP_SUBS, GROUP_SUBS, 0)
    order = split_order(2 * B)
    blocks = B // LANES
    sector_width = 4 * B // (beam_count * sub_count)
    direct = group_count == 1 and sector_width == 4 * LANES
    if direct:
        shard_of = jnp.arange(blocks, dtype=jnp.int32) // sub_count
        sector_of = jnp.arange(blocks, dtype=jnp.int32) % sub_count
        holder = jnp.argmax(owners[shard_of] == sector_of[:, None], axis=1).astype(jnp.int32)
        sequence = flip_order(members, beam_count)
        position = jnp.asarray(np.argsort(sequence).astype(np.int32))
        slots = position[jnp.bitwise_xor(member_at, holder * beam_count + shard_of)]
    else:
        slots = jnp.arange(blocks, dtype=jnp.int32)
    merged = merge_call(
        slots,
        gathered,
        merge_tables(shifts, ratios, B),
        *kernel_tables(B),
    )
    if direct:
        ordered = merged.transpose(0, 2, 4, 1, 3).reshape(blocks, 2, sector_width, own_rows)
        received = swap_ordered(ordered, member_at, ("sub4", "beam"), sequence)
        received = received.transpose(1, 2, 0, 3)
        return received.reshape(1, 1, 2, sector_width, members * own_rows)
    merged = merged.transpose(1, 2, 3, 0, 4).reshape(4, 2, own_rows, B)

    tiles = merged.reshape(4, 2, own_rows, beam_count, sub_count, sector_width // 4)
    beam_ids = jnp.arange(beam_count, dtype=jnp.int32)[:, None]
    picked = tiles[:, :, :, beam_ids, owners, :]
    outgoing = picked.transpose(4, 3, 1, 5, 0, 2).reshape(
        sub_count * beam_count, 2, sector_width, own_rows
    )
    received = lax.all_to_all(outgoing, ("grp", "sub4", "beam"), 0, 0, tiled=True)
    received = received.reshape(group_count, members, 2, sector_width, own_rows)
    received = received.transpose(0, 2, 3, 1, 4)
    return received.reshape(1, group_count, 2, sector_width, members * own_rows)


def solution(mesh):
    shape = dict(mesh.shape)
    devices = mesh.devices.reshape(
        shape["swath"], shape["sub"] // GROUP_SUBS, GROUP_SUBS, shape["beam"], shape["half"]
    )
    split = Mesh(devices, ("swath", "grp", "sub4", "beam", "half"))
    placed = (P(("grp", "sub4"), None, ("swath", "half"), "beam"), P(), P())
    return jax.shard_map(
        body,
        mesh=split,
        in_specs=placed,
        out_specs=P(("grp", "sub4", "beam"), None, None, None, ("swath", "half")),
        check_vma=False,
    )
```

```python
import math

import jax
import numpy as np
import jax.numpy as jnp
from jax import lax
from jax.experimental import pallas as pl
from jax.experimental.pallas import tpu as pltpu
from jax.sharding import Mesh
from jax.sharding import PartitionSpec as P

B = 1024
NR = 1024
GROUP_SUBS = 4


def odd_values(beam_total):
    spacing = np.arange(beam_total, dtype=np.int64)[None, :] - np.arange(beam_total, dtype=np.int64)[:, None]
    parity = np.where(spacing % 2 == 0, 1.0, -1.0).astype(np.float32)
    angles = (2.0 * spacing.astype(np.float32) + np.float32(1.0)) * np.float32(math.pi / (2.0 * beam_total))
    values = parity * np.cos(angles) / (np.float32(beam_total) * np.sin(angles))
    return values.astype(np.float32).astype(jnp.bfloat16)


def split_order(beam_total):
    return np.concatenate([np.arange(0, beam_total, 2), np.arange(1, beam_total, 2)])


def spin(parts, scale, lead, first_at, beams_out):
    count = parts.shape[-1]
    lanes = 128
    coarse = jnp.asarray(
        (2.0 * lead * lanes / beams_out) * np.arange(count // lanes) + ((2 * first_at + 1) / beams_out - 1.0),
        jnp.float32,
    )
    fine = jnp.asarray((2.0 * lead / beams_out) * np.arange(lanes), jnp.float32)
    rough = scale[..., None] * coarse
    small = scale[..., None] * fine
    c1 = jnp.cos(rough)[..., None]
    s1 = jnp.sin(rough)[..., None]
    c2 = jnp.cos(small)[..., None, :]
    s2 = jnp.sin(small)[..., None, :]
    cosine = c1 * c2 - s1 * s2
    sines = s1 * c2 + c1 * s2
    grid = parts.shape[:-3] + (parts.shape[-2], count // lanes, lanes)
    real_part = parts[..., 0, :, :].reshape(grid)
    imag_part = parts[..., 1, :, :].reshape(grid)
    turned = jnp.stack(
        [real_part * cosine - imag_part * sines, real_part * sines + imag_part * cosine], -4
    )
    return turned.reshape(parts.shape)


def odd_local(children, kernel):
    product = jnp.dot(
        children.reshape(-1, children.shape[-1]), kernel, preferred_element_type=jnp.float32
    )
    return product.reshape(children.shape[:-1] + (kernel.shape[1],))


LANES = 128


TILE = 256


def toeplitz_tiles(matrix):
    count = matrix.shape[0] // TILE
    tiles = []
    for gap in range(-(count - 1), count):
        i = max(0, -gap)
        j = i + gap
        tiles.append(matrix[i * TILE:(i + 1) * TILE, j * TILE:(j + 1) * TILE])
    tiles = np.stack(tiles)
    for i in range(count):
        for j in range(count):
            assert np.array_equal(matrix[i * TILE:(i + 1) * TILE, j * TILE:(j + 1) * TILE], tiles[j - i + count - 1])
    return tiles


def kernel_tables(width):
    one = toeplitz_tiles(odd_values(width))
    order = split_order(2 * width)
    two = odd_values(2 * width)[order][:, order]
    assert np.array_equal(two[:width, :width], two[width:, width:])
    quads = np.stack([toeplitz_tiles(two[:width, :width]), toeplitz_tiles(two[:width, width:]),
                      toeplitz_tiles(two[width:, :width])])
    return jnp.asarray(np.concatenate([one[None], quads]))


def merge_kernel(slot_ref, x_ref, t1c, t1s, f1c, f1s, t2c, t2s, f2c, f2s, k_hbm, o_ref,
                 k1_v, k2_v, first_v, odd1_v, odd2_v, sems):
    members, _, rows, local = x_ref.shape
    beam_count = members // 4
    blocks = local // LANES
    wide = beam_count * blocks
    half = wide * LANES
    load_one = pltpu.make_async_copy(k_hbm.at[0], k1_v, sems.at[0])
    load_two = pltpu.make_async_copy(k_hbm.at[pl.ds(1, 3)], k2_v, sems.at[1])
    load_one.start()
    load_two.start()

    def turn(xr, xi, c1, s1, c2, s2):
        cosine = c1 * c2 - s1 * s2
        sines = s1 * c2 + c1 * s2
        return xr * cosine - xi * sines, xr * sines + xi * cosine

    for pair in range(2):
        for u in range(wide):
            b, k = divmod(u, blocks)
            cols = pl.ds(k * LANES, LANES)
            re_sum = None
            for m in range(2):
                s = 2 * pair + m
                xr = x_ref[s * beam_count + b, 0, :, cols].astype(jnp.float32)
                xi = x_ref[s * beam_count + b, 1, :, cols].astype(jnp.float32)
                re, im = turn(xr, xi, t1c[s, 0, u], t1s[s, 0, u], f1c[s], f1s[s])
                re_sum = re if re_sum is None else re_sum + re
                im_sum = im if m == 0 else im_sum + im
            out_cols = pl.ds(u * LANES, LANES)
            first_v[pair, pl.ds(0, rows), out_cols] = re_sum.astype(first_v.dtype)
            first_v[pair, pl.ds(rows, rows), out_cols] = im_sum.astype(first_v.dtype)

    load_one.wait()
    count = half // TILE
    per_piece = local // TILE
    parts = []
    for i in range(count):
        b, k = divmod(i, per_piece)
        stacked = [x_ref[s * beam_count + b, :, :, pl.ds(k * TILE, TILE)] for s in range(4)]
        parts.append(jnp.concatenate(stacked, axis=0).reshape(8 * rows, TILE))
    for j in range(count):
        total = None
        for i in range(count):
            term = jnp.dot(parts[i], k1_v[j - i + count - 1], preferred_element_type=jnp.float32)
            total = term if total is None else total + term
        odd1_v[:, :, pl.ds(j * TILE, TILE)] = total.reshape(4, 2 * rows, TILE)

    for pair in range(2):
        for u in range(wide):
            cols = pl.ds(u * LANES, LANES)
            for m in range(2):
                s = 2 * pair + m
                xr = odd1_v[s, pl.ds(0, rows), cols]
                xi = odd1_v[s, pl.ds(rows, rows), cols]
                re, im = turn(xr, xi, t1c[s, 1, u], t1s[s, 1, u], f1c[s], f1s[s])
                re_sum = re if m == 0 else re_sum + re
                im_sum = im if m == 0 else im_sum + im
            out_cols = pl.ds(half + u * LANES, LANES)
            first_v[pair, pl.ds(0, rows), out_cols] = re_sum.astype(first_v.dtype)
            first_v[pair, pl.ds(rows, rows), out_cols] = im_sum.astype(first_v.dtype)

    load_two.wait()
    evens = [first_v[:, :, pl.ds(i * TILE, TILE)].reshape(4 * rows, TILE) for i in range(count)]
    odds = [first_v[:, :, pl.ds(half + i * TILE, TILE)].reshape(4 * rows, TILE) for i in range(count)]
    for j in range(count):
        even_out = None
        odd_out = None
        for i in range(count):
            gap = j - i + count - 1
            term_e = jnp.dot(evens[i], k2_v[0, gap], preferred_element_type=jnp.float32)
            term_e += jnp.dot(odds[i], k2_v[2, gap], preferred_element_type=jnp.float32)
            term_o = jnp.dot(evens[i], k2_v[1, gap], preferred_element_type=jnp.float32)
            term_o += jnp.dot(odds[i], k2_v[0, gap], preferred_element_type=jnp.float32)
            even_out = term_e if even_out is None else even_out + term_e
            odd_out = term_o if odd_out is None else odd_out + term_o
        odd2_v[:, :, pl.ds(j * TILE, TILE)] = even_out.reshape(2, 2 * rows, TILE)
        odd2_v[:, :, pl.ds(half + j * TILE, TILE)] = odd_out.reshape(2, 2 * rows, TILE)

    for t in range(4):
        for u in range(wide):
            at = (t // 2) * half + u * LANES if t % 2 == 0 else (t // 2) * half + u * LANES
            cols = pl.ds(at, LANES)
            for pair in range(2):
                if t % 2 == 0:
                    xr = first_v[pair, pl.ds(0, rows), cols].astype(jnp.float32)
                    xi = first_v[pair, pl.ds(rows, rows), cols].astype(jnp.float32)
                else:
                    xr = odd2_v[pair, pl.ds(0, rows), cols]
                    xi = odd2_v[pair, pl.ds(rows, rows), cols]
                re, im = turn(xr, xi, t2c[pair, t, u], t2s[pair, t, u], f2c[pair], f2s[pair])
                re_sum = re if pair == 0 else re_sum + re
                im_sum = im if pair == 0 else im_sum + im
            slot = slot_ref[u]
            o_ref[slot, t, 0] = re_sum.astype(o_ref.dtype)
            o_ref[slot, t, 1] = im_sum.astype(o_ref.dtype)


def merge_call(slots, x, tables, kernels, interpret=False):
    members, _, rows, local = x.shape
    width = local * members // 4
    vmem = pl.BlockSpec(memory_space=pltpu.VMEM)
    hbm = pl.BlockSpec(memory_space=pl.ANY)
    smem = pl.BlockSpec(memory_space=pltpu.SMEM)
    return pl.pallas_call(
        merge_kernel,
        out_shape=jax.ShapeDtypeStruct((width // LANES, 4, 2, rows, LANES), jnp.bfloat16),
        in_specs=[smem] + [vmem] * 9 + [hbm],
        out_specs=vmem,
        scratch_shapes=[
            pltpu.VMEM(kernels.shape[1:], jnp.bfloat16),
            pltpu.VMEM((3,) + kernels.shape[1:], jnp.bfloat16),
            pltpu.VMEM((2, 2 * rows, 2 * width), jnp.bfloat16),
            pltpu.VMEM((4, 2 * rows, width), jnp.float32),
            pltpu.VMEM((2, 2 * rows, 2 * width), jnp.float32),
            pltpu.SemaphoreType.DMA((2,)),
        ],
        compiler_params=pltpu.CompilerParams(vmem_limit_bytes=48 * 1024 * 1024),
        interpret=interpret,
    )(slots, x, *tables, kernels)


def merge_tables(shifts, ratios, width):
    units = np.arange(width // LANES)
    fine = jnp.asarray(np.arange(LANES) / 512.0, jnp.float32)
    scale_one = shifts[:, None] * ratios[None, :]
    coarse_one = jnp.asarray(
        [0.25 * units + ((2 * t + 1) / (2 * width) - 1.0) for t in range(2)], jnp.float32
    )
    rough_one = (scale_one[:, None, None, :] * coarse_one[None, :, :, None])[..., None]
    small_one = scale_one[:, :, None] * fine
    centers = (shifts[0::2] + shifts[1::2]) * 0.5
    scale_two = centers[:, None] * ratios[None, :]
    coarse_two = jnp.asarray(
        [0.25 * units + ((2 * t + 1) / (4 * width) - 1.0) for t in range(4)], jnp.float32
    )
    rough_two = (scale_two[:, None, None, :] * coarse_two[None, :, :, None])[..., None]
    small_two = scale_two[:, :, None] * fine
    return (jnp.cos(rough_one), jnp.sin(rough_one), jnp.cos(small_one), jnp.sin(small_one),
            jnp.cos(rough_two), jnp.sin(rough_two), jnp.cos(small_two), jnp.sin(small_two))


def flip_order(count, beam_count):
    rest = sorted(range(1, count), key=lambda f: (-(f // beam_count), f))
    return np.array([0] + rest, dtype=np.int32)


def swap_ordered(ordered, place, axes, order):
    count = ordered.shape[0]
    moved = [ordered[0]]
    for at in range(1, count):
        flip = int(order[at])
        pairs = [(i, i ^ flip) for i in range(count)]
        moved.append(lax.ppermute(ordered[at], axes, pairs))
    position = jnp.asarray(np.argsort(order).astype(np.int32))
    senders = position[jnp.bitwise_xor(place, jnp.arange(count, dtype=jnp.int32))]
    return jnp.take(jnp.stack(moved), senders, axis=0)


def body(images, offsets, owners):
    group_count = lax.axis_size("grp")
    sub_count = group_count * GROUP_SUBS
    beam_count = lax.axis_size("beam")
    group_at = lax.axis_index("grp")
    member_at = lax.axis_index("sub4") * beam_count + lax.axis_index("beam")
    half_side = lax.axis_index("half")
    members = GROUP_SUBS * beam_count
    half_rows = images.shape[2]
    own_rows = half_rows // members
    local_beams = images.shape[3]

    pieces = images[0].reshape(2, members, own_rows, local_beams).transpose(1, 0, 2, 3)
    gathered = lax.all_to_all(pieces, ("sub4", "beam"), 0, 0, tiled=True)
    rows_at = half_side * half_rows + member_at * own_rows + jnp.arange(own_rows, dtype=jnp.int32)
    ratios = NR / (NR + rows_at.astype(jnp.float32))
    shifts = lax.dynamic_slice_in_dim(offsets, group_at * GROUP_SUBS, GROUP_SUBS, 0)
    order = split_order(2 * B)
    blocks = B // LANES
    sector_width = 4 * B // (beam_count * sub_count)
    direct = group_count == 1 and sector_width == 4 * LANES
    if direct:
        shard_of = jnp.arange(blocks, dtype=jnp.int32) // sub_count
        sector_of = jnp.arange(blocks, dtype=jnp.int32) % sub_count
        holder = jnp.argmax(owners[shard_of] == sector_of[:, None], axis=1).astype(jnp.int32)
        sequence = flip_order(members, beam_count)
        position = jnp.asarray(np.argsort(sequence).astype(np.int32))
        slots = position[jnp.bitwise_xor(member_at, holder * beam_count + shard_of)]
    else:
        slots = jnp.arange(blocks, dtype=jnp.int32)
    merged = merge_call(
        slots,
        gathered,
        merge_tables(shifts, ratios, B),
        kernel_tables(B),
    )
    if direct:
        ordered = merged.transpose(0, 2, 4, 1, 3).reshape(blocks, 2, sector_width, own_rows)
        received = swap_ordered(ordered, member_at, ("sub4", "beam"), sequence)
        received = received.transpose(1, 2, 0, 3)
        return received.reshape(1, 1, 2, sector_width, members * own_rows)
    merged = merged.transpose(1, 2, 3, 0, 4).reshape(4, 2, own_rows, B)

    tiles = merged.reshape(4, 2, own_rows, beam_count, sub_count, sector_width // 4)
    beam_ids = jnp.arange(beam_count, dtype=jnp.int32)[:, None]
    picked = tiles[:, :, :, beam_ids, owners, :]
    outgoing = picked.transpose(4, 3, 1, 5, 0, 2).reshape(
        sub_count * beam_count, 2, sector_width, own_rows
    )
    received = lax.all_to_all(outgoing, ("grp", "sub4", "beam"), 0, 0, tiled=True)
    received = received.reshape(group_count, members, 2, sector_width, own_rows)
    received = received.transpose(0, 2, 3, 1, 4)
    return received.reshape(1, group_count, 2, sector_width, members * own_rows)


def solution(mesh):
    shape = dict(mesh.shape)
    devices = mesh.devices.reshape(
        shape["swath"], shape["sub"] // GROUP_SUBS, GROUP_SUBS, shape["beam"], shape["half"]
    )
    split = Mesh(devices, ("swath", "grp", "sub4", "beam", "half"))
    placed = (P(("grp", "sub4"), None, ("swath", "half"), "beam"), P(), P())
    return jax.shard_map(
        body,
        mesh=split,
        in_specs=placed,
        out_specs=P(("grp", "sub4", "beam"), None, None, None, ("swath", "half")),
        check_vma=False,
    )
```

```python
import math

import jax
import numpy as np
import jax.numpy as jnp
from jax import lax
from jax.experimental import pallas as pl
from jax.experimental.pallas import tpu as pltpu
from jax.sharding import Mesh
from jax.sharding import PartitionSpec as P

B = 1024
NR = 1024
GROUP_SUBS = 4


def odd_values(beam_total):
    spacing = np.arange(beam_total, dtype=np.int64)[None, :] - np.arange(beam_total, dtype=np.int64)[:, None]
    parity = np.where(spacing % 2 == 0, 1.0, -1.0).astype(np.float32)
    angles = (2.0 * spacing.astype(np.float32) + np.float32(1.0)) * np.float32(math.pi / (2.0 * beam_total))
    values = parity * np.cos(angles) / (np.float32(beam_total) * np.sin(angles))
    return values.astype(np.float32).astype(jnp.bfloat16)


def split_order(beam_total):
    return np.concatenate([np.arange(0, beam_total, 2), np.arange(1, beam_total, 2)])


def spin(parts, scale, lead, first_at, beams_out):
    count = parts.shape[-1]
    lanes = 128
    coarse = jnp.asarray(
        (2.0 * lead * lanes / beams_out) * np.arange(count // lanes) + ((2 * first_at + 1) / beams_out - 1.0),
        jnp.float32,
    )
    fine = jnp.asarray((2.0 * lead / beams_out) * np.arange(lanes), jnp.float32)
    rough = scale[..., None] * coarse
    small = scale[..., None] * fine
    c1 = jnp.cos(rough)[..., None]
    s1 = jnp.sin(rough)[..., None]
    c2 = jnp.cos(small)[..., None, :]
    s2 = jnp.sin(small)[..., None, :]
    cosine = c1 * c2 - s1 * s2
    sines = s1 * c2 + c1 * s2
    grid = parts.shape[:-3] + (parts.shape[-2], count // lanes, lanes)
    real_part = parts[..., 0, :, :].reshape(grid)
    imag_part = parts[..., 1, :, :].reshape(grid)
    turned = jnp.stack(
        [real_part * cosine - imag_part * sines, real_part * sines + imag_part * cosine], -4
    )
    return turned.reshape(parts.shape)


def odd_local(children, kernel):
    product = jnp.dot(
        children.reshape(-1, children.shape[-1]), kernel, preferred_element_type=jnp.float32
    )
    return product.reshape(children.shape[:-1] + (kernel.shape[1],))


LANES = 128


TILE = 256


def toeplitz_tiles(matrix):
    count = matrix.shape[0] // TILE
    tiles = []
    for gap in range(-(count - 1), count):
        i = max(0, -gap)
        j = i + gap
        tiles.append(matrix[i * TILE:(i + 1) * TILE, j * TILE:(j + 1) * TILE])
    tiles = np.stack(tiles)
    for i in range(count):
        for j in range(count):
            assert np.array_equal(matrix[i * TILE:(i + 1) * TILE, j * TILE:(j + 1) * TILE], tiles[j - i + count - 1])
    return tiles


def kernel_tables(width):
    one = toeplitz_tiles(odd_values(width))
    order = split_order(2 * width)
    two = odd_values(2 * width)[order][:, order]
    assert np.array_equal(two[:width, :width], two[width:, width:])
    quads = np.stack([toeplitz_tiles(two[:width, :width]), toeplitz_tiles(two[:width, width:]),
                      toeplitz_tiles(two[width:, :width])])
    return jnp.asarray(np.concatenate([one[None], quads]))


def merge_kernel(slot_ref, x_ref, t1c, t1s, f1c, f1s, t2c, t2s, f2c, f2s, k_hbm, o_ref,
                 k1_v, k2_v, first_v, odd1_v, odd2_v, sems):
    members, _, rows, local = x_ref.shape
    beam_count = members // 4
    blocks = local // LANES
    wide = beam_count * blocks
    half = wide * LANES
    load_one = pltpu.make_async_copy(k_hbm.at[0], k1_v, sems.at[0])
    load_two = pltpu.make_async_copy(k_hbm.at[pl.ds(1, 3)], k2_v, sems.at[1])
    load_one.start()
    load_two.start()

    def column(ref, a, b, u):
        return ref[a, b][:, u:u + 1]

    def turn(xr, xi, c1, s1, c2, s2):
        cosine = c1 * c2 - s1 * s2
        sines = s1 * c2 + c1 * s2
        return xr * cosine - xi * sines, xr * sines + xi * cosine

    for pair in range(2):
        for u in range(wide):
            b, k = divmod(u, blocks)
            cols = pl.ds(k * LANES, LANES)
            re_sum = None
            for m in range(2):
                s = 2 * pair + m
                xr = x_ref[s * beam_count + b, 0, :, cols].astype(jnp.float32)
                xi = x_ref[s * beam_count + b, 1, :, cols].astype(jnp.float32)
                re, im = turn(xr, xi, column(t1c, s, 0, u), column(t1s, s, 0, u), f1c[s], f1s[s])
                re_sum = re if re_sum is None else re_sum + re
                im_sum = im if m == 0 else im_sum + im
            out_cols = pl.ds(u * LANES, LANES)
            first_v[pair, pl.ds(0, rows), out_cols] = re_sum.astype(first_v.dtype)
            first_v[pair, pl.ds(rows, rows), out_cols] = im_sum.astype(first_v.dtype)

    load_one.wait()
    count = half // TILE
    per_piece = local // TILE
    parts = []
    for i in range(count):
        b, k = divmod(i, per_piece)
        stacked = [x_ref[s * beam_count + b, :, :, pl.ds(k * TILE, TILE)] for s in range(4)]
        parts.append(jnp.concatenate(stacked, axis=0).reshape(8 * rows, TILE))
    for j in range(count):
        total = None
        for i in range(count):
            term = jnp.dot(parts[i], k1_v[j - i + count - 1], preferred_element_type=jnp.float32)
            total = term if total is None else total + term
        odd1_v[:, :, pl.ds(j * TILE, TILE)] = total.reshape(4, 2 * rows, TILE)

    for pair in range(2):
        for u in range(wide):
            cols = pl.ds(u * LANES, LANES)
            for m in range(2):
                s = 2 * pair + m
                xr = odd1_v[s, pl.ds(0, rows), cols]
                xi = odd1_v[s, pl.ds(rows, rows), cols]
                re, im = turn(xr, xi, column(t1c, s, 1, u), column(t1s, s, 1, u), f1c[s], f1s[s])
                re_sum = re if m == 0 else re_sum + re
                im_sum = im if m == 0 else im_sum + im
            out_cols = pl.ds(half + u * LANES, LANES)
            first_v[pair, pl.ds(0, rows), out_cols] = re_sum.astype(first_v.dtype)
            first_v[pair, pl.ds(rows, rows), out_cols] = im_sum.astype(first_v.dtype)

    load_two.wait()
    evens = [first_v[:, :, pl.ds(i * TILE, TILE)].reshape(4 * rows, TILE) for i in range(count)]
    odds = [first_v[:, :, pl.ds(half + i * TILE, TILE)].reshape(4 * rows, TILE) for i in range(count)]
    for j in range(count):
        even_out = None
        odd_out = None
        for i in range(count):
            gap = j - i + count - 1
            term_e = jnp.dot(evens[i], k2_v[0, gap], preferred_element_type=jnp.float32)
            term_e += jnp.dot(odds[i], k2_v[2, gap], preferred_element_type=jnp.float32)
            term_o = jnp.dot(evens[i], k2_v[1, gap], preferred_element_type=jnp.float32)
            term_o += jnp.dot(odds[i], k2_v[0, gap], preferred_element_type=jnp.float32)
            even_out = term_e if even_out is None else even_out + term_e
            odd_out = term_o if odd_out is None else odd_out + term_o
        odd2_v[:, :, pl.ds(j * TILE, TILE)] = even_out.reshape(2, 2 * rows, TILE)
        odd2_v[:, :, pl.ds(half + j * TILE, TILE)] = odd_out.reshape(2, 2 * rows, TILE)

    for t in range(4):
        for u in range(wide):
            at = (t // 2) * half + u * LANES if t % 2 == 0 else (t // 2) * half + u * LANES
            cols = pl.ds(at, LANES)
            for pair in range(2):
                if t % 2 == 0:
                    xr = first_v[pair, pl.ds(0, rows), cols].astype(jnp.float32)
                    xi = first_v[pair, pl.ds(rows, rows), cols].astype(jnp.float32)
                else:
                    xr = odd2_v[pair, pl.ds(0, rows), cols]
                    xi = odd2_v[pair, pl.ds(rows, rows), cols]
                re, im = turn(xr, xi, column(t2c, pair, t, u), column(t2s, pair, t, u), f2c[pair], f2s[pair])
                re_sum = re if pair == 0 else re_sum + re
                im_sum = im if pair == 0 else im_sum + im
            slot = slot_ref[u]
            o_ref[slot, t, 0] = re_sum.astype(o_ref.dtype)
            o_ref[slot, t, 1] = im_sum.astype(o_ref.dtype)


def merge_call(slots, x, tables, kernels, interpret=False):
    members, _, rows, local = x.shape
    width = local * members // 4
    vmem = pl.BlockSpec(memory_space=pltpu.VMEM)
    hbm = pl.BlockSpec(memory_space=pl.ANY)
    smem = pl.BlockSpec(memory_space=pltpu.SMEM)
    return pl.pallas_call(
        merge_kernel,
        out_shape=jax.ShapeDtypeStruct((width // LANES, 4, 2, rows, LANES), jnp.bfloat16),
        in_specs=[smem] + [vmem] * 9 + [hbm],
        out_specs=vmem,
        scratch_shapes=[
            pltpu.VMEM(kernels.shape[1:], jnp.bfloat16),
            pltpu.VMEM((3,) + kernels.shape[1:], jnp.bfloat16),
            pltpu.VMEM((2, 2 * rows, 2 * width), jnp.bfloat16),
            pltpu.VMEM((4, 2 * rows, width), jnp.float32),
            pltpu.VMEM((2, 2 * rows, 2 * width), jnp.float32),
            pltpu.SemaphoreType.DMA((2,)),
        ],
        compiler_params=pltpu.CompilerParams(vmem_limit_bytes=48 * 1024 * 1024),
        interpret=interpret,
    )(slots, x, *tables, kernels)


def merge_tables(shifts, ratios, width):
    units = np.arange(width // LANES)
    fine = jnp.asarray(np.arange(LANES) / 512.0, jnp.float32)
    scale_one = shifts[:, None] * ratios[None, :]
    coarse_one = jnp.asarray(
        [0.25 * units + ((2 * t + 1) / (2 * width) - 1.0) for t in range(2)], jnp.float32
    )
    rough_one = scale_one[:, None, None, :] * coarse_one[None, :, :, None]
    small_one = scale_one[:, :, None] * fine
    centers = (shifts[0::2] + shifts[1::2]) * 0.5
    scale_two = centers[:, None] * ratios[None, :]
    coarse_two = jnp.asarray(
        [0.25 * units + ((2 * t + 1) / (4 * width) - 1.0) for t in range(4)], jnp.float32
    )
    rough_two = scale_two[:, None, None, :] * coarse_two[None, :, :, None]
    small_two = scale_two[:, :, None] * fine
    rough_one = jnp.swapaxes(rough_one, -1, -2)
    rough_two = jnp.swapaxes(rough_two, -1, -2)
    return (jnp.cos(rough_one), jnp.sin(rough_one), jnp.cos(small_one), jnp.sin(small_one),
            jnp.cos(rough_two), jnp.sin(rough_two), jnp.cos(small_two), jnp.sin(small_two))


def flip_order(count, beam_count):
    rest = sorted(range(1, count), key=lambda f: (-(f // beam_count), f))
    return np.array([0] + rest, dtype=np.int32)


def swap_ordered(ordered, place, axes, order):
    count = ordered.shape[0]
    moved = [ordered[0]]
    for at in range(1, count):
        flip = int(order[at])
        pairs = [(i, i ^ flip) for i in range(count)]
        moved.append(lax.ppermute(ordered[at], axes, pairs))
    position = jnp.asarray(np.argsort(order).astype(np.int32))
    senders = position[jnp.bitwise_xor(place, jnp.arange(count, dtype=jnp.int32))]
    return jnp.take(jnp.stack(moved), senders, axis=0)


def body(images, offsets, owners):
    group_count = lax.axis_size("grp")
    sub_count = group_count * GROUP_SUBS
    beam_count = lax.axis_size("beam")
    group_at = lax.axis_index("grp")
    member_at = lax.axis_index("sub4") * beam_count + lax.axis_index("beam")
    half_side = lax.axis_index("half")
    members = GROUP_SUBS * beam_count
    half_rows = images.shape[2]
    own_rows = half_rows // members
    local_beams = images.shape[3]

    pieces = images[0].reshape(2, members, own_rows, local_beams).transpose(1, 0, 2, 3)
    gathered = lax.all_to_all(pieces, ("sub4", "beam"), 0, 0, tiled=True)
    rows_at = half_side * half_rows + member_at * own_rows + jnp.arange(own_rows, dtype=jnp.int32)
    ratios = NR / (NR + rows_at.astype(jnp.float32))
    shifts = lax.dynamic_slice_in_dim(offsets, group_at * GROUP_SUBS, GROUP_SUBS, 0)
    order = split_order(2 * B)
    blocks = B // LANES
    sector_width = 4 * B // (beam_count * sub_count)
    direct = group_count == 1 and sector_width == 4 * LANES
    if direct:
        shard_of = jnp.arange(blocks, dtype=jnp.int32) // sub_count
        sector_of = jnp.arange(blocks, dtype=jnp.int32) % sub_count
        holder = jnp.argmax(owners[shard_of] == sector_of[:, None], axis=1).astype(jnp.int32)
        sequence = flip_order(members, beam_count)
        position = jnp.asarray(np.argsort(sequence).astype(np.int32))
        slots = position[jnp.bitwise_xor(member_at, holder * beam_count + shard_of)]
    else:
        slots = jnp.arange(blocks, dtype=jnp.int32)
    merged = merge_call(
        slots,
        gathered,
        merge_tables(shifts, ratios, B),
        kernel_tables(B),
    )
    if direct:
        ordered = merged.transpose(0, 2, 4, 1, 3).reshape(blocks, 2, sector_width, own_rows)
        received = swap_ordered(ordered, member_at, ("sub4", "beam"), sequence)
        received = received.transpose(1, 2, 0, 3)
        return received.reshape(1, 1, 2, sector_width, members * own_rows)
    merged = merged.transpose(1, 2, 3, 0, 4).reshape(4, 2, own_rows, B)

    tiles = merged.reshape(4, 2, own_rows, beam_count, sub_count, sector_width // 4)
    beam_ids = jnp.arange(beam_count, dtype=jnp.int32)[:, None]
    picked = tiles[:, :, :, beam_ids, owners, :]
    outgoing = picked.transpose(4, 3, 1, 5, 0, 2).reshape(
        sub_count * beam_count, 2, sector_width, own_rows
    )
    received = lax.all_to_all(outgoing, ("grp", "sub4", "beam"), 0, 0, tiled=True)
    received = received.reshape(group_count, members, 2, sector_width, own_rows)
    received = received.transpose(0, 2, 3, 1, 4)
    return received.reshape(1, group_count, 2, sector_width, members * own_rows)


def solution(mesh):
    shape = dict(mesh.shape)
    devices = mesh.devices.reshape(
        shape["swath"], shape["sub"] // GROUP_SUBS, GROUP_SUBS, shape["beam"], shape["half"]
    )
    split = Mesh(devices, ("swath", "grp", "sub4", "beam", "half"))
    placed = (P(("grp", "sub4"), None, ("swath", "half"), "beam"), P(), P())
    return jax.shard_map(
        body,
        mesh=split,
        in_specs=placed,
        out_specs=P(("grp", "sub4", "beam"), None, None, None, ("swath", "half")),
        check_vma=False,
    )
```

```python
import math

import jax
import numpy as np
import jax.numpy as jnp
from jax import lax
from jax.experimental import pallas as pl
from jax.experimental.pallas import tpu as pltpu
from jax.sharding import Mesh
from jax.sharding import PartitionSpec as P

B = 1024
NR = 1024
GROUP_SUBS = 4


def odd_values(beam_total):
    spacing = np.arange(beam_total, dtype=np.int64)[None, :] - np.arange(beam_total, dtype=np.int64)[:, None]
    parity = np.where(spacing % 2 == 0, 1.0, -1.0).astype(np.float32)
    angles = (2.0 * spacing.astype(np.float32) + np.float32(1.0)) * np.float32(math.pi / (2.0 * beam_total))
    values = parity * np.cos(angles) / (np.float32(beam_total) * np.sin(angles))
    return values.astype(np.float32).astype(jnp.bfloat16)


def split_order(beam_total):
    return np.concatenate([np.arange(0, beam_total, 2), np.arange(1, beam_total, 2)])


def spin(parts, scale, lead, first_at, beams_out):
    count = parts.shape[-1]
    lanes = 128
    coarse = jnp.asarray(
        (2.0 * lead * lanes / beams_out) * np.arange(count // lanes) + ((2 * first_at + 1) / beams_out - 1.0),
        jnp.float32,
    )
    fine = jnp.asarray((2.0 * lead / beams_out) * np.arange(lanes), jnp.float32)
    rough = scale[..., None] * coarse
    small = scale[..., None] * fine
    c1 = jnp.cos(rough)[..., None]
    s1 = jnp.sin(rough)[..., None]
    c2 = jnp.cos(small)[..., None, :]
    s2 = jnp.sin(small)[..., None, :]
    cosine = c1 * c2 - s1 * s2
    sines = s1 * c2 + c1 * s2
    grid = parts.shape[:-3] + (parts.shape[-2], count // lanes, lanes)
    real_part = parts[..., 0, :, :].reshape(grid)
    imag_part = parts[..., 1, :, :].reshape(grid)
    turned = jnp.stack(
        [real_part * cosine - imag_part * sines, real_part * sines + imag_part * cosine], -4
    )
    return turned.reshape(parts.shape)


def odd_local(children, kernel):
    product = jnp.dot(
        children.reshape(-1, children.shape[-1]), kernel, preferred_element_type=jnp.float32
    )
    return product.reshape(children.shape[:-1] + (kernel.shape[1],))


LANES = 128


TILE = 256


def toeplitz_tiles(matrix):
    count = matrix.shape[0] // TILE
    tiles = []
    for gap in range(-(count - 1), count):
        i = max(0, -gap)
        j = i + gap
        tiles.append(matrix[i * TILE:(i + 1) * TILE, j * TILE:(j + 1) * TILE])
    tiles = np.stack(tiles)
    for i in range(count):
        for j in range(count):
            assert np.array_equal(matrix[i * TILE:(i + 1) * TILE, j * TILE:(j + 1) * TILE], tiles[j - i + count - 1])
    return tiles


def kernel_tables(width):
    one = toeplitz_tiles(odd_values(width))
    order = split_order(2 * width)
    two = odd_values(2 * width)[order][:, order]
    assert np.array_equal(two[:width, :width], two[width:, width:])
    quads = np.stack([toeplitz_tiles(two[:width, :width]), toeplitz_tiles(two[:width, width:]),
                      toeplitz_tiles(two[width:, :width])])
    return jnp.asarray(np.concatenate([one[None], quads]))


def merge_kernel(slot_ref, x_ref, t1c, t1s, f1c, f1s, t2c, t2s, f2c, f2s, k_hbm, o_ref,
                 k1_v, k2_v, first_v, odd1_v, odd2_v, sems):
    members, _, rows, local = x_ref.shape
    beam_count = members // 4
    blocks = local // LANES
    wide = beam_count * blocks
    half = wide * LANES
    load_one = pltpu.make_async_copy(k_hbm.at[0], k1_v, sems.at[0])
    load_two = pltpu.make_async_copy(k_hbm.at[pl.ds(1, 3)], k2_v, sems.at[1])
    load_one.start()

    def column(ref, a, b, u):
        return ref[a, b][:, u:u + 1]

    def turn(xr, xi, c1, s1, c2, s2):
        cosine = c1 * c2 - s1 * s2
        sines = s1 * c2 + c1 * s2
        return xr * cosine - xi * sines, xr * sines + xi * cosine

    for pair in range(2):
        for u in range(wide):
            b, k = divmod(u, blocks)
            cols = pl.ds(k * LANES, LANES)
            re_sum = None
            for m in range(2):
                s = 2 * pair + m
                xr = x_ref[s * beam_count + b, 0, :, cols].astype(jnp.float32)
                xi = x_ref[s * beam_count + b, 1, :, cols].astype(jnp.float32)
                re, im = turn(xr, xi, column(t1c, s, 0, u), column(t1s, s, 0, u), f1c[s], f1s[s])
                re_sum = re if re_sum is None else re_sum + re
                im_sum = im if m == 0 else im_sum + im
            out_cols = pl.ds(u * LANES, LANES)
            first_v[pair, pl.ds(0, rows), out_cols] = re_sum.astype(first_v.dtype)
            first_v[pair, pl.ds(rows, rows), out_cols] = im_sum.astype(first_v.dtype)

    load_one.wait()
    load_two.start()
    count = half // TILE
    per_piece = local // TILE
    parts = []
    for i in range(count):
        b, k = divmod(i, per_piece)
        stacked = [x_ref[s * beam_count + b, :, :, pl.ds(k * TILE, TILE)] for s in range(4)]
        parts.append(jnp.concatenate(stacked, axis=0).reshape(8 * rows, TILE))
    for j in range(count):
        total = None
        for i in range(count):
            term = jnp.dot(parts[i], k1_v[j - i + count - 1], preferred_element_type=jnp.float32)
            total = term if total is None else total + term
        odd1_v[:, :, pl.ds(j * TILE, TILE)] = total.reshape(4, 2 * rows, TILE)

    for pair in range(2):
        for u in range(wide):
            cols = pl.ds(u * LANES, LANES)
            for m in range(2):
                s = 2 * pair + m
                xr = odd1_v[s, pl.ds(0, rows), cols]
                xi = odd1_v[s, pl.ds(rows, rows), cols]
                re, im = turn(xr, xi, column(t1c, s, 1, u), column(t1s, s, 1, u), f1c[s], f1s[s])
                re_sum = re if m == 0 else re_sum + re
                im_sum = im if m == 0 else im_sum + im
            out_cols = pl.ds(half + u * LANES, LANES)
            first_v[pair, pl.ds(0, rows), out_cols] = re_sum.astype(first_v.dtype)
            first_v[pair, pl.ds(rows, rows), out_cols] = im_sum.astype(first_v.dtype)

    load_two.wait()
    evens = [first_v[:, :, pl.ds(i * TILE, TILE)].reshape(4 * rows, TILE) for i in range(count)]
    odds = [first_v[:, :, pl.ds(half + i * TILE, TILE)].reshape(4 * rows, TILE) for i in range(count)]
    for j in range(count):
        even_out = None
        odd_out = None
        for i in range(count):
            gap = j - i + count - 1
            term_e = jnp.dot(evens[i], k2_v[0, gap], preferred_element_type=jnp.float32)
            term_e += jnp.dot(odds[i], k2_v[2, gap], preferred_element_type=jnp.float32)
            term_o = jnp.dot(evens[i], k2_v[1, gap], preferred_element_type=jnp.float32)
            term_o += jnp.dot(odds[i], k2_v[0, gap], preferred_element_type=jnp.float32)
            even_out = term_e if even_out is None else even_out + term_e
            odd_out = term_o if odd_out is None else odd_out + term_o
        odd2_v[:, :, pl.ds(j * TILE, TILE)] = even_out.reshape(2, 2 * rows, TILE)
        odd2_v[:, :, pl.ds(half + j * TILE, TILE)] = odd_out.reshape(2, 2 * rows, TILE)

    for t in range(4):
        for u in range(wide):
            at = (t // 2) * half + u * LANES if t % 2 == 0 else (t // 2) * half + u * LANES
            cols = pl.ds(at, LANES)
            for pair in range(2):
                if t % 2 == 0:
                    xr = first_v[pair, pl.ds(0, rows), cols].astype(jnp.float32)
                    xi = first_v[pair, pl.ds(rows, rows), cols].astype(jnp.float32)
                else:
                    xr = odd2_v[pair, pl.ds(0, rows), cols]
                    xi = odd2_v[pair, pl.ds(rows, rows), cols]
                re, im = turn(xr, xi, column(t2c, pair, t, u), column(t2s, pair, t, u), f2c[pair], f2s[pair])
                re_sum = re if pair == 0 else re_sum + re
                im_sum = im if pair == 0 else im_sum + im
            slot = slot_ref[u]
            o_ref[slot, t, 0] = re_sum.astype(o_ref.dtype)
            o_ref[slot, t, 1] = im_sum.astype(o_ref.dtype)


def merge_call(slots, x, tables, kernels, interpret=False):
    members, _, rows, local = x.shape
    width = local * members // 4
    vmem = pl.BlockSpec(memory_space=pltpu.VMEM)
    hbm = pl.BlockSpec(memory_space=pl.ANY)
    smem = pl.BlockSpec(memory_space=pltpu.SMEM)
    return pl.pallas_call(
        merge_kernel,
        out_shape=jax.ShapeDtypeStruct((width // LANES, 4, 2, rows, LANES), jnp.bfloat16),
        in_specs=[smem] + [vmem] * 9 + [hbm],
        out_specs=vmem,
        scratch_shapes=[
            pltpu.VMEM(kernels.shape[1:], jnp.bfloat16),
            pltpu.VMEM((3,) + kernels.shape[1:], jnp.bfloat16),
            pltpu.VMEM((2, 2 * rows, 2 * width), jnp.bfloat16),
            pltpu.VMEM((4, 2 * rows, width), jnp.float32),
            pltpu.VMEM((2, 2 * rows, 2 * width), jnp.float32),
            pltpu.SemaphoreType.DMA((2,)),
        ],
        compiler_params=pltpu.CompilerParams(vmem_limit_bytes=48 * 1024 * 1024),
        interpret=interpret,
    )(slots, x, *tables, kernels)


def merge_tables(shifts, ratios, width):
    units = np.arange(width // LANES)
    fine = jnp.asarray(np.arange(LANES) / 512.0, jnp.float32)
    scale_one = shifts[:, None] * ratios[None, :]
    coarse_one = jnp.asarray(
        [0.25 * units + ((2 * t + 1) / (2 * width) - 1.0) for t in range(2)], jnp.float32
    )
    rough_one = scale_one[:, None, None, :] * coarse_one[None, :, :, None]
    small_one = scale_one[:, :, None] * fine
    centers = (shifts[0::2] + shifts[1::2]) * 0.5
    scale_two = centers[:, None] * ratios[None, :]
    coarse_two = jnp.asarray(
        [0.25 * units + ((2 * t + 1) / (4 * width) - 1.0) for t in range(4)], jnp.float32
    )
    rough_two = scale_two[:, None, None, :] * coarse_two[None, :, :, None]
    small_two = scale_two[:, :, None] * fine
    rough_one = jnp.swapaxes(rough_one, -1, -2)
    rough_two = jnp.swapaxes(rough_two, -1, -2)
    return (jnp.cos(rough_one), jnp.sin(rough_one), jnp.cos(small_one), jnp.sin(small_one),
            jnp.cos(rough_two), jnp.sin(rough_two), jnp.cos(small_two), jnp.sin(small_two))


def flip_order(count, beam_count):
    rest = sorted(range(1, count), key=lambda f: (-(f // beam_count), f))
    return np.array([0] + rest, dtype=np.int32)


def swap_ordered(ordered, place, axes, order):
    count = ordered.shape[0]
    moved = [ordered[0]]
    for at in range(1, count):
        flip = int(order[at])
        pairs = [(i, i ^ flip) for i in range(count)]
        moved.append(lax.ppermute(ordered[at], axes, pairs))
    position = jnp.asarray(np.argsort(order).astype(np.int32))
    senders = position[jnp.bitwise_xor(place, jnp.arange(count, dtype=jnp.int32))]
    return jnp.take(jnp.stack(moved), senders, axis=0)


def body(images, offsets, owners):
    group_count = lax.axis_size("grp")
    sub_count = group_count * GROUP_SUBS
    beam_count = lax.axis_size("beam")
    group_at = lax.axis_index("grp")
    member_at = lax.axis_index("sub4") * beam_count + lax.axis_index("beam")
    half_side = lax.axis_index("half")
    members = GROUP_SUBS * beam_count
    half_rows = images.shape[2]
    own_rows = half_rows // members
    local_beams = images.shape[3]

    pieces = images[0].reshape(2, members, own_rows, local_beams).transpose(1, 0, 2, 3)
    gathered = lax.all_to_all(pieces, ("sub4", "beam"), 0, 0, tiled=True)
    rows_at = half_side * half_rows + member_at * own_rows + jnp.arange(own_rows, dtype=jnp.int32)
    ratios = NR / (NR + rows_at.astype(jnp.float32))
    shifts = lax.dynamic_slice_in_dim(offsets, group_at * GROUP_SUBS, GROUP_SUBS, 0)
    order = split_order(2 * B)
    blocks = B // LANES
    sector_width = 4 * B // (beam_count * sub_count)
    direct = group_count == 1 and sector_width == 4 * LANES
    if direct:
        shard_of = jnp.arange(blocks, dtype=jnp.int32) // sub_count
        sector_of = jnp.arange(blocks, dtype=jnp.int32) % sub_count
        holder = jnp.argmax(owners[shard_of] == sector_of[:, None], axis=1).astype(jnp.int32)
        sequence = flip_order(members, beam_count)
        position = jnp.asarray(np.argsort(sequence).astype(np.int32))
        slots = position[jnp.bitwise_xor(member_at, holder * beam_count + shard_of)]
    else:
        slots = jnp.arange(blocks, dtype=jnp.int32)
    merged = merge_call(
        slots,
        gathered,
        merge_tables(shifts, ratios, B),
        kernel_tables(B),
    )
    if direct:
        ordered = merged.transpose(0, 2, 4, 1, 3).reshape(blocks, 2, sector_width, own_rows)
        received = swap_ordered(ordered, member_at, ("sub4", "beam"), sequence)
        received = received.transpose(1, 2, 0, 3)
        return received.reshape(1, 1, 2, sector_width, members * own_rows)
    merged = merged.transpose(1, 2, 3, 0, 4).reshape(4, 2, own_rows, B)

    tiles = merged.reshape(4, 2, own_rows, beam_count, sub_count, sector_width // 4)
    beam_ids = jnp.arange(beam_count, dtype=jnp.int32)[:, None]
    picked = tiles[:, :, :, beam_ids, owners, :]
    outgoing = picked.transpose(4, 3, 1, 5, 0, 2).reshape(
        sub_count * beam_count, 2, sector_width, own_rows
    )
    received = lax.all_to_all(outgoing, ("grp", "sub4", "beam"), 0, 0, tiled=True)
    received = received.reshape(group_count, members, 2, sector_width, own_rows)
    received = received.transpose(0, 2, 3, 1, 4)
    return received.reshape(1, group_count, 2, sector_width, members * own_rows)


def solution(mesh):
    shape = dict(mesh.shape)
    devices = mesh.devices.reshape(
        shape["swath"], shape["sub"] // GROUP_SUBS, GROUP_SUBS, shape["beam"], shape["half"]
    )
    split = Mesh(devices, ("swath", "grp", "sub4", "beam", "half"))
    placed = (P(("grp", "sub4"), None, ("swath", "half"), "beam"), P(), P())
    return jax.shard_map(
        body,
        mesh=split,
        in_specs=placed,
        out_specs=P(("grp", "sub4", "beam"), None, None, None, ("swath", "half")),
        check_vma=False,
    )
```

```python
import math

import jax
import numpy as np
import jax.numpy as jnp
from jax import lax
from jax.experimental import pallas as pl
from jax.experimental.pallas import tpu as pltpu
from jax.sharding import Mesh
from jax.sharding import PartitionSpec as P

B = 1024
NR = 1024
GROUP_SUBS = 4


def odd_values(beam_total):
    spacing = np.arange(beam_total, dtype=np.int64)[None, :] - np.arange(beam_total, dtype=np.int64)[:, None]
    parity = np.where(spacing % 2 == 0, 1.0, -1.0).astype(np.float32)
    angles = (2.0 * spacing.astype(np.float32) + np.float32(1.0)) * np.float32(math.pi / (2.0 * beam_total))
    values = parity * np.cos(angles) / (np.float32(beam_total) * np.sin(angles))
    return values.astype(np.float32).astype(jnp.bfloat16)


def split_order(beam_total):
    return np.concatenate([np.arange(0, beam_total, 2), np.arange(1, beam_total, 2)])


def spin(parts, scale, lead, first_at, beams_out):
    count = parts.shape[-1]
    lanes = 128
    coarse = jnp.asarray(
        (2.0 * lead * lanes / beams_out) * np.arange(count // lanes) + ((2 * first_at + 1) / beams_out - 1.0),
        jnp.float32,
    )
    fine = jnp.asarray((2.0 * lead / beams_out) * np.arange(lanes), jnp.float32)
    rough = scale[..., None] * coarse
    small = scale[..., None] * fine
    c1 = jnp.cos(rough)[..., None]
    s1 = jnp.sin(rough)[..., None]
    c2 = jnp.cos(small)[..., None, :]
    s2 = jnp.sin(small)[..., None, :]
    cosine = c1 * c2 - s1 * s2
    sines = s1 * c2 + c1 * s2
    grid = parts.shape[:-3] + (parts.shape[-2], count // lanes, lanes)
    real_part = parts[..., 0, :, :].reshape(grid)
    imag_part = parts[..., 1, :, :].reshape(grid)
    turned = jnp.stack(
        [real_part * cosine - imag_part * sines, real_part * sines + imag_part * cosine], -4
    )
    return turned.reshape(parts.shape)


def odd_local(children, kernel):
    product = jnp.dot(
        children.reshape(-1, children.shape[-1]), kernel, preferred_element_type=jnp.float32
    )
    return product.reshape(children.shape[:-1] + (kernel.shape[1],))


LANES = 128


TILE = 256


def toeplitz_tiles(matrix):
    count = matrix.shape[0] // TILE
    tiles = []
    for gap in range(-(count - 1), count):
        i = max(0, -gap)
        j = i + gap
        tiles.append(matrix[i * TILE:(i + 1) * TILE, j * TILE:(j + 1) * TILE])
    tiles = np.stack(tiles)
    for i in range(count):
        for j in range(count):
            assert np.array_equal(matrix[i * TILE:(i + 1) * TILE, j * TILE:(j + 1) * TILE], tiles[j - i + count - 1])
    return tiles


def kernel_tables(width):
    one = toeplitz_tiles(odd_values(width))
    order = split_order(2 * width)
    two = odd_values(2 * width)[order][:, order]
    assert np.array_equal(two[:width, :width], two[width:, width:])
    quads = np.stack([toeplitz_tiles(two[:width, :width]), toeplitz_tiles(two[:width, width:]),
                      toeplitz_tiles(two[width:, :width])])
    return jnp.asarray(np.concatenate([one[None], quads]))


def merge_kernel(slot_ref, x_ref, t1c, t1s, f1c, f1s, t2c, t2s, f2c, f2s, k_hbm, o_ref,
                 k1_v, k2_v, first_v, odd1_v, odd2_v, sems):
    members, _, rows, local = x_ref.shape
    beam_count = members // 4
    blocks = local // LANES
    wide = beam_count * blocks
    half = wide * LANES
    load_one = pltpu.make_async_copy(k_hbm.at[0], k1_v, sems.at[0])
    load_two = pltpu.make_async_copy(k_hbm.at[pl.ds(1, 3)], k2_v, sems.at[1])
    load_one.start()
    load_two.start()

    def column(ref, a, b, u):
        return ref[a, b][:, u:u + 1]

    def turn(xr, xi, c1, s1, c2, s2):
        cosine = c1 * c2 - s1 * s2
        sines = s1 * c2 + c1 * s2
        return xr * cosine - xi * sines, xr * sines + xi * cosine

    for pair in range(2):
        for u in range(wide):
            b, k = divmod(u, blocks)
            cols = pl.ds(k * LANES, LANES)
            re_sum = None
            for m in range(2):
                s = 2 * pair + m
                xr = x_ref[s * beam_count + b, 0, :, cols].astype(jnp.float32)
                xi = x_ref[s * beam_count + b, 1, :, cols].astype(jnp.float32)
                re, im = turn(xr, xi, column(t1c, s, 0, u), column(t1s, s, 0, u), f1c[s], f1s[s])
                re_sum = re if re_sum is None else re_sum + re
                im_sum = im if m == 0 else im_sum + im
            out_cols = pl.ds(u * LANES, LANES)
            first_v[pair, pl.ds(0, rows), out_cols] = re_sum.astype(first_v.dtype)
            first_v[pair, pl.ds(rows, rows), out_cols] = im_sum.astype(first_v.dtype)

    load_one.wait()
    count = half // TILE
    per_piece = local // TILE
    parts = []
    for i in range(count):
        b, k = divmod(i, per_piece)
        stacked = [x_ref[s * beam_count + b, :, :, pl.ds(k * TILE, TILE)] for s in range(4)]
        parts.append(jnp.concatenate(stacked, axis=0).reshape(8 * rows, TILE))
    for j in range(count):
        total = None
        for i in range(count):
            term = jnp.dot(parts[i], k1_v[j - i + count - 1], preferred_element_type=jnp.float32)
            total = term if total is None else total + term
        odd1_v[:, :, pl.ds(j * TILE, TILE)] = total.reshape(4, 2 * rows, TILE)

    for pair in range(2):
        for u in range(wide):
            cols = pl.ds(u * LANES, LANES)
            for m in range(2):
                s = 2 * pair + m
                xr = odd1_v[s, pl.ds(0, rows), cols]
                xi = odd1_v[s, pl.ds(rows, rows), cols]
                re, im = turn(xr, xi, column(t1c, s, 1, u), column(t1s, s, 1, u), f1c[s], f1s[s])
                re_sum = re if m == 0 else re_sum + re
                im_sum = im if m == 0 else im_sum + im
            out_cols = pl.ds(half + u * LANES, LANES)
            first_v[pair, pl.ds(0, rows), out_cols] = re_sum.astype(first_v.dtype)
            first_v[pair, pl.ds(rows, rows), out_cols] = im_sum.astype(first_v.dtype)

    load_two.wait()
    evens = [first_v[:, :, pl.ds(i * TILE, TILE)].reshape(4 * rows, TILE) for i in range(count)]
    odds = [first_v[:, :, pl.ds(half + i * TILE, TILE)].reshape(4 * rows, TILE) for i in range(count)]
    for j in range(count):
        even_out = None
        odd_out = None
        for i in range(count):
            gap = j - i + count - 1
            term_e = jnp.dot(evens[i], k2_v[0, gap], preferred_element_type=jnp.float32)
            term_e += jnp.dot(odds[i], k2_v[2, gap], preferred_element_type=jnp.float32)
            term_o = jnp.dot(evens[i], k2_v[1, gap], preferred_element_type=jnp.float32)
            term_o += jnp.dot(odds[i], k2_v[0, gap], preferred_element_type=jnp.float32)
            even_out = term_e if even_out is None else even_out + term_e
            odd_out = term_o if odd_out is None else odd_out + term_o
        odd2_v[:, :, pl.ds(j * TILE, TILE)] = even_out.reshape(2, 2 * rows, TILE)
        odd2_v[:, :, pl.ds(half + j * TILE, TILE)] = odd_out.reshape(2, 2 * rows, TILE)

    for t in range(4):
        for u in range(wide):
            at = (t // 2) * half + u * LANES if t % 2 == 0 else (t // 2) * half + u * LANES
            cols = pl.ds(at, LANES)
            for pair in range(2):
                if t % 2 == 0:
                    xr = first_v[pair, pl.ds(0, rows), cols].astype(jnp.float32)
                    xi = first_v[pair, pl.ds(rows, rows), cols].astype(jnp.float32)
                else:
                    xr = odd2_v[pair, pl.ds(0, rows), cols]
                    xi = odd2_v[pair, pl.ds(rows, rows), cols]
                re, im = turn(xr, xi, column(t2c, pair, t, u), column(t2s, pair, t, u), f2c[pair], f2s[pair])
                re_sum = re if pair == 0 else re_sum + re
                im_sum = im if pair == 0 else im_sum + im
            slot = slot_ref[u]
            o_ref[slot, t, 0] = re_sum.astype(o_ref.dtype)
            o_ref[slot, t, 1] = im_sum.astype(o_ref.dtype)


def merge_call(slots, x, tables, kernels, interpret=False):
    members, _, rows, local = x.shape
    width = local * members // 4
    vmem = pl.BlockSpec(memory_space=pltpu.VMEM)
    hbm = pl.BlockSpec(memory_space=pl.ANY)
    smem = pl.BlockSpec(memory_space=pltpu.SMEM)
    return pl.pallas_call(
        merge_kernel,
        out_shape=jax.ShapeDtypeStruct((width // LANES, 4, 2, rows, LANES), jnp.bfloat16),
        in_specs=[smem] + [vmem] * 9 + [hbm],
        out_specs=vmem,
        scratch_shapes=[
            pltpu.VMEM(kernels.shape[1:], jnp.bfloat16),
            pltpu.VMEM((3,) + kernels.shape[1:], jnp.bfloat16),
            pltpu.VMEM((2, 2 * rows, 2 * width), jnp.bfloat16),
            pltpu.VMEM((4, 2 * rows, width), jnp.float32),
            pltpu.VMEM((2, 2 * rows, 2 * width), jnp.float32),
            pltpu.SemaphoreType.DMA((2,)),
        ],
        compiler_params=pltpu.CompilerParams(vmem_limit_bytes=48 * 1024 * 1024),
        interpret=interpret,
    )(slots, x, *tables, kernels)


def merge_tables(shifts, ratios, width):
    units = np.arange(width // LANES)
    fine = jnp.asarray(np.arange(LANES) / 512.0, jnp.float32)
    scale_one = shifts[:, None] * ratios[None, :]
    coarse_one = jnp.asarray(
        [0.25 * units + ((2 * t + 1) / (2 * width) - 1.0) for t in range(2)], jnp.float32
    )
    rough_one = scale_one[:, None, None, :] * coarse_one[None, :, :, None]
    small_one = scale_one[:, :, None] * fine
    centers = (shifts[0::2] + shifts[1::2]) * 0.5
    scale_two = centers[:, None] * ratios[None, :]
    coarse_two = jnp.asarray(
        [0.25 * units + ((2 * t + 1) / (4 * width) - 1.0) for t in range(4)], jnp.float32
    )
    rough_two = scale_two[:, None, None, :] * coarse_two[None, :, :, None]
    small_two = scale_two[:, :, None] * fine
    rough_one = jnp.swapaxes(rough_one, -1, -2)
    rough_two = jnp.swapaxes(rough_two, -1, -2)
    return (jnp.cos(rough_one), jnp.sin(rough_one), jnp.cos(small_one), jnp.sin(small_one),
            jnp.cos(rough_two), jnp.sin(rough_two), jnp.cos(small_two), jnp.sin(small_two))


def flip_order(count, beam_count):
    rest = sorted(range(1, count), key=lambda f: (-(f // beam_count), -f))
    return np.array([0] + rest, dtype=np.int32)


def swap_ordered(ordered, place, axes, order):
    count = ordered.shape[0]
    moved = [ordered[0]]
    for at in range(1, count):
        flip = int(order[at])
        pairs = [(i, i ^ flip) for i in range(count)]
        moved.append(lax.ppermute(ordered[at], axes, pairs))
    position = jnp.asarray(np.argsort(order).astype(np.int32))
    senders = position[jnp.bitwise_xor(place, jnp.arange(count, dtype=jnp.int32))]
    return jnp.take(jnp.stack(moved), senders, axis=0)


def body(images, offsets, owners):
    group_count = lax.axis_size("grp")
    sub_count = group_count * GROUP_SUBS
    beam_count = lax.axis_size("beam")
    group_at = lax.axis_index("grp")
    member_at = lax.axis_index("sub4") * beam_count + lax.axis_index("beam")
    half_side = lax.axis_index("half")
    members = GROUP_SUBS * beam_count
    half_rows = images.shape[2]
    own_rows = half_rows // members
    local_beams = images.shape[3]

    pieces = images[0].reshape(2, members, own_rows, local_beams).transpose(1, 0, 2, 3)
    gathered = lax.all_to_all(pieces, ("sub4", "beam"), 0, 0, tiled=True)
    rows_at = half_side * half_rows + member_at * own_rows + jnp.arange(own_rows, dtype=jnp.int32)
    ratios = NR / (NR + rows_at.astype(jnp.float32))
    shifts = lax.dynamic_slice_in_dim(offsets, group_at * GROUP_SUBS, GROUP_SUBS, 0)
    order = split_order(2 * B)
    blocks = B // LANES
    sector_width = 4 * B // (beam_count * sub_count)
    direct = group_count == 1 and sector_width == 4 * LANES
    if direct:
        shard_of = jnp.arange(blocks, dtype=jnp.int32) // sub_count
        sector_of = jnp.arange(blocks, dtype=jnp.int32) % sub_count
        holder = jnp.argmax(owners[shard_of] == sector_of[:, None], axis=1).astype(jnp.int32)
        sequence = flip_order(members, beam_count)
        position = jnp.asarray(np.argsort(sequence).astype(np.int32))
        slots = position[jnp.bitwise_xor(member_at, holder * beam_count + shard_of)]
    else:
        slots = jnp.arange(blocks, dtype=jnp.int32)
    merged = merge_call(
        slots,
        gathered,
        merge_tables(shifts, ratios, B),
        kernel_tables(B),
    )
    if direct:
        ordered = merged.transpose(0, 2, 4, 1, 3).reshape(blocks, 2, sector_width, own_rows)
        received = swap_ordered(ordered, member_at, ("sub4", "beam"), sequence)
        received = received.transpose(1, 2, 0, 3)
        return received.reshape(1, 1, 2, sector_width, members * own_rows)
    merged = merged.transpose(1, 2, 3, 0, 4).reshape(4, 2, own_rows, B)

    tiles = merged.reshape(4, 2, own_rows, beam_count, sub_count, sector_width // 4)
    beam_ids = jnp.arange(beam_count, dtype=jnp.int32)[:, None]
    picked = tiles[:, :, :, beam_ids, owners, :]
    outgoing = picked.transpose(4, 3, 1, 5, 0, 2).reshape(
        sub_count * beam_count, 2, sector_width, own_rows
    )
    received = lax.all_to_all(outgoing, ("grp", "sub4", "beam"), 0, 0, tiled=True)
    received = received.reshape(group_count, members, 2, sector_width, own_rows)
    received = received.transpose(0, 2, 3, 1, 4)
    return received.reshape(1, group_count, 2, sector_width, members * own_rows)


def solution(mesh):
    shape = dict(mesh.shape)
    devices = mesh.devices.reshape(
        shape["swath"], shape["sub"] // GROUP_SUBS, GROUP_SUBS, shape["beam"], shape["half"]
    )
    split = Mesh(devices, ("swath", "grp", "sub4", "beam", "half"))
    placed = (P(("grp", "sub4"), None, ("swath", "half"), "beam"), P(), P())
    return jax.shard_map(
        body,
        mesh=split,
        in_specs=placed,
        out_specs=P(("grp", "sub4", "beam"), None, None, None, ("swath", "half")),
        check_vma=False,
    )
```

```python
import math

import jax
import numpy as np
import jax.numpy as jnp
from jax import lax
from jax.experimental import pallas as pl
from jax.experimental.pallas import tpu as pltpu
from jax.sharding import Mesh
from jax.sharding import PartitionSpec as P

B = 1024
NR = 1024
GROUP_SUBS = 4


def odd_values(beam_total):
    spacing = np.arange(beam_total, dtype=np.int64)[None, :] - np.arange(beam_total, dtype=np.int64)[:, None]
    parity = np.where(spacing % 2 == 0, 1.0, -1.0).astype(np.float32)
    angles = (2.0 * spacing.astype(np.float32) + np.float32(1.0)) * np.float32(math.pi / (2.0 * beam_total))
    values = parity * np.cos(angles) / (np.float32(beam_total) * np.sin(angles))
    return values.astype(np.float32).astype(jnp.bfloat16)


def split_order(beam_total):
    return np.concatenate([np.arange(0, beam_total, 2), np.arange(1, beam_total, 2)])


def spin(parts, scale, lead, first_at, beams_out):
    count = parts.shape[-1]
    lanes = 128
    coarse = jnp.asarray(
        (2.0 * lead * lanes / beams_out) * np.arange(count // lanes) + ((2 * first_at + 1) / beams_out - 1.0),
        jnp.float32,
    )
    fine = jnp.asarray((2.0 * lead / beams_out) * np.arange(lanes), jnp.float32)
    rough = scale[..., None] * coarse
    small = scale[..., None] * fine
    c1 = jnp.cos(rough)[..., None]
    s1 = jnp.sin(rough)[..., None]
    c2 = jnp.cos(small)[..., None, :]
    s2 = jnp.sin(small)[..., None, :]
    cosine = c1 * c2 - s1 * s2
    sines = s1 * c2 + c1 * s2
    grid = parts.shape[:-3] + (parts.shape[-2], count // lanes, lanes)
    real_part = parts[..., 0, :, :].reshape(grid)
    imag_part = parts[..., 1, :, :].reshape(grid)
    turned = jnp.stack(
        [real_part * cosine - imag_part * sines, real_part * sines + imag_part * cosine], -4
    )
    return turned.reshape(parts.shape)


def odd_local(children, kernel):
    product = jnp.dot(
        children.reshape(-1, children.shape[-1]), kernel, preferred_element_type=jnp.float32
    )
    return product.reshape(children.shape[:-1] + (kernel.shape[1],))


LANES = 128


TILE = 256


def toeplitz_tiles(matrix):
    count = matrix.shape[0] // TILE
    tiles = []
    for gap in range(-(count - 1), count):
        i = max(0, -gap)
        j = i + gap
        tiles.append(matrix[i * TILE:(i + 1) * TILE, j * TILE:(j + 1) * TILE])
    tiles = np.stack(tiles)
    for i in range(count):
        for j in range(count):
            assert np.array_equal(matrix[i * TILE:(i + 1) * TILE, j * TILE:(j + 1) * TILE], tiles[j - i + count - 1])
    return tiles


def kernel_tables(width):
    one = toeplitz_tiles(odd_values(width))
    order = split_order(2 * width)
    two = odd_values(2 * width)[order][:, order]
    assert np.array_equal(two[:width, :width], two[width:, width:])
    quads = np.stack([toeplitz_tiles(two[:width, :width]), toeplitz_tiles(two[:width, width:]),
                      toeplitz_tiles(two[width:, :width])])
    return jnp.asarray(np.concatenate([one[None], quads]))


def merge_kernel(slot_ref, x_ref, t1c, t1s, f1c, f1s, t2c, t2s, f2c, f2s, k_hbm, o_ref,
                 k1_v, k2_v, first_v, odd1_v, odd2_v, sems):
    members, _, rows, local = x_ref.shape
    beam_count = members // 4
    blocks = local // LANES
    wide = beam_count * blocks
    half = wide * LANES
    gaps = k1_v.shape[0]
    first_use = [gaps // 2 - g for g in range(gaps // 2 + 1)] + list(range(gaps // 2 + 1, gaps))
    load_one = {g: pltpu.make_async_copy(k_hbm.at[0, g], k1_v.at[g], sems.at[0, g]) for g in first_use}
    load_two = {g: pltpu.make_async_copy(k_hbm.at[pl.ds(1, 3), g], k2_v.at[:, g], sems.at[1, g]) for g in first_use}
    for g in first_use:
        load_one[g].start()
    for g in first_use:
        load_two[g].start()
    landed = set()

    def tile_one(g):
        if ("one", g) not in landed:
            load_one[g].wait()
            landed.add(("one", g))
        return k1_v[g]

    def tile_two(q, g):
        if ("two", g) not in landed:
            load_two[g].wait()
            landed.add(("two", g))
        return k2_v[q, g]

    def column(ref, a, b, u):
        return ref[a, b][:, u:u + 1]

    def turn(xr, xi, c1, s1, c2, s2):
        cosine = c1 * c2 - s1 * s2
        sines = s1 * c2 + c1 * s2
        return xr * cosine - xi * sines, xr * sines + xi * cosine

    for pair in range(2):
        for u in range(wide):
            b, k = divmod(u, blocks)
            cols = pl.ds(k * LANES, LANES)
            re_sum = None
            for m in range(2):
                s = 2 * pair + m
                xr = x_ref[s * beam_count + b, 0, :, cols].astype(jnp.float32)
                xi = x_ref[s * beam_count + b, 1, :, cols].astype(jnp.float32)
                re, im = turn(xr, xi, column(t1c, s, 0, u), column(t1s, s, 0, u), f1c[s], f1s[s])
                re_sum = re if re_sum is None else re_sum + re
                im_sum = im if m == 0 else im_sum + im
            out_cols = pl.ds(u * LANES, LANES)
            first_v[pair, pl.ds(0, rows), out_cols] = re_sum.astype(first_v.dtype)
            first_v[pair, pl.ds(rows, rows), out_cols] = im_sum.astype(first_v.dtype)

    count = half // TILE
    per_piece = local // TILE
    parts = []
    for i in range(count):
        b, k = divmod(i, per_piece)
        stacked = [x_ref[s * beam_count + b, :, :, pl.ds(k * TILE, TILE)] for s in range(4)]
        parts.append(jnp.concatenate(stacked, axis=0).reshape(8 * rows, TILE))
    for j in range(count):
        total = None
        for i in range(count):
            term = jnp.dot(parts[i], tile_one(j - i + count - 1), preferred_element_type=jnp.float32)
            total = term if total is None else total + term
        odd1_v[:, :, pl.ds(j * TILE, TILE)] = total.reshape(4, 2 * rows, TILE)

    for pair in range(2):
        for u in range(wide):
            cols = pl.ds(u * LANES, LANES)
            for m in range(2):
                s = 2 * pair + m
                xr = odd1_v[s, pl.ds(0, rows), cols]
                xi = odd1_v[s, pl.ds(rows, rows), cols]
                re, im = turn(xr, xi, column(t1c, s, 1, u), column(t1s, s, 1, u), f1c[s], f1s[s])
                re_sum = re if m == 0 else re_sum + re
                im_sum = im if m == 0 else im_sum + im
            out_cols = pl.ds(half + u * LANES, LANES)
            first_v[pair, pl.ds(0, rows), out_cols] = re_sum.astype(first_v.dtype)
            first_v[pair, pl.ds(rows, rows), out_cols] = im_sum.astype(first_v.dtype)

    evens = [first_v[:, :, pl.ds(i * TILE, TILE)].reshape(4 * rows, TILE) for i in range(count)]
    odds = [first_v[:, :, pl.ds(half + i * TILE, TILE)].reshape(4 * rows, TILE) for i in range(count)]
    for j in range(count):
        even_out = None
        odd_out = None
        for i in range(count):
            gap = j - i + count - 1
            term_e = jnp.dot(evens[i], tile_two(0, gap), preferred_element_type=jnp.float32)
            term_e += jnp.dot(odds[i], tile_two(2, gap), preferred_element_type=jnp.float32)
            term_o = jnp.dot(evens[i], tile_two(1, gap), preferred_element_type=jnp.float32)
            term_o += jnp.dot(odds[i], tile_two(0, gap), preferred_element_type=jnp.float32)
            even_out = term_e if even_out is None else even_out + term_e
            odd_out = term_o if odd_out is None else odd_out + term_o
        odd2_v[:, :, pl.ds(j * TILE, TILE)] = even_out.reshape(2, 2 * rows, TILE)
        odd2_v[:, :, pl.ds(half + j * TILE, TILE)] = odd_out.reshape(2, 2 * rows, TILE)

    for t in range(4):
        for u in range(wide):
            at = (t // 2) * half + u * LANES if t % 2 == 0 else (t // 2) * half + u * LANES
            cols = pl.ds(at, LANES)
            for pair in range(2):
                if t % 2 == 0:
                    xr = first_v[pair, pl.ds(0, rows), cols].astype(jnp.float32)
                    xi = first_v[pair, pl.ds(rows, rows), cols].astype(jnp.float32)
                else:
                    xr = odd2_v[pair, pl.ds(0, rows), cols]
                    xi = odd2_v[pair, pl.ds(rows, rows), cols]
                re, im = turn(xr, xi, column(t2c, pair, t, u), column(t2s, pair, t, u), f2c[pair], f2s[pair])
                re_sum = re if pair == 0 else re_sum + re
                im_sum = im if pair == 0 else im_sum + im
            slot = slot_ref[u]
            o_ref[slot, t, 0] = re_sum.astype(o_ref.dtype)
            o_ref[slot, t, 1] = im_sum.astype(o_ref.dtype)


def merge_call(slots, x, tables, kernels, interpret=False):
    members, _, rows, local = x.shape
    width = local * members // 4
    vmem = pl.BlockSpec(memory_space=pltpu.VMEM)
    hbm = pl.BlockSpec(memory_space=pl.ANY)
    smem = pl.BlockSpec(memory_space=pltpu.SMEM)
    return pl.pallas_call(
        merge_kernel,
        out_shape=jax.ShapeDtypeStruct((width // LANES, 4, 2, rows, LANES), jnp.bfloat16),
        in_specs=[smem] + [vmem] * 9 + [hbm],
        out_specs=vmem,
        scratch_shapes=[
            pltpu.VMEM(kernels.shape[1:], jnp.bfloat16),
            pltpu.VMEM((3,) + kernels.shape[1:], jnp.bfloat16),
            pltpu.VMEM((2, 2 * rows, 2 * width), jnp.bfloat16),
            pltpu.VMEM((4, 2 * rows, width), jnp.float32),
            pltpu.VMEM((2, 2 * rows, 2 * width), jnp.float32),
            pltpu.SemaphoreType.DMA((2, kernels.shape[1])),
        ],
        compiler_params=pltpu.CompilerParams(vmem_limit_bytes=48 * 1024 * 1024),
        interpret=interpret,
    )(slots, x, *tables, kernels)


def merge_tables(shifts, ratios, width):
    units = np.arange(width // LANES)
    fine = jnp.asarray(np.arange(LANES) / 512.0, jnp.float32)
    scale_one = shifts[:, None] * ratios[None, :]
    coarse_one = jnp.asarray(
        [0.25 * units + ((2 * t + 1) / (2 * width) - 1.0) for t in range(2)], jnp.float32
    )
    rough_one = scale_one[:, None, None, :] * coarse_one[None, :, :, None]
    small_one = scale_one[:, :, None] * fine
    centers = (shifts[0::2] + shifts[1::2]) * 0.5
    scale_two = centers[:, None] * ratios[None, :]
    coarse_two = jnp.asarray(
        [0.25 * units + ((2 * t + 1) / (4 * width) - 1.0) for t in range(4)], jnp.float32
    )
    rough_two = scale_two[:, None, None, :] * coarse_two[None, :, :, None]
    small_two = scale_two[:, :, None] * fine
    rough_one = jnp.swapaxes(rough_one, -1, -2)
    rough_two = jnp.swapaxes(rough_two, -1, -2)
    return (jnp.cos(rough_one), jnp.sin(rough_one), jnp.cos(small_one), jnp.sin(small_one),
            jnp.cos(rough_two), jnp.sin(rough_two), jnp.cos(small_two), jnp.sin(small_two))


def flip_order(count, beam_count):
    rest = sorted(range(1, count), key=lambda f: (-(f // beam_count), f))
    return np.array([0] + rest, dtype=np.int32)


def swap_ordered(ordered, place, axes, order):
    count = ordered.shape[0]
    moved = [ordered[0]]
    for at in range(1, count):
        flip = int(order[at])
        pairs = [(i, i ^ flip) for i in range(count)]
        moved.append(lax.ppermute(ordered[at], axes, pairs))
    position = jnp.asarray(np.argsort(order).astype(np.int32))
    senders = position[jnp.bitwise_xor(place, jnp.arange(count, dtype=jnp.int32))]
    return jnp.take(jnp.stack(moved), senders, axis=0)


def body(images, offsets, owners):
    group_count = lax.axis_size("grp")
    sub_count = group_count * GROUP_SUBS
    beam_count = lax.axis_size("beam")
    group_at = lax.axis_index("grp")
    member_at = lax.axis_index("sub4") * beam_count + lax.axis_index("beam")
    half_side = lax.axis_index("half")
    members = GROUP_SUBS * beam_count
    half_rows = images.shape[2]
    own_rows = half_rows // members
    local_beams = images.shape[3]

    pieces = images[0].reshape(2, members, own_rows, local_beams).transpose(1, 0, 2, 3)
    gathered = lax.all_to_all(pieces, ("sub4", "beam"), 0, 0, tiled=True)
    rows_at = half_side * half_rows + member_at * own_rows + jnp.arange(own_rows, dtype=jnp.int32)
    ratios = NR / (NR + rows_at.astype(jnp.float32))
    shifts = lax.dynamic_slice_in_dim(offsets, group_at * GROUP_SUBS, GROUP_SUBS, 0)
    order = split_order(2 * B)
    blocks = B // LANES
    sector_width = 4 * B // (beam_count * sub_count)
    direct = group_count == 1 and sector_width == 4 * LANES
    if direct:
        shard_of = jnp.arange(blocks, dtype=jnp.int32) // sub_count
        sector_of = jnp.arange(blocks, dtype=jnp.int32) % sub_count
        holder = jnp.argmax(owners[shard_of] == sector_of[:, None], axis=1).astype(jnp.int32)
        sequence = flip_order(members, beam_count)
        position = jnp.asarray(np.argsort(sequence).astype(np.int32))
        slots = position[jnp.bitwise_xor(member_at, holder * beam_count + shard_of)]
    else:
        slots = jnp.arange(blocks, dtype=jnp.int32)
    merged = merge_call(
        slots,
        gathered,
        merge_tables(shifts, ratios, B),
        kernel_tables(B),
    )
    if direct:
        ordered = merged.transpose(0, 2, 4, 1, 3).reshape(blocks, 2, sector_width, own_rows)
        received = swap_ordered(ordered, member_at, ("sub4", "beam"), sequence)
        received = received.transpose(1, 2, 0, 3)
        return received.reshape(1, 1, 2, sector_width, members * own_rows)
    merged = merged.transpose(1, 2, 3, 0, 4).reshape(4, 2, own_rows, B)

    tiles = merged.reshape(4, 2, own_rows, beam_count, sub_count, sector_width // 4)
    beam_ids = jnp.arange(beam_count, dtype=jnp.int32)[:, None]
    picked = tiles[:, :, :, beam_ids, owners, :]
    outgoing = picked.transpose(4, 3, 1, 5, 0, 2).reshape(
        sub_count * beam_count, 2, sector_width, own_rows
    )
    received = lax.all_to_all(outgoing, ("grp", "sub4", "beam"), 0, 0, tiled=True)
    received = received.reshape(group_count, members, 2, sector_width, own_rows)
    received = received.transpose(0, 2, 3, 1, 4)
    return received.reshape(1, group_count, 2, sector_width, members * own_rows)


def solution(mesh):
    shape = dict(mesh.shape)
    devices = mesh.devices.reshape(
        shape["swath"], shape["sub"] // GROUP_SUBS, GROUP_SUBS, shape["beam"], shape["half"]
    )
    split = Mesh(devices, ("swath", "grp", "sub4", "beam", "half"))
    placed = (P(("grp", "sub4"), None, ("swath", "half"), "beam"), P(), P())
    return jax.shard_map(
        body,
        mesh=split,
        in_specs=placed,
        out_specs=P(("grp", "sub4", "beam"), None, None, None, ("swath", "half")),
        check_vma=False,
    )
```

```python
import math

import jax
import numpy as np
import jax.numpy as jnp
from jax import lax
from jax.experimental import pallas as pl
from jax.experimental.pallas import tpu as pltpu
from jax.sharding import Mesh
from jax.sharding import PartitionSpec as P

B = 1024
NR = 1024
GROUP_SUBS = 4


def odd_values(beam_total):
    spacing = np.arange(beam_total, dtype=np.int64)[None, :] - np.arange(beam_total, dtype=np.int64)[:, None]
    parity = np.where(spacing % 2 == 0, 1.0, -1.0).astype(np.float32)
    angles = (2.0 * spacing.astype(np.float32) + np.float32(1.0)) * np.float32(math.pi / (2.0 * beam_total))
    values = parity * np.cos(angles) / (np.float32(beam_total) * np.sin(angles))
    return values.astype(np.float32).astype(jnp.bfloat16)


def split_order(beam_total):
    return np.concatenate([np.arange(0, beam_total, 2), np.arange(1, beam_total, 2)])


def spin(parts, scale, lead, first_at, beams_out):
    count = parts.shape[-1]
    lanes = 128
    coarse = jnp.asarray(
        (2.0 * lead * lanes / beams_out) * np.arange(count // lanes) + ((2 * first_at + 1) / beams_out - 1.0),
        jnp.float32,
    )
    fine = jnp.asarray((2.0 * lead / beams_out) * np.arange(lanes), jnp.float32)
    rough = scale[..., None] * coarse
    small = scale[..., None] * fine
    c1 = jnp.cos(rough)[..., None]
    s1 = jnp.sin(rough)[..., None]
    c2 = jnp.cos(small)[..., None, :]
    s2 = jnp.sin(small)[..., None, :]
    cosine = c1 * c2 - s1 * s2
    sines = s1 * c2 + c1 * s2
    grid = parts.shape[:-3] + (parts.shape[-2], count // lanes, lanes)
    real_part = parts[..., 0, :, :].reshape(grid)
    imag_part = parts[..., 1, :, :].reshape(grid)
    turned = jnp.stack(
        [real_part * cosine - imag_part * sines, real_part * sines + imag_part * cosine], -4
    )
    return turned.reshape(parts.shape)


def odd_local(children, kernel):
    product = jnp.dot(
        children.reshape(-1, children.shape[-1]), kernel, preferred_element_type=jnp.float32
    )
    return product.reshape(children.shape[:-1] + (kernel.shape[1],))


LANES = 128


TILE = 256


def toeplitz_tiles(matrix):
    count = matrix.shape[0] // TILE
    tiles = []
    for gap in range(-(count - 1), count):
        i = max(0, -gap)
        j = i + gap
        tiles.append(matrix[i * TILE:(i + 1) * TILE, j * TILE:(j + 1) * TILE])
    tiles = np.stack(tiles)
    for i in range(count):
        for j in range(count):
            assert np.array_equal(matrix[i * TILE:(i + 1) * TILE, j * TILE:(j + 1) * TILE], tiles[j - i + count - 1])
    return tiles


def kernel_tables(width):
    one = toeplitz_tiles(odd_values(width))
    order = split_order(2 * width)
    two = odd_values(2 * width)[order][:, order]
    assert np.array_equal(two[:width, :width], two[width:, width:])
    quads = np.stack([toeplitz_tiles(two[:width, :width]), toeplitz_tiles(two[:width, width:]),
                      toeplitz_tiles(two[width:, :width])])
    return jnp.asarray(np.concatenate([one[None], quads]))


def merge_kernel(slot_ref, x_ref, t1c, t1s, f1c, f1s, t2c, t2s, f2c, f2s, k_hbm, o_ref,
                 k1_v, k2_v, first_v, odd1_v, odd2_v, sems):
    members, _, rows, local = x_ref.shape
    beam_count = members // 4
    blocks = local // LANES
    wide = beam_count * blocks
    half = wide * LANES
    load_one = pltpu.make_async_copy(k_hbm.at[0], k1_v, sems.at[0])
    load_two = pltpu.make_async_copy(k_hbm.at[pl.ds(1, 3)], k2_v, sems.at[1])
    load_one.start()
    load_two.start()

    def column(ref, a, b, u):
        return ref[a, b][:, u:u + 1]

    def turn(xr, xi, c1, s1, c2, s2):
        cosine = c1 * c2 - s1 * s2
        sines = s1 * c2 + c1 * s2
        return xr * cosine - xi * sines, xr * sines + xi * cosine

    for pair in range(2):
        for u in range(wide):
            b, k = divmod(u, blocks)
            cols = pl.ds(k * LANES, LANES)
            re_sum = None
            for m in range(2):
                s = 2 * pair + m
                xr = x_ref[s * beam_count + b, 0, :, cols].astype(jnp.float32)
                xi = x_ref[s * beam_count + b, 1, :, cols].astype(jnp.float32)
                re, im = turn(xr, xi, column(t1c, s, 0, u), column(t1s, s, 0, u), f1c[s], f1s[s])
                re_sum = re if re_sum is None else re_sum + re
                im_sum = im if m == 0 else im_sum + im
            out_cols = pl.ds(u * LANES, LANES)
            first_v[pair, pl.ds(0, rows), out_cols] = re_sum.astype(first_v.dtype)
            first_v[pair, pl.ds(rows, rows), out_cols] = im_sum.astype(first_v.dtype)

    load_one.wait()
    count = half // TILE
    per_piece = local // TILE
    parts = []
    for i in range(count):
        b, k = divmod(i, per_piece)
        stacked = [x_ref[s * beam_count + b, :, :, pl.ds(k * TILE, TILE)] for s in range(4)]
        parts.append(jnp.concatenate(stacked, axis=0).reshape(8 * rows, TILE))
    for j in range(count):
        total = None
        for i in range(count):
            term = jnp.dot(parts[i], k1_v[j - i + count - 1], preferred_element_type=jnp.float32)
            total = term if total is None else total + term
        odd1_v[:, :, pl.ds(j * TILE, TILE)] = total.reshape(4, 2 * rows, TILE)

    for pair in range(2):
        for u in range(wide):
            cols = pl.ds(u * LANES, LANES)
            for m in range(2):
                s = 2 * pair + m
                xr = odd1_v[s, pl.ds(0, rows), cols]
                xi = odd1_v[s, pl.ds(rows, rows), cols]
                re, im = turn(xr, xi, column(t1c, s, 1, u), column(t1s, s, 1, u), f1c[s], f1s[s])
                re_sum = re if m == 0 else re_sum + re
                im_sum = im if m == 0 else im_sum + im
            out_cols = pl.ds(half + u * LANES, LANES)
            first_v[pair, pl.ds(0, rows), out_cols] = re_sum.astype(first_v.dtype)
            first_v[pair, pl.ds(rows, rows), out_cols] = im_sum.astype(first_v.dtype)

    load_two.wait()
    evens = [first_v[:, :, pl.ds(i * TILE, TILE)].reshape(4 * rows, TILE) for i in range(count)]
    odds = [first_v[:, :, pl.ds(half + i * TILE, TILE)].reshape(4 * rows, TILE) for i in range(count)]
    for j in range(count):
        even_out = None
        odd_out = None
        for i in range(count):
            gap = j - i + count - 1
            term_e = jnp.dot(evens[i], k2_v[0, gap], preferred_element_type=jnp.float32)
            term_e += jnp.dot(odds[i], k2_v[2, gap], preferred_element_type=jnp.float32)
            term_o = jnp.dot(evens[i], k2_v[1, gap], preferred_element_type=jnp.float32)
            term_o += jnp.dot(odds[i], k2_v[0, gap], preferred_element_type=jnp.float32)
            even_out = term_e if even_out is None else even_out + term_e
            odd_out = term_o if odd_out is None else odd_out + term_o
        odd2_v[:, :, pl.ds(j * TILE, TILE)] = even_out.reshape(2, 2 * rows, TILE)
        odd2_v[:, :, pl.ds(half + j * TILE, TILE)] = odd_out.reshape(2, 2 * rows, TILE)

    for t in range(4):
        for u in range(wide):
            at = (t // 2) * half + u * LANES if t % 2 == 0 else (t // 2) * half + u * LANES
            cols = pl.ds(at, LANES)
            for pair in range(2):
                if t % 2 == 0:
                    xr = first_v[pair, pl.ds(0, rows), cols].astype(jnp.float32)
                    xi = first_v[pair, pl.ds(rows, rows), cols].astype(jnp.float32)
                else:
                    xr = odd2_v[pair, pl.ds(0, rows), cols]
                    xi = odd2_v[pair, pl.ds(rows, rows), cols]
                re, im = turn(xr, xi, column(t2c, pair, t, u), column(t2s, pair, t, u), f2c[pair], f2s[pair])
                re_sum = re if pair == 0 else re_sum + re
                im_sum = im if pair == 0 else im_sum + im
            slot = slot_ref[u]
            o_ref[slot, t, 0] = re_sum.astype(o_ref.dtype)
            o_ref[slot, t, 1] = im_sum.astype(o_ref.dtype)


def merge_call(slots, x, tables, kernels, interpret=False):
    members, _, rows, local = x.shape
    width = local * members // 4
    vmem = pl.BlockSpec(memory_space=pltpu.VMEM)
    hbm = pl.BlockSpec(memory_space=pl.ANY)
    smem = pl.BlockSpec(memory_space=pltpu.SMEM)
    return pl.pallas_call(
        merge_kernel,
        out_shape=jax.ShapeDtypeStruct((width // LANES, 4, 2, rows, LANES), jnp.bfloat16),
        in_specs=[smem] + [vmem] * 9 + [hbm],
        out_specs=vmem,
        scratch_shapes=[
            pltpu.VMEM(kernels.shape[1:], jnp.bfloat16),
            pltpu.VMEM((3,) + kernels.shape[1:], jnp.bfloat16),
            pltpu.VMEM((2, 2 * rows, 2 * width), jnp.bfloat16),
            pltpu.VMEM((4, 2 * rows, width), jnp.float32),
            pltpu.VMEM((2, 2 * rows, 2 * width), jnp.float32),
            pltpu.SemaphoreType.DMA((2,)),
        ],
        compiler_params=pltpu.CompilerParams(vmem_limit_bytes=48 * 1024 * 1024),
        interpret=interpret,
    )(slots, x, *tables, kernels)


def merge_tables(shifts, ratios, width):
    units = np.arange(width // LANES)
    fine = jnp.asarray(np.arange(LANES) / 512.0, jnp.float32)
    scale_one = shifts[:, None] * ratios[None, :]
    coarse_one = jnp.asarray(
        [0.25 * units + ((2 * t + 1) / (2 * width) - 1.0) for t in range(2)], jnp.float32
    )
    rough_one = scale_one[:, None, None, :] * coarse_one[None, :, :, None]
    small_one = scale_one[:, :, None] * fine
    centers = (shifts[0::2] + shifts[1::2]) * 0.5
    scale_two = centers[:, None] * ratios[None, :]
    coarse_two = jnp.asarray(
        [0.25 * units + ((2 * t + 1) / (4 * width) - 1.0) for t in range(4)], jnp.float32
    )
    rough_two = scale_two[:, None, None, :] * coarse_two[None, :, :, None]
    small_two = scale_two[:, :, None] * fine
    rough_one = jnp.swapaxes(rough_one, -1, -2)
    rough_two = jnp.swapaxes(rough_two, -1, -2)
    return (jnp.cos(rough_one), jnp.sin(rough_one), jnp.cos(small_one), jnp.sin(small_one),
            jnp.cos(rough_two), jnp.sin(rough_two), jnp.cos(small_two), jnp.sin(small_two))


def flip_order(count, beam_count):
    rest = sorted(range(1, count), key=lambda f: (-(f // beam_count), f))
    return np.array([0] + rest, dtype=np.int32)


def swap_ordered(ordered, place, axes, order):
    count = ordered.shape[0]
    moved = [ordered[0]]
    for at in range(1, count):
        flip = int(order[at])
        pairs = [(i, i ^ flip) for i in range(count)]
        moved.append(lax.ppermute(ordered[at], axes, pairs))
    position = jnp.asarray(np.argsort(order).astype(np.int32))
    senders = position[jnp.bitwise_xor(place, jnp.arange(count, dtype=jnp.int32))]
    return jnp.take(jnp.stack(moved), senders, axis=0)


def body(images, offsets, owners):
    group_count = lax.axis_size("grp")
    sub_count = group_count * GROUP_SUBS
    beam_count = lax.axis_size("beam")
    group_at = lax.axis_index("grp")
    member_at = lax.axis_index("sub4") * beam_count + lax.axis_index("beam")
    half_side = lax.axis_index("half")
    members = GROUP_SUBS * beam_count
    half_rows = images.shape[2]
    own_rows = half_rows // members
    local_beams = images.shape[3]

    pieces = images[0].reshape(2, members, own_rows, local_beams).transpose(1, 0, 2, 3)
    gathered = lax.all_to_all(pieces, ("sub4", "beam"), 0, 0, tiled=True)
    rows_at = half_side * half_rows + member_at * own_rows + jnp.arange(own_rows, dtype=jnp.int32)
    ratios = NR / (NR + rows_at.astype(jnp.float32))
    shifts = lax.dynamic_slice_in_dim(offsets, group_at * GROUP_SUBS, GROUP_SUBS, 0)
    order = split_order(2 * B)
    blocks = B // LANES
    sector_width = 4 * B // (beam_count * sub_count)
    direct = group_count == 1 and sector_width == 4 * LANES
    if direct:
        shard_of = jnp.arange(blocks, dtype=jnp.int32) // sub_count
        sector_of = jnp.arange(blocks, dtype=jnp.int32) % sub_count
        holder = jnp.argmax(owners[shard_of] == sector_of[:, None], axis=1).astype(jnp.int32)
        sequence = flip_order(members, beam_count)
        position = jnp.asarray(np.argsort(sequence).astype(np.int32))
        slots = position[jnp.bitwise_xor(member_at, holder * beam_count + shard_of)]
    else:
        slots = jnp.arange(blocks, dtype=jnp.int32)
    merged = merge_call(
        slots,
        gathered,
        merge_tables(shifts, ratios, B),
        kernel_tables(B),
    )
    if direct:
        ordered = merged
        received = swap_ordered(ordered, member_at, ("sub4", "beam"), sequence)
        received = received.transpose(2, 4, 1, 0, 3)
        return received.reshape(1, 1, 2, sector_width, members * own_rows)
    merged = merged.transpose(1, 2, 3, 0, 4).reshape(4, 2, own_rows, B)

    tiles = merged.reshape(4, 2, own_rows, beam_count, sub_count, sector_width // 4)
    beam_ids = jnp.arange(beam_count, dtype=jnp.int32)[:, None]
    picked = tiles[:, :, :, beam_ids, owners, :]
    outgoing = picked.transpose(4, 3, 1, 5, 0, 2).reshape(
        sub_count * beam_count, 2, sector_width, own_rows
    )
    received = lax.all_to_all(outgoing, ("grp", "sub4", "beam"), 0, 0, tiled=True)
    received = received.reshape(group_count, members, 2, sector_width, own_rows)
    received = received.transpose(0, 2, 3, 1, 4)
    return received.reshape(1, group_count, 2, sector_width, members * own_rows)


def solution(mesh):
    shape = dict(mesh.shape)
    devices = mesh.devices.reshape(
        shape["swath"], shape["sub"] // GROUP_SUBS, GROUP_SUBS, shape["beam"], shape["half"]
    )
    split = Mesh(devices, ("swath", "grp", "sub4", "beam", "half"))
    placed = (P(("grp", "sub4"), None, ("swath", "half"), "beam"), P(), P())
    return jax.shard_map(
        body,
        mesh=split,
        in_specs=placed,
        out_specs=P(("grp", "sub4", "beam"), None, None, None, ("swath", "half")),
        check_vma=False,
    )
```

```python
import math

import jax
import numpy as np
import jax.numpy as jnp
from jax import lax
from jax.experimental import pallas as pl
from jax.experimental.pallas import tpu as pltpu
from jax.sharding import Mesh
from jax.sharding import PartitionSpec as P

B = 1024
NR = 1024
GROUP_SUBS = 4


def odd_values(beam_total):
    spacing = np.arange(beam_total, dtype=np.int64)[None, :] - np.arange(beam_total, dtype=np.int64)[:, None]
    parity = np.where(spacing % 2 == 0, 1.0, -1.0).astype(np.float32)
    angles = (2.0 * spacing.astype(np.float32) + np.float32(1.0)) * np.float32(math.pi / (2.0 * beam_total))
    values = parity * np.cos(angles) / (np.float32(beam_total) * np.sin(angles))
    return values.astype(np.float32).astype(jnp.bfloat16)


def split_order(beam_total):
    return np.concatenate([np.arange(0, beam_total, 2), np.arange(1, beam_total, 2)])


def spin(parts, scale, lead, first_at, beams_out):
    count = parts.shape[-1]
    lanes = 128
    coarse = jnp.asarray(
        (2.0 * lead * lanes / beams_out) * np.arange(count // lanes) + ((2 * first_at + 1) / beams_out - 1.0),
        jnp.float32,
    )
    fine = jnp.asarray((2.0 * lead / beams_out) * np.arange(lanes), jnp.float32)
    rough = scale[..., None] * coarse
    small = scale[..., None] * fine
    c1 = jnp.cos(rough)[..., None]
    s1 = jnp.sin(rough)[..., None]
    c2 = jnp.cos(small)[..., None, :]
    s2 = jnp.sin(small)[..., None, :]
    cosine = c1 * c2 - s1 * s2
    sines = s1 * c2 + c1 * s2
    grid = parts.shape[:-3] + (parts.shape[-2], count // lanes, lanes)
    real_part = parts[..., 0, :, :].reshape(grid)
    imag_part = parts[..., 1, :, :].reshape(grid)
    turned = jnp.stack(
        [real_part * cosine - imag_part * sines, real_part * sines + imag_part * cosine], -4
    )
    return turned.reshape(parts.shape)


def odd_local(children, kernel):
    product = jnp.dot(
        children.reshape(-1, children.shape[-1]), kernel, preferred_element_type=jnp.float32
    )
    return product.reshape(children.shape[:-1] + (kernel.shape[1],))


LANES = 128


TILE = 256


def toeplitz_tiles(matrix):
    count = matrix.shape[0] // TILE
    tiles = []
    for gap in range(-(count - 1), count):
        i = max(0, -gap)
        j = i + gap
        tiles.append(matrix[i * TILE:(i + 1) * TILE, j * TILE:(j + 1) * TILE])
    tiles = np.stack(tiles)
    for i in range(count):
        for j in range(count):
            assert np.array_equal(matrix[i * TILE:(i + 1) * TILE, j * TILE:(j + 1) * TILE], tiles[j - i + count - 1])
    return tiles


def kernel_tables(width):
    one = toeplitz_tiles(odd_values(width))
    order = split_order(2 * width)
    two = odd_values(2 * width)[order][:, order]
    assert np.array_equal(two[:width, :width], two[width:, width:])
    quads = np.stack([toeplitz_tiles(two[:width, :width]), toeplitz_tiles(two[:width, width:]),
                      toeplitz_tiles(two[width:, :width])])
    return jnp.asarray(np.concatenate([one[None], quads]))


def merge_kernel(slot_ref, x_ref, t1c, t1s, f1c, f1s, t2c, t2s, f2c, f2s, k_hbm, o_ref,
                 k1_v, k2_v, first_v, odd1_v, odd2_v, sems):
    members, _, rows, local = x_ref.shape
    beam_count = members // 4
    blocks = local // LANES
    wide = beam_count * blocks
    half = wide * LANES
    load_one = pltpu.make_async_copy(k_hbm.at[0], k1_v, sems.at[0])
    load_two = pltpu.make_async_copy(k_hbm.at[pl.ds(1, 3)], k2_v, sems.at[1])
    load_one.start()
    load_two.start()

    def column(ref, a, b, u):
        return ref[a, b][:, u:u + 1]

    def turn(xr, xi, c1, s1, c2, s2):
        cosine = c1 * c2 - s1 * s2
        sines = s1 * c2 + c1 * s2
        return xr * cosine - xi * sines, xr * sines + xi * cosine

    for pair in range(2):
        for u in range(wide):
            b, k = divmod(u, blocks)
            cols = pl.ds(k * LANES, LANES)
            re_sum = None
            for m in range(2):
                s = 2 * pair + m
                xr = x_ref[s * beam_count + b, 0, :, cols].astype(jnp.float32)
                xi = x_ref[s * beam_count + b, 1, :, cols].astype(jnp.float32)
                re, im = turn(xr, xi, column(t1c, s, 0, u), column(t1s, s, 0, u), f1c[s], f1s[s])
                re_sum = re if re_sum is None else re_sum + re
                im_sum = im if m == 0 else im_sum + im
            out_cols = pl.ds(u * LANES, LANES)
            first_v[pair, pl.ds(0, rows), out_cols] = re_sum.astype(first_v.dtype)
            first_v[pair, pl.ds(rows, rows), out_cols] = im_sum.astype(first_v.dtype)

    load_one.wait()
    count = half // TILE
    per_piece = local // TILE
    parts = []
    for i in range(count):
        b, k = divmod(i, per_piece)
        stacked = [x_ref[s * beam_count + b, :, :, pl.ds(k * TILE, TILE)] for s in range(4)]
        parts.append(jnp.concatenate(stacked, axis=0).reshape(8 * rows, TILE))
    for j in range(count):
        total = None
        for i in range(count):
            term = jnp.dot(parts[i], k1_v[j - i + count - 1], preferred_element_type=jnp.float32)
            total = term if total is None else total + term
        odd1_v[:, :, pl.ds(j * TILE, TILE)] = total.reshape(4, 2 * rows, TILE)

    for pair in range(2):
        for u in range(wide):
            cols = pl.ds(u * LANES, LANES)
            for m in range(2):
                s = 2 * pair + m
                xr = odd1_v[s, pl.ds(0, rows), cols]
                xi = odd1_v[s, pl.ds(rows, rows), cols]
                re, im = turn(xr, xi, column(t1c, s, 1, u), column(t1s, s, 1, u), f1c[s], f1s[s])
                re_sum = re if m == 0 else re_sum + re
                im_sum = im if m == 0 else im_sum + im
            out_cols = pl.ds(half + u * LANES, LANES)
            first_v[pair, pl.ds(0, rows), out_cols] = re_sum.astype(first_v.dtype)
            first_v[pair, pl.ds(rows, rows), out_cols] = im_sum.astype(first_v.dtype)

    load_two.wait()
    evens = [first_v[:, :, pl.ds(i * TILE, TILE)].reshape(4 * rows, TILE) for i in range(count)]
    odds = [first_v[:, :, pl.ds(half + i * TILE, TILE)].reshape(4 * rows, TILE) for i in range(count)]
    for j in range(count):
        even_out = None
        odd_out = None
        for i in range(count):
            gap = j - i + count - 1
            term_e = jnp.dot(evens[i], k2_v[0, gap], preferred_element_type=jnp.float32)
            term_e += jnp.dot(odds[i], k2_v[2, gap], preferred_element_type=jnp.float32)
            term_o = jnp.dot(evens[i], k2_v[1, gap], preferred_element_type=jnp.float32)
            term_o += jnp.dot(odds[i], k2_v[0, gap], preferred_element_type=jnp.float32)
            even_out = term_e if even_out is None else even_out + term_e
            odd_out = term_o if odd_out is None else odd_out + term_o
        odd2_v[:, :, pl.ds(j * TILE, TILE)] = even_out.reshape(2, 2 * rows, TILE)
        odd2_v[:, :, pl.ds(half + j * TILE, TILE)] = odd_out.reshape(2, 2 * rows, TILE)

    for t in range(4):
        for u in range(wide):
            at = (t // 2) * half + u * LANES if t % 2 == 0 else (t // 2) * half + u * LANES
            cols = pl.ds(at, LANES)
            for pair in range(2):
                if t % 2 == 0:
                    xr = first_v[pair, pl.ds(0, rows), cols].astype(jnp.float32)
                    xi = first_v[pair, pl.ds(rows, rows), cols].astype(jnp.float32)
                else:
                    xr = odd2_v[pair, pl.ds(0, rows), cols]
                    xi = odd2_v[pair, pl.ds(rows, rows), cols]
                re, im = turn(xr, xi, column(t2c, pair, t, u), column(t2s, pair, t, u), f2c[pair], f2s[pair])
                re_sum = re if pair == 0 else re_sum + re
                im_sum = im if pair == 0 else im_sum + im
            slot = slot_ref[u]
            o_ref[slot, t, 0] = re_sum.astype(o_ref.dtype)
            o_ref[slot, t, 1] = im_sum.astype(o_ref.dtype)


def merge_call(slots, x, tables, kernels, interpret=False):
    members, _, rows, local = x.shape
    width = local * members // 4
    vmem = pl.BlockSpec(memory_space=pltpu.VMEM)
    hbm = pl.BlockSpec(memory_space=pl.ANY)
    smem = pl.BlockSpec(memory_space=pltpu.SMEM)
    return pl.pallas_call(
        merge_kernel,
        out_shape=jax.ShapeDtypeStruct((width // LANES, 4, 2, rows, LANES), jnp.bfloat16),
        in_specs=[smem] + [vmem] * 9 + [hbm],
        out_specs=vmem,
        scratch_shapes=[
            pltpu.VMEM(kernels.shape[1:], jnp.bfloat16),
            pltpu.VMEM((3,) + kernels.shape[1:], jnp.bfloat16),
            pltpu.VMEM((2, 2 * rows, 2 * width), jnp.bfloat16),
            pltpu.VMEM((4, 2 * rows, width), jnp.float32),
            pltpu.VMEM((2, 2 * rows, 2 * width), jnp.float32),
            pltpu.SemaphoreType.DMA((2,)),
        ],
        compiler_params=pltpu.CompilerParams(vmem_limit_bytes=48 * 1024 * 1024),
        interpret=interpret,
    )(slots, x, *tables, kernels)


def merge_tables(shifts, ratios, width):
    units = np.arange(width // LANES)
    fine = jnp.asarray(np.arange(LANES) / 512.0, jnp.float32)
    scale_one = shifts[:, None] * ratios[None, :]
    coarse_one = jnp.asarray(
        [0.25 * units + ((2 * t + 1) / (2 * width) - 1.0) for t in range(2)], jnp.float32
    )
    rough_one = scale_one[:, None, None, :] * coarse_one[None, :, :, None]
    small_one = scale_one[:, :, None] * fine
    centers = (shifts[0::2] + shifts[1::2]) * 0.5
    scale_two = centers[:, None] * ratios[None, :]
    coarse_two = jnp.asarray(
        [0.25 * units + ((2 * t + 1) / (4 * width) - 1.0) for t in range(4)], jnp.float32
    )
    rough_two = scale_two[:, None, None, :] * coarse_two[None, :, :, None]
    small_two = scale_two[:, :, None] * fine
    rough_one = jnp.swapaxes(rough_one, -1, -2)
    rough_two = jnp.swapaxes(rough_two, -1, -2)
    return (jnp.cos(rough_one), jnp.sin(rough_one), jnp.cos(small_one), jnp.sin(small_one),
            jnp.cos(rough_two), jnp.sin(rough_two), jnp.cos(small_two), jnp.sin(small_two))


def flip_order(count, beam_count):
    rest = sorted(range(1, count), key=lambda f: (f // beam_count, f))
    return np.array([0] + rest, dtype=np.int32)


def swap_ordered(ordered, place, axes, order):
    count = ordered.shape[0]
    moved = [ordered[0]]
    for at in range(1, count):
        flip = int(order[at])
        pairs = [(i, i ^ flip) for i in range(count)]
        moved.append(lax.ppermute(ordered[at], axes, pairs))
    position = jnp.asarray(np.argsort(order).astype(np.int32))
    senders = position[jnp.bitwise_xor(place, jnp.arange(count, dtype=jnp.int32))]
    return jnp.take(jnp.stack(moved), senders, axis=0)


def body(images, offsets, owners):
    group_count = lax.axis_size("grp")
    sub_count = group_count * GROUP_SUBS
    beam_count = lax.axis_size("beam")
    group_at = lax.axis_index("grp")
    member_at = lax.axis_index("sub4") * beam_count + lax.axis_index("beam")
    half_side = lax.axis_index("half")
    members = GROUP_SUBS * beam_count
    half_rows = images.shape[2]
    own_rows = half_rows // members
    local_beams = images.shape[3]

    pieces = images[0].reshape(2, members, own_rows, local_beams).transpose(1, 0, 2, 3)
    gathered = lax.all_to_all(pieces, ("sub4", "beam"), 0, 0, tiled=True)
    rows_at = half_side * half_rows + member_at * own_rows + jnp.arange(own_rows, dtype=jnp.int32)
    ratios = NR / (NR + rows_at.astype(jnp.float32))
    shifts = lax.dynamic_slice_in_dim(offsets, group_at * GROUP_SUBS, GROUP_SUBS, 0)
    order = split_order(2 * B)
    blocks = B // LANES
    sector_width = 4 * B // (beam_count * sub_count)
    direct = group_count == 1 and sector_width == 4 * LANES
    if direct:
        shard_of = jnp.arange(blocks, dtype=jnp.int32) // sub_count
        sector_of = jnp.arange(blocks, dtype=jnp.int32) % sub_count
        holder = jnp.argmax(owners[shard_of] == sector_of[:, None], axis=1).astype(jnp.int32)
        sequence = flip_order(members, beam_count)
        position = jnp.asarray(np.argsort(sequence).astype(np.int32))
        slots = position[jnp.bitwise_xor(member_at, holder * beam_count + shard_of)]
    else:
        slots = jnp.arange(blocks, dtype=jnp.int32)
    merged = merge_call(
        slots,
        gathered,
        merge_tables(shifts, ratios, B),
        kernel_tables(B),
    )
    if direct:
        ordered = merged.transpose(0, 2, 4, 1, 3).reshape(blocks, 2, sector_width, own_rows)
        received = swap_ordered(ordered, member_at, ("sub4", "beam"), sequence)
        received = received.transpose(1, 2, 0, 3)
        return received.reshape(1, 1, 2, sector_width, members * own_rows)
    merged = merged.transpose(1, 2, 3, 0, 4).reshape(4, 2, own_rows, B)

    tiles = merged.reshape(4, 2, own_rows, beam_count, sub_count, sector_width // 4)
    beam_ids = jnp.arange(beam_count, dtype=jnp.int32)[:, None]
    picked = tiles[:, :, :, beam_ids, owners, :]
    outgoing = picked.transpose(4, 3, 1, 5, 0, 2).reshape(
        sub_count * beam_count, 2, sector_width, own_rows
    )
    received = lax.all_to_all(outgoing, ("grp", "sub4", "beam"), 0, 0, tiled=True)
    received = received.reshape(group_count, members, 2, sector_width, own_rows)
    received = received.transpose(0, 2, 3, 1, 4)
    return received.reshape(1, group_count, 2, sector_width, members * own_rows)


def solution(mesh):
    shape = dict(mesh.shape)
    devices = mesh.devices.reshape(
        shape["swath"], shape["sub"] // GROUP_SUBS, GROUP_SUBS, shape["beam"], shape["half"]
    )
    split = Mesh(devices, ("swath", "grp", "sub4", "beam", "half"))
    placed = (P(("grp", "sub4"), None, ("swath", "half"), "beam"), P(), P())
    return jax.shard_map(
        body,
        mesh=split,
        in_specs=placed,
        out_specs=P(("grp", "sub4", "beam"), None, None, None, ("swath", "half")),
        check_vma=False,
    )
```

```python
import math

import jax
import numpy as np
import jax.numpy as jnp
from jax import lax
from jax.experimental import pallas as pl
from jax.experimental.pallas import tpu as pltpu
from jax.sharding import Mesh
from jax.sharding import PartitionSpec as P

B = 1024
NR = 1024
GROUP_SUBS = 4


def odd_values(beam_total):
    spacing = np.arange(beam_total, dtype=np.int64)[None, :] - np.arange(beam_total, dtype=np.int64)[:, None]
    parity = np.where(spacing % 2 == 0, 1.0, -1.0).astype(np.float32)
    angles = (2.0 * spacing.astype(np.float32) + np.float32(1.0)) * np.float32(math.pi / (2.0 * beam_total))
    values = parity * np.cos(angles) / (np.float32(beam_total) * np.sin(angles))
    return values.astype(np.float32).astype(jnp.bfloat16)


def split_order(beam_total):
    return np.concatenate([np.arange(0, beam_total, 2), np.arange(1, beam_total, 2)])


def spin(parts, scale, lead, first_at, beams_out):
    count = parts.shape[-1]
    lanes = 128
    coarse = jnp.asarray(
        (2.0 * lead * lanes / beams_out) * np.arange(count // lanes) + ((2 * first_at + 1) / beams_out - 1.0),
        jnp.float32,
    )
    fine = jnp.asarray((2.0 * lead / beams_out) * np.arange(lanes), jnp.float32)
    rough = scale[..., None] * coarse
    small = scale[..., None] * fine
    c1 = jnp.cos(rough)[..., None]
    s1 = jnp.sin(rough)[..., None]
    c2 = jnp.cos(small)[..., None, :]
    s2 = jnp.sin(small)[..., None, :]
    cosine = c1 * c2 - s1 * s2
    sines = s1 * c2 + c1 * s2
    grid = parts.shape[:-3] + (parts.shape[-2], count // lanes, lanes)
    real_part = parts[..., 0, :, :].reshape(grid)
    imag_part = parts[..., 1, :, :].reshape(grid)
    turned = jnp.stack(
        [real_part * cosine - imag_part * sines, real_part * sines + imag_part * cosine], -4
    )
    return turned.reshape(parts.shape)


def odd_local(children, kernel):
    product = jnp.dot(
        children.reshape(-1, children.shape[-1]), kernel, preferred_element_type=jnp.float32
    )
    return product.reshape(children.shape[:-1] + (kernel.shape[1],))


LANES = 128


TILE = 256


def toeplitz_tiles(matrix):
    count = matrix.shape[0] // TILE
    tiles = []
    for gap in range(-(count - 1), count):
        i = max(0, -gap)
        j = i + gap
        tiles.append(matrix[i * TILE:(i + 1) * TILE, j * TILE:(j + 1) * TILE])
    tiles = np.stack(tiles)
    for i in range(count):
        for j in range(count):
            assert np.array_equal(matrix[i * TILE:(i + 1) * TILE, j * TILE:(j + 1) * TILE], tiles[j - i + count - 1])
    return tiles


def kernel_tables(width):
    one = toeplitz_tiles(odd_values(width))
    order = split_order(2 * width)
    two = odd_values(2 * width)[order][:, order]
    assert np.array_equal(two[:width, :width], two[width:, width:])
    quads = np.stack([toeplitz_tiles(two[:width, :width]), toeplitz_tiles(two[:width, width:]),
                      toeplitz_tiles(two[width:, :width])])
    return jnp.asarray(np.concatenate([one[None], quads]))


def merge_kernel(slot_ref, x_ref, t1c, t1s, f1c, f1s, t2c, t2s, f2c, f2s, k_hbm, o_ref,
                 k1_v, k2_v, first_v, odd1_v, odd2_v, sems):
    members, _, rows, local = x_ref.shape
    beam_count = members // 4
    blocks = local // LANES
    wide = beam_count * blocks
    half = wide * LANES
    load_one = pltpu.make_async_copy(k_hbm.at[0], k1_v, sems.at[0])
    load_two = pltpu.make_async_copy(k_hbm.at[pl.ds(1, 3)], k2_v, sems.at[1])
    load_one.start()
    load_two.start()

    def column(ref, a, b, u):
        return ref[a, b][:, u:u + 1]

    def turn(xr, xi, c1, s1, c2, s2):
        cosine = c1 * c2 - s1 * s2
        sines = s1 * c2 + c1 * s2
        return xr * cosine - xi * sines, xr * sines + xi * cosine

    for pair in range(2):
        for u in range(wide):
            b, k = divmod(u, blocks)
            cols = pl.ds(k * LANES, LANES)
            re_sum = None
            for m in range(2):
                s = 2 * pair + m
                xr = x_ref[s * beam_count + b, 0, :, cols].astype(jnp.float32)
                xi = x_ref[s * beam_count + b, 1, :, cols].astype(jnp.float32)
                re, im = turn(xr, xi, column(t1c, s, 0, u), column(t1s, s, 0, u), f1c[s], f1s[s])
                re_sum = re if re_sum is None else re_sum + re
                im_sum = im if m == 0 else im_sum + im
            out_cols = pl.ds(u * LANES, LANES)
            first_v[pair, pl.ds(0, rows), out_cols] = re_sum.astype(first_v.dtype)
            first_v[pair, pl.ds(rows, rows), out_cols] = im_sum.astype(first_v.dtype)

    load_one.wait()
    count = half // TILE
    per_piece = local // TILE
    parts = []
    for i in range(count):
        b, k = divmod(i, per_piece)
        stacked = [x_ref[s * beam_count + b, :, :, pl.ds(k * TILE, TILE)] for s in range(4)]
        parts.append(jnp.concatenate(stacked, axis=0).reshape(8 * rows, TILE))
    for j in range(count):
        total = None
        for i in range(count):
            term = jnp.dot(parts[i], k1_v[j - i + count - 1], preferred_element_type=jnp.float32)
            total = term if total is None else total + term
        odd1_v[:, :, pl.ds(j * TILE, TILE)] = total.reshape(4, 2 * rows, TILE)

    for pair in range(2):
        for u in range(wide):
            cols = pl.ds(u * LANES, LANES)
            for m in range(2):
                s = 2 * pair + m
                xr = odd1_v[s, pl.ds(0, rows), cols]
                xi = odd1_v[s, pl.ds(rows, rows), cols]
                re, im = turn(xr, xi, column(t1c, s, 1, u), column(t1s, s, 1, u), f1c[s], f1s[s])
                re_sum = re if m == 0 else re_sum + re
                im_sum = im if m == 0 else im_sum + im
            out_cols = pl.ds(half + u * LANES, LANES)
            first_v[pair, pl.ds(0, rows), out_cols] = re_sum.astype(first_v.dtype)
            first_v[pair, pl.ds(rows, rows), out_cols] = im_sum.astype(first_v.dtype)

    load_two.wait()
    evens = [first_v[:, :, pl.ds(i * TILE, TILE)].reshape(4 * rows, TILE) for i in range(count)]
    odds = [first_v[:, :, pl.ds(half + i * TILE, TILE)].reshape(4 * rows, TILE) for i in range(count)]
    both = [jnp.concatenate([evens[i], odds[i]], axis=0) for i in range(count)]
    for j in range(count):
        even_out = None
        odd_out = None
        for i in range(count):
            gap = j - i + count - 1
            shared = jnp.dot(both[i], k2_v[0, gap], preferred_element_type=jnp.float32)
            term_e = shared[:4 * rows] + jnp.dot(odds[i], k2_v[2, gap], preferred_element_type=jnp.float32)
            term_o = jnp.dot(evens[i], k2_v[1, gap], preferred_element_type=jnp.float32) + shared[4 * rows:]
            even_out = term_e if even_out is None else even_out + term_e
            odd_out = term_o if odd_out is None else odd_out + term_o
        odd2_v[:, :, pl.ds(j * TILE, TILE)] = even_out.reshape(2, 2 * rows, TILE)
        odd2_v[:, :, pl.ds(half + j * TILE, TILE)] = odd_out.reshape(2, 2 * rows, TILE)

    for t in range(4):
        for u in range(wide):
            at = (t // 2) * half + u * LANES if t % 2 == 0 else (t // 2) * half + u * LANES
            cols = pl.ds(at, LANES)
            for pair in range(2):
                if t % 2 == 0:
                    xr = first_v[pair, pl.ds(0, rows), cols].astype(jnp.float32)
                    xi = first_v[pair, pl.ds(rows, rows), cols].astype(jnp.float32)
                else:
                    xr = odd2_v[pair, pl.ds(0, rows), cols]
                    xi = odd2_v[pair, pl.ds(rows, rows), cols]
                re, im = turn(xr, xi, column(t2c, pair, t, u), column(t2s, pair, t, u), f2c[pair], f2s[pair])
                re_sum = re if pair == 0 else re_sum + re
                im_sum = im if pair == 0 else im_sum + im
            slot = slot_ref[u]
            o_ref[slot, t, 0] = re_sum.astype(o_ref.dtype)
            o_ref[slot, t, 1] = im_sum.astype(o_ref.dtype)


def merge_call(slots, x, tables, kernels, interpret=False):
    members, _, rows, local = x.shape
    width = local * members // 4
    vmem = pl.BlockSpec(memory_space=pltpu.VMEM)
    hbm = pl.BlockSpec(memory_space=pl.ANY)
    smem = pl.BlockSpec(memory_space=pltpu.SMEM)
    return pl.pallas_call(
        merge_kernel,
        out_shape=jax.ShapeDtypeStruct((width // LANES, 4, 2, rows, LANES), jnp.bfloat16),
        in_specs=[smem] + [vmem] * 9 + [hbm],
        out_specs=vmem,
        scratch_shapes=[
            pltpu.VMEM(kernels.shape[1:], jnp.bfloat16),
            pltpu.VMEM((3,) + kernels.shape[1:], jnp.bfloat16),
            pltpu.VMEM((2, 2 * rows, 2 * width), jnp.bfloat16),
            pltpu.VMEM((4, 2 * rows, width), jnp.float32),
            pltpu.VMEM((2, 2 * rows, 2 * width), jnp.float32),
            pltpu.SemaphoreType.DMA((2,)),
        ],
        compiler_params=pltpu.CompilerParams(vmem_limit_bytes=48 * 1024 * 1024),
        interpret=interpret,
    )(slots, x, *tables, kernels)


def merge_tables(shifts, ratios, width):
    units = np.arange(width // LANES)
    fine = jnp.asarray(np.arange(LANES) / 512.0, jnp.float32)
    scale_one = shifts[:, None] * ratios[None, :]
    coarse_one = jnp.asarray(
        [0.25 * units + ((2 * t + 1) / (2 * width) - 1.0) for t in range(2)], jnp.float32
    )
    rough_one = scale_one[:, None, None, :] * coarse_one[None, :, :, None]
    small_one = scale_one[:, :, None] * fine
    centers = (shifts[0::2] + shifts[1::2]) * 0.5
    scale_two = centers[:, None] * ratios[None, :]
    coarse_two = jnp.asarray(
        [0.25 * units + ((2 * t + 1) / (4 * width) - 1.0) for t in range(4)], jnp.float32
    )
    rough_two = scale_two[:, None, None, :] * coarse_two[None, :, :, None]
    small_two = scale_two[:, :, None] * fine
    rough_one = jnp.swapaxes(rough_one, -1, -2)
    rough_two = jnp.swapaxes(rough_two, -1, -2)
    return (jnp.cos(rough_one), jnp.sin(rough_one), jnp.cos(small_one), jnp.sin(small_one),
            jnp.cos(rough_two), jnp.sin(rough_two), jnp.cos(small_two), jnp.sin(small_two))


def flip_order(count, beam_count):
    rest = sorted(range(1, count), key=lambda f: (-(f // beam_count), f))
    return np.array([0] + rest, dtype=np.int32)


def swap_ordered(ordered, place, axes, order):
    count = ordered.shape[0]
    moved = [ordered[0]]
    for at in range(1, count):
        flip = int(order[at])
        pairs = [(i, i ^ flip) for i in range(count)]
        moved.append(lax.ppermute(ordered[at], axes, pairs))
    position = jnp.asarray(np.argsort(order).astype(np.int32))
    senders = position[jnp.bitwise_xor(place, jnp.arange(count, dtype=jnp.int32))]
    return jnp.take(jnp.stack(moved), senders, axis=0)


def body(images, offsets, owners):
    group_count = lax.axis_size("grp")
    sub_count = group_count * GROUP_SUBS
    beam_count = lax.axis_size("beam")
    group_at = lax.axis_index("grp")
    member_at = lax.axis_index("sub4") * beam_count + lax.axis_index("beam")
    half_side = lax.axis_index("half")
    members = GROUP_SUBS * beam_count
    half_rows = images.shape[2]
    own_rows = half_rows // members
    local_beams = images.shape[3]

    pieces = images[0].reshape(2, members, own_rows, local_beams).transpose(1, 0, 2, 3)
    gathered = lax.all_to_all(pieces, ("sub4", "beam"), 0, 0, tiled=True)
    rows_at = half_side * half_rows + member_at * own_rows + jnp.arange(own_rows, dtype=jnp.int32)
    ratios = NR / (NR + rows_at.astype(jnp.float32))
    shifts = lax.dynamic_slice_in_dim(offsets, group_at * GROUP_SUBS, GROUP_SUBS, 0)
    order = split_order(2 * B)
    blocks = B // LANES
    sector_width = 4 * B // (beam_count * sub_count)
    direct = group_count == 1 and sector_width == 4 * LANES
    if direct:
        shard_of = jnp.arange(blocks, dtype=jnp.int32) // sub_count
        sector_of = jnp.arange(blocks, dtype=jnp.int32) % sub_count
        holder = jnp.argmax(owners[shard_of] == sector_of[:, None], axis=1).astype(jnp.int32)
        sequence = flip_order(members, beam_count)
        position = jnp.asarray(np.argsort(sequence).astype(np.int32))
        slots = position[jnp.bitwise_xor(member_at, holder * beam_count + shard_of)]
    else:
        slots = jnp.arange(blocks, dtype=jnp.int32)
    merged = merge_call(
        slots,
        gathered,
        merge_tables(shifts, ratios, B),
        kernel_tables(B),
    )
    if direct:
        ordered = merged.transpose(0, 2, 4, 1, 3).reshape(blocks, 2, sector_width, own_rows)
        received = swap_ordered(ordered, member_at, ("sub4", "beam"), sequence)
        received = received.transpose(1, 2, 0, 3)
        return received.reshape(1, 1, 2, sector_width, members * own_rows)
    merged = merged.transpose(1, 2, 3, 0, 4).reshape(4, 2, own_rows, B)

    tiles = merged.reshape(4, 2, own_rows, beam_count, sub_count, sector_width // 4)
    beam_ids = jnp.arange(beam_count, dtype=jnp.int32)[:, None]
    picked = tiles[:, :, :, beam_ids, owners, :]
    outgoing = picked.transpose(4, 3, 1, 5, 0, 2).reshape(
        sub_count * beam_count, 2, sector_width, own_rows
    )
    received = lax.all_to_all(outgoing, ("grp", "sub4", "beam"), 0, 0, tiled=True)
    received = received.reshape(group_count, members, 2, sector_width, own_rows)
    received = received.transpose(0, 2, 3, 1, 4)
    return received.reshape(1, group_count, 2, sector_width, members * own_rows)


def solution(mesh):
    shape = dict(mesh.shape)
    devices = mesh.devices.reshape(
        shape["swath"], shape["sub"] // GROUP_SUBS, GROUP_SUBS, shape["beam"], shape["half"]
    )
    split = Mesh(devices, ("swath", "grp", "sub4", "beam", "half"))
    placed = (P(("grp", "sub4"), None, ("swath", "half"), "beam"), P(), P())
    return jax.shard_map(
        body,
        mesh=split,
        in_specs=placed,
        out_specs=P(("grp", "sub4", "beam"), None, None, None, ("swath", "half")),
        check_vma=False,
    )
```
